32 devices in a mesh: req: 4 (over y, x), exp: 4 (over z), ffn: 2 (over core).
Axes of the slice: x: 2, y: 2, z: 4, core: 2. Of those that a mesh axis runs over, the one named last changes fastest.
Arguments:
- residual: bfloat16 [2048, 2048], P(('req', 'exp')), may hold values from -5 to 5
- queries: bfloat16 [2048, 4608], P(('req', 'exp'), 'ffn'), may hold values from -30 to 30
- new_latent: bfloat16 [2048, 576], P(('req', 'exp')), may hold values from -6 to 6
- cache_pool: bfloat16 [512, 9216], P(('req', 'exp')), may hold values from -5 to 5
- page_table: int32 [8, 64], replicated, may hold values from 0 to 511, as said below
- cached_len: int32 [8], replicated, may hold values from 0 to 1024
- tenant_start: int32 [8], replicated, may hold values from 0 to 512, as said below
- routes: int32 [2048, 6], P(('req', 'exp')), may hold values from 0 to 31, all different within a row; in each aligned block of 64 rows (0 to 63, 64 to 127, ...) at most 16 rows name the same one
- value_up: bfloat16 [512, 1024], P(None, 'ffn'), may hold values from -0.25 to 0.25
- out_proj: bfloat16 [1024, 2048], P('ffn'), may hold values from -0.1875 to 0.1875
- norm_gain: bfloat16 [2048], replicated, may hold values from 0.099609375 to 1.8984375
- router: bfloat16 [2048, 32], replicated, may hold values from -0.125 to 0.125
- gate_weight: bfloat16 [32, 2048, 1408], P('exp', None, 'ffn'), may hold values from -0.125 to 0.125
- up_weight: bfloat16 [32, 2048, 1408], P('exp', None, 'ffn'), may hold values from -0.125 to 0.125
- down_weight: bfloat16 [32, 1408, 2048], P('exp', 'ffn'), may hold values from -0.15625 to 0.15625
Outputs:
- hidden_out: bfloat16 [2048, 2048], P(('req', 'exp'), 'ffn')
- moe_out: bfloat16 [2048, 2048], P(('req', 'exp'), 'ffn')
The draws below stay inside these ranges and needn't reach their ends.
Inputs may be any that keep to these rules, and one draw needn't show every extreme that they name: `page_table`: row i lists, in order, the pool pages of request i's cache; the 2 requests of group g = i // 2 use pool pages g * 2 * 64 to (g + 1) * 2 * 64 - 1, each exactly once. tenant_start[i] is at most half of cached_len[i]. `routes`: A row names 6 different experts; in each aligned block of 64 rows at most 16 rows name the same expert.
All inputs are finite; a program needn't handle non-finite values.
Results may differ from the reference program's by a relative error of at most 0.025.
Values may be sent and summed in bfloat16 or wider, within the bound.
No kernel may reach another device: no remote copies, remote signals or barrier semaphores. Data moves between devices by JAX's collectives and lax.ppermute only.
A program may use at most 128 MiB of HBM per device.

```python
import math
import jax
import jax.numpy as jnp
import numpy as np
from jax import lax

D = 2048
HEADS = 8
LATENT = 512
ROPE_DIM = 64
HEAD_DIM = 128
QKD = 576
FF = 1408
EXPERTS = 32
TOP = 6
CAPACITY = 16
REQ_GRP = 2
CMAX = 1024
PAGE = 16
MAXPAGES = 64
NEW_TOK = 256
REQS = 8
TOKENS = 2048
POOL_PAGES = 512
BLOCK_ROWS = 64


def latent_values(key):
    values = jnp.clip(jax.random.normal(jax.random.fold_in(key, 11), (TOKENS, QKD), jnp.float32), -5.0, 5.0)
    return values


def draw_new_latent(key, part):
    return latent_values(key).astype(jnp.bfloat16)


def draw_queries(key, part):
    values = jnp.clip(jax.random.normal(jax.random.fold_in(key, 21), (TOKENS, HEADS, QKD), jnp.float32), -5.0, 5.0)
    return values.reshape(TOKENS, HEADS * QKD).astype(jnp.bfloat16)


def draw_page_table(key, part):
    group_pages = REQ_GRP * MAXPAGES
    groups = REQS // REQ_GRP
    group_keys = jax.random.split(jax.random.fold_in(key, 31), groups)
    orders = jax.vmap(lambda subkey: jax.random.permutation(subkey, group_pages))(group_keys)
    offsets = (jnp.arange(groups, dtype=jnp.int32) * group_pages)[:, None]
    return (orders.astype(jnp.int32) + offsets).reshape(REQS, MAXPAGES)


def length_pair(key):
    base_key = jax.random.fold_in(key, 41)
    drawn = jax.random.randint(jax.random.fold_in(base_key, 1), (REQS,), 0, CMAX + 1)
    skewed = drawn * drawn // CMAX
    longest = jax.random.randint(jax.random.fold_in(base_key, 2), (), 0, REQS)
    shortest = (longest + 1) % REQS
    request_ids = jnp.arange(REQS, dtype=jnp.int32)
    lengths = jnp.where(request_ids == longest, CMAX, jnp.where(request_ids == shortest, 0, skewed)).astype(jnp.int32)
    fraction = jax.random.randint(jax.random.fold_in(base_key, 3), (REQS,), 0, CMAX + 1)
    starts = (fraction * lengths // (2 * CMAX)).astype(jnp.int32)
    starts = jnp.where(request_ids == longest, CMAX // 2, starts).astype(jnp.int32)
    return (lengths, starts)


def draw_cached_len(key, part):
    lengths, starts = length_pair(key)
    return lengths


def draw_tenant_start(key, part):
    lengths, starts = length_pair(key)
    return starts


def block_scale(key, shape, shards, low, top_value):
    def one(dim, blocks):
        draws = jax.random.uniform(jax.random.fold_in(jax.random.fold_in(key, 6), dim), (blocks,), jnp.float32, low / len(shards), top_value / len(shards))
        return jnp.repeat(jnp.exp(draws), shape[dim] // blocks).reshape((-1,) + (1,) * (len(shape) - dim - 1))

    level = one(*shards[0])
    for cut in shards[1:]:
        level = level * one(*cut)
    return level


def shared_out(key, own, number, rows, amount, top, most, lean):
    order = jax.random.permutation(key, amount)
    heavy_load, usual = portions_of(amount, rows * top, most, lean, True), portions_of(amount, rows * top, most, lean, False)
    places = jnp.arange(amount)

    def named(tallies, offset_by):
        used = int((tallies > 0).sum())
        fixed = max(1, used // 4)
        passed = fixed + (places - fixed + offset_by * (used - fixed)) % max(1, amount - fixed)
        return jnp.zeros((amount,), jnp.int32).at[order[jnp.where(places < fixed, places, passed)]].set(jnp.asarray(tallies, jnp.int32))

    tallies = jnp.where(number % 4 == 0, named(heavy_load, number // 4), named(usual, number - number // 4 - 1))
    mixed = jax.random.permutation(jax.random.fold_in(own, 3), amount)
    source_of, receiver = mixed[0:amount // 2 * 2:2], mixed[1:amount // 2 * 2:2]
    margin = jnp.minimum(tallies[source_of] - 1, most - tallies[receiver]) // 2
    margin = jnp.where((source_of == order[0]) | (receiver == order[0]) | (tallies[receiver] == 0), 0, jnp.maximum(margin, 0))
    passed = jax.random.randint(jax.random.fold_in(own, 4), (amount // 2,), 0, 1 << 20) % (margin + 1)
    tallies = tallies.at[source_of].add(-passed).at[receiver].add(passed)
    labels = jnp.searchsorted(jnp.cumsum(tallies), jnp.arange(rows * top), side="right").astype(jnp.int32)
    listing = labels.reshape(top, rows).T
    listing = listing[jax.random.permutation(jax.random.fold_in(own, 1), rows)]
    offset_by = jax.random.randint(jax.random.fold_in(own, 2), (rows, 1), 0, top)
    return jnp.take_along_axis(listing, (jnp.arange(top)[None, :] + offset_by) % top, axis=1)


def portions_of(amount, total, most, slope, full):
    loads = [(1 << 20) // math.isqrt(grade ** slope) + 1 for grade in range(1, amount + 1)]
    largest = most if full else min(most, max(-(-total // amount), total * loads[0] // sum(loads)))
    least = 1 if total - largest >= amount - 1 else 0
    counts, rest = [largest] + [least] * (amount - 1), total - largest - least * (amount - 1)
    while rest > 0:
        movable = [i for i in range(1, amount) if counts[i] < largest] or [i for i in range(1, amount) if counts[i] < most]
        pool, budget = sum([loads[i] for i in movable]), rest
        for i in movable:
            addition = min(most - counts[i], max(1, budget * loads[i] // pool), rest)
            counts[i] = counts[i] + addition
            rest = rest - addition
    return np.array(counts)


def gaussian(rng, extent, spread, bound, shards=(), kind=jnp.bfloat16):
    result = jax.random.normal(rng, extent, jnp.float32) * spread
    if len(shards) > 0:
        result = block_scale(rng, extent, shards, -0.22, 0.18) * result
    return jnp.clip(result, min=-bound, max=bound).astype(kind)


def setup_inputs(seed: int = 0) -> dict:
    key_of = jax.random.split(jax.random.key(seed), 16)
    residual = gaussian(key_of[0], (TOKENS, D), 1.0, 5.0, ((0, 16),))
    queries = draw_queries(jax.random.fold_in(key_of[15], 71), 0)
    new_latent = draw_new_latent(jax.random.fold_in(key_of[15], 71), 0)
    cache_pool = gaussian(key_of[3], (POOL_PAGES, PAGE * QKD), 1.0, 5.0, ((0, 16),))
    page_table = draw_page_table(jax.random.fold_in(key_of[15], 71), 0)
    cached_len = draw_cached_len(jax.random.fold_in(key_of[15], 71), 0)
    tenant_start = draw_tenant_start(jax.random.fold_in(key_of[15], 71), 0)
    routes_keys = jax.random.split(jax.random.fold_in(key_of[7], 1), TOKENS // BLOCK_ROWS)
    routes_turns = jax.random.permutation(jax.random.fold_in(key_of[7], 3), TOKENS // BLOCK_ROWS)
    routes = jax.vmap(lambda own, number: shared_out(jax.random.fold_in(key_of[7], 2), own, number, BLOCK_ROWS, EXPERTS, TOP, CAPACITY, 2))(routes_keys, routes_turns).reshape((TOKENS, TOP))
    value_up = gaussian(key_of[8], (LATENT, HEADS * HEAD_DIM), LATENT ** -0.5, 0.25, ((1, 2),))
    out_proj = gaussian(key_of[9], (HEADS * HEAD_DIM, D), (HEADS * HEAD_DIM) ** -0.5, 0.1875, ((0, 2),))
    norm_gain = jnp.clip(1.0 + 0.18 * jax.random.normal(key_of[10], (D,), jnp.float32), 0.099609375, 1.8984375).astype(jnp.bfloat16)
    router = gaussian(key_of[11], (D, EXPERTS), D ** -0.5, 0.125)
    gate_weight = gaussian(key_of[12], (EXPERTS, D, FF), D ** -0.5, 0.125, ((0, 4), (2, 2)))
    up_weight = gaussian(key_of[13], (EXPERTS, D, FF), D ** -0.5, 0.125, ((0, 4), (2, 2)))
    down_weight = gaussian(key_of[14], (EXPERTS, FF, D), FF ** -0.5, 0.15625, ((0, 4), (1, 2)))
    return {"residual": residual, "queries": queries, "new_latent": new_latent, "cache_pool": cache_pool, "page_table": page_table, "cached_len": cached_len, "tenant_start": tenant_start, "routes": routes, "value_up": value_up, "out_proj": out_proj, "norm_gain": norm_gain, "router": router, "gate_weight": gate_weight, "up_weight": up_weight, "down_weight": down_weight}


EPSILON = 1e-06
NEG_FILL = -1e+30

def attend_request(request, queries, new_latent, cache_pool, page_table, cached_len, tenant_start):
    scale_factor = (HEAD_DIM + ROPE_DIM) ** (-0.5)
    cached_keys = jnp.take(cache_pool, page_table[request], axis=0).reshape(CMAX, QKD)
    first_row = (request * NEW_TOK).astype(jnp.int32)
    fresh_keys = lax.dynamic_slice_in_dim(new_latent, first_row, NEW_TOK, 0)
    all_keys = jnp.concatenate([cached_keys, fresh_keys], axis=0)
    query_rows = lax.dynamic_slice_in_dim(queries, first_row, NEW_TOK, 0)
    key_pos = lax.broadcasted_iota(jnp.int32, (1, CMAX + NEW_TOK), 1)
    tok_pos = lax.broadcasted_iota(jnp.int32, (NEW_TOK, 1), 0)
    cached_ok = (key_pos >= tenant_start[request]) & (key_pos < cached_len[request])
    fresh_ok = (key_pos >= CMAX) & (key_pos - CMAX <= tok_pos)
    visible = cached_ok | fresh_ok
    values = all_keys[:, :LATENT]
    results = []
    for head_pos in range(HEADS):
        head_query = query_rows[:, head_pos * QKD:(head_pos + 1) * QKD]
        scores = jnp.dot(head_query, all_keys.T, preferred_element_type=jnp.float32) * scale_factor
        scores = jnp.where(visible, scores, NEG_FILL)
        top_score = lax.optimization_barrier(jnp.max(scores, axis=1, keepdims=True))
        weights = jnp.exp(scores - top_score)
        attn_probs = (weights / lax.optimization_barrier(jnp.sum(weights, axis=1, keepdims=True))).astype(jnp.bfloat16)
        results.append(jnp.dot(attn_probs, values, preferred_element_type=jnp.float32).astype(jnp.bfloat16))
    return jnp.stack(results, axis=1)

def reference(residual, queries, new_latent, cache_pool, page_table, cached_len, tenant_start, routes, value_up, out_proj, norm_gain, router, gate_weight, up_weight, down_weight):

    def one_request(request):
        return attend_request(request, queries, new_latent, cache_pool, page_table, cached_len, tenant_start)
    latent_out = lax.map(one_request, jnp.arange(REQS, dtype=jnp.int32)).reshape(TOKENS, HEADS, LATENT)
    value_heads = value_up.reshape(LATENT, HEADS, HEAD_DIM)
    head_out = jnp.einsum('thl,lhd->thd', latent_out.astype(jnp.float32), value_heads.astype(jnp.float32))
    head_out = head_out.astype(jnp.bfloat16).reshape(TOKENS, HEADS * HEAD_DIM)
    attention = jnp.dot(head_out, out_proj, preferred_element_type=jnp.float32)
    hidden = (residual.astype(jnp.float32) + attention).astype(jnp.bfloat16)
    hidden_wide = hidden.astype(jnp.float32)
    mean_square = lax.optimization_barrier(jnp.mean(hidden_wide * hidden_wide, axis=1, keepdims=True))
    normed = (hidden_wide * lax.rsqrt(mean_square + EPSILON) * norm_gain.astype(jnp.float32)).astype(jnp.bfloat16)
    logits = jnp.dot(normed, router, preferred_element_type=jnp.float32)
    raised = jnp.exp(jnp.take_along_axis(logits, routes, axis=1))
    gate_weights = raised / lax.optimization_barrier(jnp.sum(raised, axis=1, keepdims=True))
    most_rows = TOKENS // BLOCK_ROWS * CAPACITY
    flat_routes = routes.reshape(TOKENS * TOP)
    flat_gates = gate_weights.reshape(TOKENS * TOP)

    def one_expert(accumulated, expert):
        matches = flat_routes == expert
        pair_ids, = jnp.nonzero(matches, size=most_rows, fill_value=0)
        row_total = jnp.sum(matches.astype(jnp.int32))
        live_rows = (jnp.arange(most_rows, dtype=jnp.int32) < row_total).astype(jnp.float32)
        token_ids = pair_ids // TOP
        picked_rows = jnp.take(normed, token_ids, axis=0)
        gate_part = jnp.dot(picked_rows, gate_weight[expert], preferred_element_type=jnp.float32)
        up_part = jnp.dot(picked_rows, up_weight[expert], preferred_element_type=jnp.float32)
        active = (jax.nn.silu(gate_part) * up_part).astype(jnp.bfloat16)
        expert_out = jnp.dot(active, down_weight[expert], preferred_element_type=jnp.float32)
        scaled = expert_out * (jnp.take(flat_gates, pair_ids) * live_rows)[:, None]
        return (accumulated.at[token_ids].add(scaled), None)
    accumulated, ignored = lax.scan(one_expert, jnp.zeros((TOKENS, D), jnp.float32), jnp.arange(EXPERTS, dtype=jnp.int32))
    return (hidden, accumulated.astype(jnp.bfloat16))
```

```python
import jax
import jax.numpy as jnp
from jax import lax
from jax.sharding import PartitionSpec as P

LATENT = 512
ROPE_DIM = 64
HEAD_DIM = 128
QKD = 576
EXPERTS = 32
TOP = 6
CAPACITY = 16
REQ_GRP = 2
CMAX = 1024
BLOCK_ROWS = 64


EPSILON = 1e-06
NEG_FILL = -1e30


def slot_numbers(route_block):
    expert_ids = lax.broadcasted_iota(jnp.int32, (1, EXPERTS), 1)
    onehot = (route_block[:, None] == expert_ids).astype(jnp.int32)
    before = jnp.cumsum(onehot, axis=0) - onehot
    return jnp.sum(before * onehot, axis=1)


def local(
    residual,
    queries,
    new_latent,
    cache_pool,
    page_table,
    cached_len,
    tenant_start,
    routes,
    value_up,
    out_proj,
    norm_gain,
    router,
    gate_weight,
    up_weight,
    down_weight,
):
    exp_size = lax.axis_size("exp")
    ffn_size = lax.axis_size("ffn")
    req_index = lax.axis_index("req")
    exp_index = lax.axis_index("exp")
    ffn_index = lax.axis_index("ffn")
    token_rows = residual.shape[0]
    feature_count = residual.shape[1]
    fresh_len = token_rows * exp_size // REQ_GRP
    first_token = (req_index * exp_size + exp_index) * token_rows
    request = first_token // fresh_len
    offset = first_token - request * fresh_len
    pool_all, latent_all = (
        lax.all_gather(cache_pool, "exp", axis=0, tiled=True),
        lax.all_gather(new_latent, "exp", axis=0, tiled=True),
    )
    pool_base = req_index * pool_all.shape[0]
    page_rows = page_table[request] - pool_base
    cached_keys = jnp.take(pool_all, page_rows, axis=0).reshape(CMAX, QKD)
    local_request = request - req_index * REQ_GRP
    fresh_keys = lax.dynamic_slice_in_dim(latent_all, local_request * fresh_len, fresh_len, 0)
    all_keys = jnp.concatenate([cached_keys, fresh_keys], axis=0)
    heads_here = queries.shape[1] // QKD
    query_heads = queries.reshape(token_rows, heads_here, QKD)
    scale_factor = (HEAD_DIM + ROPE_DIM) ** (-0.5)
    scores = (
        jnp.einsum("thd,kd->thk", query_heads, all_keys, preferred_element_type=jnp.float32)
        * scale_factor
    )
    key_pos = lax.broadcasted_iota(jnp.int32, (1, CMAX + fresh_len), 1)
    tok_pos = offset + lax.broadcasted_iota(jnp.int32, (token_rows, 1), 0)
    cached_ok = (key_pos >= tenant_start[request]) & (key_pos < cached_len[request])
    fresh_ok = (key_pos >= CMAX) & (key_pos - CMAX <= tok_pos)
    visible = cached_ok | fresh_ok
    scores = jnp.where(visible[:, None, :], scores, NEG_FILL)
    top_score = jnp.max(scores, axis=2, keepdims=True)
    weights = jnp.exp(scores - top_score)
    attn_probs = (weights / jnp.sum(weights, axis=2, keepdims=True)).astype(jnp.bfloat16)
    latent_out = jnp.einsum(
        "thk,kl->thl", attn_probs, all_keys[:, :LATENT], preferred_element_type=jnp.float32
    ).astype(jnp.bfloat16)
    value_heads = value_up.reshape(LATENT, heads_here, HEAD_DIM)
    head_out = jnp.einsum(
        "thl,lhd->thd", latent_out, value_heads, preferred_element_type=jnp.float32
    )
    head_out = head_out.astype(jnp.bfloat16).reshape(token_rows, heads_here * HEAD_DIM)
    partial_value = jnp.dot(head_out, out_proj, preferred_element_type=jnp.float32)
    column_count = feature_count // ffn_size
    attn_cols = lax.psum_scatter(
        partial_value.astype(jnp.bfloat16), "ffn", scatter_dimension=1, tiled=True
    ).astype(jnp.float32)
    residual_cols = lax.dynamic_slice_in_dim(residual, ffn_index * column_count, column_count, 1)
    hidden_out = (residual_cols.astype(jnp.float32) + attn_cols).astype(jnp.bfloat16)
    hidden_wide = hidden_out.astype(jnp.float32)
    square_sum = lax.psum(jnp.sum(hidden_wide * hidden_wide, axis=1, keepdims=True), "ffn")
    mean_square = square_sum / feature_count
    gain_cols = lax.dynamic_slice_in_dim(norm_gain, ffn_index * column_count, column_count, 0)
    normed_cols = (
        hidden_wide * lax.rsqrt(mean_square + EPSILON) * gain_cols.astype(jnp.float32)
    ).astype(jnp.bfloat16)
    normed_grid = lax.all_gather(normed_cols, ("exp", "ffn"), axis=0, tiled=False)
    normed_grid = normed_grid.reshape(exp_size, ffn_size, token_rows, column_count)
    group_rows = exp_size * token_rows
    routes_all = lax.all_gather(routes, "exp", axis=0, tiled=True)
    logits = jnp.einsum(
        "efrc,fck->erk",
        normed_grid,
        router.reshape(ffn_size, column_count, EXPERTS),
        preferred_element_type=jnp.float32,
    ).reshape(group_rows, EXPERTS)
    chosen = jnp.take_along_axis(logits, routes_all, axis=1)
    raised = jnp.exp(chosen)
    gate_weights = raised / jnp.sum(raised, axis=1, keepdims=True)
    blocks = group_rows // BLOCK_ROWS
    slot_within = jax.vmap(slot_numbers)(routes_all.reshape(blocks, BLOCK_ROWS * TOP))
    block_base = lax.broadcasted_iota(jnp.int32, (blocks, 1), 0) * CAPACITY
    slot_index = (slot_within + block_base).reshape(group_rows * TOP)
    slot_count = blocks * CAPACITY
    local_count = gate_weight.shape[0]
    total_slots = local_count * slot_count
    local_expert = routes_all.reshape(group_rows * TOP) - exp_index * local_count
    is_local = (local_expert >= 0) & (local_expert < local_count)
    local_target = jnp.where(is_local, local_expert * slot_count + slot_index, total_slots)
    token_ids = lax.broadcasted_iota(jnp.int32, (group_rows, TOP), 0).reshape(group_rows * TOP)
    slot_token = jnp.zeros((total_slots,), jnp.int32).at[local_target].set(token_ids, mode="drop")
    slot_weight = (
        jnp.zeros((total_slots,), jnp.float32)
        .at[local_target]
        .set(gate_weights.reshape(group_rows * TOP), mode="drop")
    )
    grouped = normed_grid[slot_token // token_rows, :, slot_token % token_rows, :]
    grouped = grouped.reshape(local_count, slot_count, feature_count)
    gate_part = jnp.einsum("jmd,jdf->jmf", grouped, gate_weight, preferred_element_type=jnp.float32)
    up_part = jnp.einsum("jmd,jdf->jmf", grouped, up_weight, preferred_element_type=jnp.float32)
    active = (jax.nn.silu(gate_part) * up_part).astype(jnp.bfloat16)
    outputs = jnp.einsum("jmf,jfd->jmd", active, down_weight, preferred_element_type=jnp.float32)
    weighted = (outputs.reshape(total_slots, feature_count) * slot_weight[:, None]).astype(
        jnp.bfloat16
    )
    row_ids = lax.broadcasted_iota(jnp.int32, (group_rows, 1), 0)
    onehot = (slot_token[None, :] == row_ids).astype(jnp.bfloat16)
    mixture = jnp.einsum(
        "ers,sfc->efrc",
        onehot.reshape(exp_size, token_rows, total_slots),
        weighted.reshape(total_slots, ffn_size, column_count),
        preferred_element_type=jnp.float32,
    ).astype(jnp.bfloat16)
    mixture = mixture.reshape(exp_size * ffn_size * token_rows, column_count)
    moe_out = lax.psum_scatter(mixture, ("exp", "ffn"), scatter_dimension=0, tiled=True)
    return (hidden_out, moe_out)


def solution(mesh):
    in_specs = (
        P(("req", "exp"), None),
        P(("req", "exp"), "ffn"),
        P(("req", "exp"), None),
        P(("req", "exp"), None),
        P(),
        P(),
        P(),
        P(("req", "exp"), None),
        P(None, "ffn"),
        P("ffn", None),
        P(),
        P(),
        P("exp", None, "ffn"),
        P("exp", None, "ffn"),
        P("exp", "ffn", None),
    )
    out_specs = (P(("req", "exp"), "ffn"), P(("req", "exp"), "ffn"))
    return jax.shard_map(local, mesh=mesh, in_specs=in_specs, out_specs=out_specs, check_vma=False)
```

```python
import jax
import jax.numpy as jnp
from jax import lax
from jax.sharding import PartitionSpec as P

LATENT = 512
ROPE_DIM = 64
HEAD_DIM = 128
QKD = 576
EXPERTS = 32
TOP = 6
CAPACITY = 16
REQ_GRP = 2
CMAX = 1024
BLOCK_ROWS = 64


EPSILON = 1e-06
NEG_FILL = -1e30


def local(
    residual,
    queries,
    new_latent,
    cache_pool,
    page_table,
    cached_len,
    tenant_start,
    routes,
    value_up,
    out_proj,
    norm_gain,
    router,
    gate_weight,
    up_weight,
    down_weight,
):
    exp_size = lax.axis_size("exp")
    ffn_size = lax.axis_size("ffn")
    req_index = lax.axis_index("req")
    exp_index = lax.axis_index("exp")
    ffn_index = lax.axis_index("ffn")
    token_rows = residual.shape[0]
    feature_count = residual.shape[1]
    fresh_len = token_rows * exp_size // REQ_GRP
    first_token = (req_index * exp_size + exp_index) * token_rows
    request = first_token // fresh_len
    offset = first_token - request * fresh_len
    pool_pages = cache_pool.shape[0]
    page_width = cache_pool.shape[1]
    latent_pages = token_rows * QKD // page_width
    route_count = token_rows * TOP
    route_pages = -(-route_count // page_width)
    route_rows = jnp.pad(
        routes.reshape(route_count).astype(jnp.bfloat16),
        (0, route_pages * page_width - route_count),
    ).reshape(route_pages, page_width)
    packed = jnp.concatenate(
        [cache_pool, new_latent.reshape(latent_pages, page_width), route_rows], axis=0
    )
    gathered = lax.all_gather(packed, "exp", axis=0, tiled=False)
    pool_all = gathered[:, :pool_pages].reshape(exp_size * pool_pages, page_width)
    latent_all = gathered[:, pool_pages : pool_pages + latent_pages].reshape(
        exp_size * token_rows, QKD
    )
    group_rows = exp_size * token_rows
    routes_all = (
        gathered[:, pool_pages + latent_pages :]
        .reshape(exp_size, route_pages * page_width)[:, :route_count]
        .reshape(group_rows, TOP)
        .astype(jnp.int32)
    )
    pool_base = req_index * pool_all.shape[0]
    page_rows = page_table[request] - pool_base
    cached_keys = jnp.take(pool_all, page_rows, axis=0).reshape(CMAX, QKD)
    local_request = request - req_index * REQ_GRP
    fresh_keys = lax.dynamic_slice_in_dim(latent_all, local_request * fresh_len, fresh_len, 0)
    all_keys = jnp.concatenate([cached_keys, fresh_keys], axis=0)
    heads_here = queries.shape[1] // QKD
    query_heads = queries.reshape(token_rows, heads_here, QKD)
    scale_factor = (HEAD_DIM + ROPE_DIM) ** (-0.5)
    scores = (
        jnp.einsum("thd,kd->thk", query_heads, all_keys, preferred_element_type=jnp.float32)
        * scale_factor
    )
    key_pos = lax.broadcasted_iota(jnp.int32, (1, CMAX + fresh_len), 1)
    tok_pos = offset + lax.broadcasted_iota(jnp.int32, (token_rows, 1), 0)
    cached_ok = (key_pos >= tenant_start[request]) & (key_pos < cached_len[request])
    fresh_ok = (key_pos >= CMAX) & (key_pos - CMAX <= tok_pos)
    visible = cached_ok | fresh_ok
    scores = jnp.where(visible[:, None, :], scores, NEG_FILL)
    top_score = jnp.max(scores, axis=2, keepdims=True)
    weights = jnp.exp(scores - top_score)
    attn_probs = (weights / jnp.sum(weights, axis=2, keepdims=True)).astype(jnp.bfloat16)
    latent_out = jnp.einsum(
        "thk,kl->thl", attn_probs, all_keys[:, :LATENT], preferred_element_type=jnp.float32
    ).astype(jnp.bfloat16)
    value_heads = value_up.reshape(LATENT, heads_here, HEAD_DIM)
    head_out = jnp.einsum(
        "thl,lhd->thd", latent_out, value_heads, preferred_element_type=jnp.float32
    )
    head_out = head_out.astype(jnp.bfloat16).reshape(token_rows, heads_here * HEAD_DIM)
    partial_value = jnp.dot(head_out, out_proj, preferred_element_type=jnp.float32)
    column_count = feature_count // ffn_size
    attn_cols = lax.psum_scatter(
        partial_value.astype(jnp.bfloat16), "ffn", scatter_dimension=1, tiled=True
    ).astype(jnp.float32)
    residual_cols = lax.dynamic_slice_in_dim(residual, ffn_index * column_count, column_count, 1)
    hidden_out = (residual_cols.astype(jnp.float32) + attn_cols).astype(jnp.bfloat16)
    hidden_wide = hidden_out.astype(jnp.float32)
    square_sum = lax.psum(jnp.sum(hidden_wide * hidden_wide, axis=1, keepdims=True), "ffn")
    mean_square = square_sum / feature_count
    gain_cols = lax.dynamic_slice_in_dim(norm_gain, ffn_index * column_count, column_count, 0)
    normed_cols = (
        hidden_wide * lax.rsqrt(mean_square + EPSILON) * gain_cols.astype(jnp.float32)
    ).astype(jnp.bfloat16)
    normed_half = lax.all_gather(normed_cols, "exp", axis=0, tiled=True)
    normed_all = lax.all_gather(normed_half, "ffn", axis=1, tiled=True)

    expert_ids = lax.broadcasted_iota(jnp.int32, (1, 1, EXPERTS), 2)
    route_hot = routes_all[:, :, None] == expert_ids
    blocks = group_rows // BLOCK_ROWS
    pair_count = BLOCK_ROWS * TOP
    pair_hot = route_hot.reshape(blocks, pair_count, EXPERTS).astype(jnp.bfloat16)
    earlier = (
        lax.broadcasted_iota(jnp.int32, (pair_count, pair_count), 1)
        < lax.broadcasted_iota(jnp.int32, (pair_count, pair_count), 0)
    ).astype(jnp.bfloat16)
    before = jnp.einsum("pq,bqx->bpx", earlier, pair_hot, preferred_element_type=jnp.float32)
    rank = jnp.sum(before * pair_hot.astype(jnp.float32), axis=2).astype(jnp.int32)
    block_base = lax.broadcasted_iota(jnp.int32, (blocks, 1), 0) * CAPACITY
    slot_index = (rank + block_base).reshape(group_rows, TOP)
    slot_count = blocks * CAPACITY
    local_count = gate_weight.shape[0]
    total_slots = local_count * slot_count
    local_expert = routes_all - exp_index * local_count
    is_local = (local_expert >= 0) & (local_expert < local_count)
    target = jnp.where(is_local, local_expert * slot_count + slot_index, -1)

    logits = jnp.dot(normed_all, router, preferred_element_type=jnp.float32)
    chosen = jnp.sum(jnp.where(route_hot, logits[:, None, :], 0.0), axis=2)
    raised = jnp.exp(chosen)
    gate_weights = raised / jnp.sum(raised, axis=1, keepdims=True)

    slot_ids = lax.broadcasted_iota(jnp.int32, (1, 1, total_slots), 2)
    slot_hit = target[:, :, None] == slot_ids
    combine = jnp.any(slot_hit, axis=1).astype(jnp.bfloat16)
    slot_weight = jnp.sum(jnp.where(slot_hit, gate_weights[:, :, None], 0.0), axis=(0, 1))
    dispatch_ids = lax.broadcasted_iota(jnp.int32, (total_slots, 1, 1), 0)
    dispatch = jnp.any(target[None, :, :] == dispatch_ids, axis=2).astype(jnp.bfloat16)
    grouped = jnp.dot(dispatch, normed_all, preferred_element_type=jnp.float32).astype(
        jnp.bfloat16
    )
    grouped = grouped.reshape(local_count, slot_count, feature_count)
    gate_part = jnp.einsum("jmd,jdf->jmf", grouped, gate_weight, preferred_element_type=jnp.float32)
    up_part = jnp.einsum("jmd,jdf->jmf", grouped, up_weight, preferred_element_type=jnp.float32)
    active = (jax.nn.silu(gate_part) * up_part).astype(jnp.bfloat16)
    outputs = jnp.einsum("jmf,jfd->jmd", active, down_weight, preferred_element_type=jnp.float32)
    weighted = (outputs.reshape(total_slots, feature_count) * slot_weight[:, None]).astype(
        jnp.bfloat16
    )
    mixture = jnp.dot(combine, weighted, preferred_element_type=jnp.float32).astype(jnp.bfloat16)
    moe_cols = lax.psum_scatter(mixture, "ffn", scatter_dimension=1, tiled=True)
    moe_out = lax.psum_scatter(moe_cols, "exp", scatter_dimension=0, tiled=True)
    return (hidden_out, moe_out)


def solution(mesh):
    in_specs = (
        P(("req", "exp"), None),
        P(("req", "exp"), "ffn"),
        P(("req", "exp"), None),
        P(("req", "exp"), None),
        P(),
        P(),
        P(),
        P(("req", "exp"), None),
        P(None, "ffn"),
        P("ffn", None),
        P(),
        P(),
        P("exp", None, "ffn"),
        P("exp", None, "ffn"),
        P("exp", "ffn", None),
    )
    out_specs = (P(("req", "exp"), "ffn"), P(("req", "exp"), "ffn"))
    return jax.shard_map(local, mesh=mesh, in_specs=in_specs, out_specs=out_specs, check_vma=False)
```

```python
import jax
import jax.numpy as jnp
from jax import lax
from jax.sharding import PartitionSpec as P

LATENT = 512
ROPE_DIM = 64
HEAD_DIM = 128
QKD = 576
EXPERTS = 32
TOP = 6
CAPACITY = 16
REQ_GRP = 2
CMAX = 1024
BLOCK_ROWS = 64


EPSILON = 1e-06
NEG_FILL = -1e30


def local(
    residual,
    queries,
    new_latent,
    cache_pool,
    page_table,
    cached_len,
    tenant_start,
    routes,
    value_up,
    out_proj,
    norm_gain,
    router,
    gate_weight,
    up_weight,
    down_weight,
):
    exp_size = lax.axis_size("exp")
    ffn_size = lax.axis_size("ffn")
    req_index = lax.axis_index("req")
    exp_index = lax.axis_index("exp")
    ffn_index = lax.axis_index("ffn")
    token_rows = residual.shape[0]
    feature_count = residual.shape[1]
    fresh_len = token_rows * exp_size // REQ_GRP
    first_token = (req_index * exp_size + exp_index) * token_rows
    request = first_token // fresh_len
    offset = first_token - request * fresh_len
    pool_pages = cache_pool.shape[0]
    page_width = cache_pool.shape[1]
    latent_pages = token_rows * QKD // page_width
    route_count = token_rows * TOP
    route_pages = -(-route_count // page_width)
    route_rows = jnp.pad(
        routes.reshape(route_count).astype(jnp.bfloat16),
        (0, route_pages * page_width - route_count),
    ).reshape(route_pages, page_width)
    packed_rows = pool_pages + latent_pages + route_pages
    share_rows = -(-packed_rows // ffn_size)
    packed = jnp.concatenate(
        [
            cache_pool,
            new_latent.reshape(latent_pages, page_width),
            route_rows,
            jnp.zeros((share_rows * ffn_size - packed_rows, page_width), jnp.bfloat16),
        ],
        axis=0,
    )
    share = lax.dynamic_slice_in_dim(packed, ffn_index * share_rows, share_rows, 0)
    gathered = lax.all_gather(share, ("exp", "ffn"), axis=0, tiled=False)
    gathered = gathered.reshape(exp_size, ffn_size * share_rows, page_width)
    pool_all = gathered[:, :pool_pages].reshape(exp_size * pool_pages, page_width)
    latent_all = gathered[:, pool_pages : pool_pages + latent_pages].reshape(
        exp_size * token_rows, QKD
    )
    group_rows = exp_size * token_rows
    routes_all = (
        gathered[:, pool_pages + latent_pages : packed_rows]
        .reshape(exp_size, route_pages * page_width)[:, :route_count]
        .reshape(group_rows, TOP)
        .astype(jnp.int32)
    )
    pool_base = req_index * pool_all.shape[0]
    page_rows = page_table[request] - pool_base
    cached_keys = jnp.take(pool_all, page_rows, axis=0).reshape(CMAX, QKD)
    local_request = request - req_index * REQ_GRP
    fresh_keys = lax.dynamic_slice_in_dim(latent_all, local_request * fresh_len, fresh_len, 0)
    all_keys = jnp.concatenate([cached_keys, fresh_keys], axis=0)
    heads_here = queries.shape[1] // QKD
    query_heads = queries.reshape(token_rows, heads_here, QKD)
    scale_factor = (HEAD_DIM + ROPE_DIM) ** (-0.5)
    scores = (
        jnp.einsum("thd,kd->thk", query_heads, all_keys, preferred_element_type=jnp.float32)
        * scale_factor
    )
    key_pos = lax.broadcasted_iota(jnp.int32, (1, CMAX + fresh_len), 1)
    tok_pos = offset + lax.broadcasted_iota(jnp.int32, (token_rows, 1), 0)
    cached_ok = (key_pos >= tenant_start[request]) & (key_pos < cached_len[request])
    fresh_ok = (key_pos >= CMAX) & (key_pos - CMAX <= tok_pos)
    visible = cached_ok | fresh_ok
    scores = jnp.where(visible[:, None, :], scores, NEG_FILL)
    top_score = jnp.max(scores, axis=2, keepdims=True)
    weights = jnp.exp(scores - top_score)
    attn_probs = (weights / jnp.sum(weights, axis=2, keepdims=True)).astype(jnp.bfloat16)
    latent_out = jnp.einsum(
        "thk,kl->thl", attn_probs, all_keys[:, :LATENT], preferred_element_type=jnp.float32
    ).astype(jnp.bfloat16)
    value_heads = value_up.reshape(LATENT, heads_here, HEAD_DIM)
    head_out = jnp.einsum(
        "thl,lhd->thd", latent_out, value_heads, preferred_element_type=jnp.float32
    )
    head_out = head_out.astype(jnp.bfloat16).reshape(token_rows, heads_here * HEAD_DIM)
    partial_value = jnp.dot(head_out, out_proj, preferred_element_type=jnp.float32)
    column_count = feature_count // ffn_size
    attn_cols = lax.psum_scatter(
        partial_value.astype(jnp.bfloat16), "ffn", scatter_dimension=1, tiled=True
    ).astype(jnp.float32)
    residual_cols = lax.dynamic_slice_in_dim(residual, ffn_index * column_count, column_count, 1)
    hidden_out = (residual_cols.astype(jnp.float32) + attn_cols).astype(jnp.bfloat16)
    hidden_wide = hidden_out.astype(jnp.float32)
    square_sum = lax.psum(jnp.sum(hidden_wide * hidden_wide, axis=1, keepdims=True), "ffn")
    mean_square = square_sum / feature_count
    gain_cols = lax.dynamic_slice_in_dim(norm_gain, ffn_index * column_count, column_count, 0)
    normed_cols = (
        hidden_wide * lax.rsqrt(mean_square + EPSILON) * gain_cols.astype(jnp.float32)
    ).astype(jnp.bfloat16)
    normed_half = lax.all_gather(normed_cols, "exp", axis=0, tiled=True)
    normed_all = lax.all_gather(normed_half, "ffn", axis=1, tiled=True)

    expert_ids = lax.broadcasted_iota(jnp.int32, (1, 1, EXPERTS), 2)
    route_hot = routes_all[:, :, None] == expert_ids
    blocks = group_rows // BLOCK_ROWS
    pair_count = BLOCK_ROWS * TOP
    pair_hot = route_hot.reshape(blocks, pair_count, EXPERTS).astype(jnp.bfloat16)
    earlier = (
        lax.broadcasted_iota(jnp.int32, (pair_count, pair_count), 1)
        < lax.broadcasted_iota(jnp.int32, (pair_count, pair_count), 0)
    ).astype(jnp.bfloat16)
    before = jnp.einsum("pq,bqx->bpx", earlier, pair_hot, preferred_element_type=jnp.float32)
    rank = jnp.sum(before * pair_hot.astype(jnp.float32), axis=2).astype(jnp.int32)
    block_base = lax.broadcasted_iota(jnp.int32, (blocks, 1), 0) * CAPACITY
    slot_index = (rank + block_base).reshape(group_rows, TOP)
    slot_count = blocks * CAPACITY
    local_count = gate_weight.shape[0]
    total_slots = local_count * slot_count
    local_expert = routes_all - exp_index * local_count
    is_local = (local_expert >= 0) & (local_expert < local_count)
    target = jnp.where(is_local, local_expert * slot_count + slot_index, -1)

    logits = jnp.dot(normed_all, router, preferred_element_type=jnp.float32)
    chosen = jnp.sum(jnp.where(route_hot, logits[:, None, :], 0.0), axis=2)
    raised = jnp.exp(chosen)
    gate_weights = raised / jnp.sum(raised, axis=1, keepdims=True)

    slot_ids = lax.broadcasted_iota(jnp.int32, (1, 1, total_slots), 2)
    slot_hit = target[:, :, None] == slot_ids
    combine = jnp.any(slot_hit, axis=1).astype(jnp.bfloat16)
    slot_weight = jnp.sum(jnp.where(slot_hit, gate_weights[:, :, None], 0.0), axis=(0, 1))
    dispatch_ids = lax.broadcasted_iota(jnp.int32, (total_slots, 1, 1), 0)
    dispatch = jnp.any(target[None, :, :] == dispatch_ids, axis=2).astype(jnp.bfloat16)
    grouped = jnp.dot(dispatch, normed_all, preferred_element_type=jnp.float32).astype(
        jnp.bfloat16
    )
    grouped = grouped.reshape(local_count, slot_count, feature_count)
    gate_part = jnp.einsum("jmd,jdf->jmf", grouped, gate_weight, preferred_element_type=jnp.float32)
    up_part = jnp.einsum("jmd,jdf->jmf", grouped, up_weight, preferred_element_type=jnp.float32)
    active = (jax.nn.silu(gate_part) * up_part).astype(jnp.bfloat16)
    outputs = jnp.einsum("jmf,jfd->jmd", active, down_weight, preferred_element_type=jnp.float32)
    weighted = (outputs.reshape(total_slots, feature_count) * slot_weight[:, None]).astype(
        jnp.bfloat16
    )
    mixture = jnp.dot(combine, weighted, preferred_element_type=jnp.float32).astype(jnp.bfloat16)
    moe_cols = lax.psum_scatter(mixture, "ffn", scatter_dimension=1, tiled=True)
    moe_out = lax.psum_scatter(moe_cols, "exp", scatter_dimension=0, tiled=True)
    return (hidden_out, moe_out)


def solution(mesh):
    in_specs = (
        P(("req", "exp"), None),
        P(("req", "exp"), "ffn"),
        P(("req", "exp"), None),
        P(("req", "exp"), None),
        P(),
        P(),
        P(),
        P(("req", "exp"), None),
        P(None, "ffn"),
        P("ffn", None),
        P(),
        P(),
        P("exp", None, "ffn"),
        P("exp", None, "ffn"),
        P("exp", "ffn", None),
    )
    out_specs = (P(("req", "exp"), "ffn"), P(("req", "exp"), "ffn"))
    return jax.shard_map(local, mesh=mesh, in_specs=in_specs, out_specs=out_specs, check_vma=False)
```

```python
import jax
import jax.numpy as jnp
from jax import lax
from jax.sharding import PartitionSpec as P

LATENT = 512
ROPE_DIM = 64
HEAD_DIM = 128
QKD = 576
EXPERTS = 32
TOP = 6
CAPACITY = 16
REQ_GRP = 2
CMAX = 1024
BLOCK_ROWS = 64


EPSILON = 1e-06
NEG_FILL = -1e30


def local(
    residual,
    queries,
    new_latent,
    cache_pool,
    page_table,
    cached_len,
    tenant_start,
    routes,
    value_up,
    out_proj,
    norm_gain,
    router,
    gate_weight,
    up_weight,
    down_weight,
):
    exp_size = lax.axis_size("exp")
    ffn_size = lax.axis_size("ffn")
    req_index = lax.axis_index("req")
    exp_index = lax.axis_index("exp")
    ffn_index = lax.axis_index("ffn")
    token_rows = residual.shape[0]
    feature_count = residual.shape[1]
    fresh_len = token_rows * exp_size // REQ_GRP
    first_token = (req_index * exp_size + exp_index) * token_rows
    request = first_token // fresh_len
    offset = first_token - request * fresh_len
    pool_pages = cache_pool.shape[0]
    page_width = cache_pool.shape[1]
    latent_pages = token_rows * QKD // page_width
    route_count = token_rows * TOP
    route_pages = -(-route_count // page_width)
    route_rows = jnp.pad(
        routes.reshape(route_count).astype(jnp.bfloat16),
        (0, route_pages * page_width - route_count),
    ).reshape(route_pages, page_width)
    packed_rows = pool_pages + latent_pages + route_pages
    share_rows = -(-packed_rows // ffn_size)
    packed = jnp.concatenate(
        [
            cache_pool,
            new_latent.reshape(latent_pages, page_width),
            route_rows,
            jnp.zeros((share_rows * ffn_size - packed_rows, page_width), jnp.bfloat16),
        ],
        axis=0,
    )
    share = lax.dynamic_slice_in_dim(packed, ffn_index * share_rows, share_rows, 0)
    gathered = lax.all_gather(share, ("exp", "ffn"), axis=0, tiled=False)
    gathered = gathered.reshape(exp_size, ffn_size * share_rows, page_width)
    stride = ffn_size * share_rows
    group_rows = exp_size * token_rows
    routes_all = (
        gathered[:, pool_pages + latent_pages : packed_rows]
        .reshape(exp_size, route_pages * page_width)[:, :route_count]
        .reshape(group_rows, TOP)
        .astype(jnp.int32)
    )
    flat_pages = gathered.reshape(exp_size * stride, page_width)
    pool_base = req_index * exp_size * pool_pages
    page_rows = page_table[request] - pool_base
    cached_rows = (page_rows // pool_pages) * stride + page_rows % pool_pages
    local_request = request - req_index * REQ_GRP
    fresh_devices = fresh_len // token_rows
    fresh_index = lax.broadcasted_iota(jnp.int32, (fresh_devices, latent_pages), 0)
    fresh_rows = (
        (local_request * fresh_devices + fresh_index) * stride
        + pool_pages
        + lax.broadcasted_iota(jnp.int32, (fresh_devices, latent_pages), 1)
    ).reshape(fresh_devices * latent_pages)
    key_rows = jnp.concatenate([cached_rows, fresh_rows], axis=0)
    all_keys = jnp.take(flat_pages, key_rows, axis=0).reshape(CMAX + fresh_len, QKD)
    heads_here = queries.shape[1] // QKD
    query_heads = queries.reshape(token_rows, heads_here, QKD)
    scale_factor = (HEAD_DIM + ROPE_DIM) ** (-0.5)
    scores = (
        jnp.einsum("thd,kd->thk", query_heads, all_keys, preferred_element_type=jnp.float32)
        * scale_factor
    )
    key_pos = lax.broadcasted_iota(jnp.int32, (1, CMAX + fresh_len), 1)
    tok_pos = offset + lax.broadcasted_iota(jnp.int32, (token_rows, 1), 0)
    cached_ok = (key_pos >= tenant_start[request]) & (key_pos < cached_len[request])
    fresh_ok = (key_pos >= CMAX) & (key_pos - CMAX <= tok_pos)
    visible = cached_ok | fresh_ok
    scores = jnp.where(visible[:, None, :], scores, NEG_FILL)
    top_score = jnp.max(scores, axis=2, keepdims=True)
    weights = jnp.exp(scores - top_score)
    attn_probs = (weights / jnp.sum(weights, axis=2, keepdims=True)).astype(jnp.bfloat16)
    latent_out = jnp.einsum(
        "thk,kl->thl", attn_probs, all_keys[:, :LATENT], preferred_element_type=jnp.float32
    ).astype(jnp.bfloat16)
    value_heads = value_up.reshape(LATENT, heads_here, HEAD_DIM)
    head_out = jnp.einsum(
        "thl,lhd->thd", latent_out, value_heads, preferred_element_type=jnp.float32
    )
    head_out = head_out.astype(jnp.bfloat16).reshape(token_rows, heads_here * HEAD_DIM)
    partial_value = jnp.dot(head_out, out_proj, preferred_element_type=jnp.float32)
    column_count = feature_count // ffn_size
    attn_cols = lax.psum_scatter(
        partial_value.astype(jnp.bfloat16), "ffn", scatter_dimension=1, tiled=True
    ).astype(jnp.float32)
    residual_cols = lax.dynamic_slice_in_dim(residual, ffn_index * column_count, column_count, 1)
    hidden_out = (residual_cols.astype(jnp.float32) + attn_cols).astype(jnp.bfloat16)
    hidden_wide = hidden_out.astype(jnp.float32)
    square_sum = lax.psum(jnp.sum(hidden_wide * hidden_wide, axis=1, keepdims=True), "ffn")
    mean_square = square_sum / feature_count
    gain_cols = lax.dynamic_slice_in_dim(norm_gain, ffn_index * column_count, column_count, 0)
    normed_cols = (
        hidden_wide * lax.rsqrt(mean_square + EPSILON) * gain_cols.astype(jnp.float32)
    ).astype(jnp.bfloat16)
    normed_half = lax.all_gather(normed_cols, "exp", axis=0, tiled=True)
    normed_all = lax.all_gather(normed_half, "ffn", axis=1, tiled=True)

    expert_ids = lax.broadcasted_iota(jnp.int32, (1, 1, EXPERTS), 2)
    route_hot = routes_all[:, :, None] == expert_ids
    blocks = group_rows // BLOCK_ROWS
    pair_count = BLOCK_ROWS * TOP
    pair_hot = route_hot.reshape(blocks, pair_count, EXPERTS).astype(jnp.bfloat16)
    earlier = (
        lax.broadcasted_iota(jnp.int32, (pair_count, pair_count), 1)
        < lax.broadcasted_iota(jnp.int32, (pair_count, pair_count), 0)
    ).astype(jnp.bfloat16)
    before = jnp.einsum("pq,bqx->bpx", earlier, pair_hot, preferred_element_type=jnp.float32)
    rank = jnp.sum(before * pair_hot.astype(jnp.float32), axis=2).astype(jnp.int32)
    block_base = lax.broadcasted_iota(jnp.int32, (blocks, 1), 0) * CAPACITY
    slot_index = (rank + block_base).reshape(group_rows, TOP)
    slot_count = blocks * CAPACITY
    local_count = gate_weight.shape[0]
    total_slots = local_count * slot_count
    local_expert = routes_all - exp_index * local_count
    is_local = (local_expert >= 0) & (local_expert < local_count)
    target = jnp.where(is_local, local_expert * slot_count + slot_index, -1)

    logits = jnp.dot(normed_all, router, preferred_element_type=jnp.float32)
    chosen = jnp.sum(jnp.where(route_hot, logits[:, None, :], 0.0), axis=2)
    raised = jnp.exp(chosen)
    gate_weights = raised / jnp.sum(raised, axis=1, keepdims=True)

    slot_ids = lax.broadcasted_iota(jnp.int32, (1, 1, total_slots), 2)
    slot_hit = target[:, :, None] == slot_ids
    combine = jnp.any(slot_hit, axis=1).astype(jnp.bfloat16)
    slot_weight = jnp.sum(jnp.where(slot_hit, gate_weights[:, :, None], 0.0), axis=(0, 1))
    dispatch_ids = lax.broadcasted_iota(jnp.int32, (total_slots, 1, 1), 0)
    dispatch = jnp.any(target[None, :, :] == dispatch_ids, axis=2).astype(jnp.bfloat16)
    grouped = jnp.dot(dispatch, normed_all, preferred_element_type=jnp.float32).astype(
        jnp.bfloat16
    )
    grouped = grouped.reshape(local_count, slot_count, feature_count)
    gate_part = jnp.einsum("jmd,jdf->jmf", grouped, gate_weight, preferred_element_type=jnp.float32)
    up_part = jnp.einsum("jmd,jdf->jmf", grouped, up_weight, preferred_element_type=jnp.float32)
    active = (jax.nn.silu(gate_part) * up_part).astype(jnp.bfloat16)
    outputs = jnp.einsum("jmf,jfd->jmd", active, down_weight, preferred_element_type=jnp.float32)
    weighted = (outputs.reshape(total_slots, feature_count) * slot_weight[:, None]).astype(
        jnp.bfloat16
    )
    mixture = jnp.dot(combine, weighted, preferred_element_type=jnp.float32).astype(jnp.bfloat16)
    moe_cols = lax.psum_scatter(mixture, "ffn", scatter_dimension=1, tiled=True)
    moe_out = lax.psum_scatter(moe_cols, "exp", scatter_dimension=0, tiled=True)
    return (hidden_out, moe_out)


def solution(mesh):
    in_specs = (
        P(("req", "exp"), None),
        P(("req", "exp"), "ffn"),
        P(("req", "exp"), None),
        P(("req", "exp"), None),
        P(),
        P(),
        P(),
        P(("req", "exp"), None),
        P(None, "ffn"),
        P("ffn", None),
        P(),
        P(),
        P("exp", None, "ffn"),
        P("exp", None, "ffn"),
        P("exp", "ffn", None),
    )
    out_specs = (P(("req", "exp"), "ffn"), P(("req", "exp"), "ffn"))
    return jax.shard_map(local, mesh=mesh, in_specs=in_specs, out_specs=out_specs, check_vma=False)
```

```python
import jax
import jax.numpy as jnp
from jax import lax
from jax.sharding import PartitionSpec as P

LATENT = 512
ROPE_DIM = 64
HEAD_DIM = 128
QKD = 576
EXPERTS = 32
TOP = 6
CAPACITY = 16
REQ_GRP = 2
CMAX = 1024
BLOCK_ROWS = 64


EPSILON = 1e-06
NEG_FILL = -1e30


def line_gather(x, axis_name):
    size = lax.axis_size(axis_name)
    position = lax.axis_index(axis_name)
    to_right = [(i, i + 1) for i in range(size - 1)]
    to_left = [(i + 1, i) for i in range(size - 1)]
    from_left = x
    from_right = x
    left_pieces = []
    right_pieces = []
    for _ in range(size - 1):
        from_left = lax.ppermute(from_left, axis_name, to_right)
        from_right = lax.ppermute(from_right, axis_name, to_left)
        left_pieces.append(from_left)
        right_pieces.append(from_right)
    stack = jnp.stack(left_pieces[::-1] + [x] + right_pieces)
    return lax.dynamic_slice_in_dim(stack, size - 1 - position, size, 0)


def local(
    residual,
    queries,
    new_latent,
    cache_pool,
    page_table,
    cached_len,
    tenant_start,
    routes,
    value_up,
    out_proj,
    norm_gain,
    router,
    gate_weight,
    up_weight,
    down_weight,
):
    exp_size = lax.axis_size("exp")
    ffn_size = lax.axis_size("ffn")
    req_index = lax.axis_index("req")
    exp_index = lax.axis_index("exp")
    ffn_index = lax.axis_index("ffn")
    token_rows = residual.shape[0]
    feature_count = residual.shape[1]
    fresh_len = token_rows * exp_size // REQ_GRP
    first_token = (req_index * exp_size + exp_index) * token_rows
    request = first_token // fresh_len
    offset = first_token - request * fresh_len
    pool_pages = cache_pool.shape[0]
    page_width = cache_pool.shape[1]
    latent_pages = token_rows * QKD // page_width
    route_count = token_rows * TOP
    route_pages = -(-route_count // page_width)
    route_rows = jnp.pad(
        routes.reshape(route_count).astype(jnp.bfloat16),
        (0, route_pages * page_width - route_count),
    ).reshape(route_pages, page_width)
    packed_rows = pool_pages + latent_pages + route_pages
    share_rows = -(-packed_rows // ffn_size)
    packed = jnp.concatenate(
        [
            cache_pool,
            new_latent.reshape(latent_pages, page_width),
            route_rows,
            jnp.zeros((share_rows * ffn_size - packed_rows, page_width), jnp.bfloat16),
        ],
        axis=0,
    )
    share = lax.dynamic_slice_in_dim(packed, ffn_index * share_rows, share_rows, 0)
    gathered = lax.all_gather(share, ("exp", "ffn"), axis=0, tiled=False)
    gathered = gathered.reshape(exp_size, ffn_size * share_rows, page_width)
    stride = ffn_size * share_rows
    group_rows = exp_size * token_rows
    routes_all = (
        gathered[:, pool_pages + latent_pages : packed_rows]
        .reshape(exp_size, route_pages * page_width)[:, :route_count]
        .reshape(group_rows, TOP)
        .astype(jnp.int32)
    )
    flat_pages = gathered.reshape(exp_size * stride, page_width)
    pool_base = req_index * exp_size * pool_pages
    page_rows = page_table[request] - pool_base
    cached_rows = (page_rows // pool_pages) * stride + page_rows % pool_pages
    local_request = request - req_index * REQ_GRP
    fresh_devices = fresh_len // token_rows
    fresh_index = lax.broadcasted_iota(jnp.int32, (fresh_devices, latent_pages), 0)
    fresh_rows = (
        (local_request * fresh_devices + fresh_index) * stride
        + pool_pages
        + lax.broadcasted_iota(jnp.int32, (fresh_devices, latent_pages), 1)
    ).reshape(fresh_devices * latent_pages)
    key_rows = jnp.concatenate([cached_rows, fresh_rows], axis=0)
    all_keys = jnp.take(flat_pages, key_rows, axis=0).reshape(CMAX + fresh_len, QKD)
    heads_here = queries.shape[1] // QKD
    query_heads = queries.reshape(token_rows, heads_here, QKD)
    scale_factor = (HEAD_DIM + ROPE_DIM) ** (-0.5)
    scores = (
        jnp.einsum("thd,kd->thk", query_heads, all_keys, preferred_element_type=jnp.float32)
        * scale_factor
    )
    key_pos = lax.broadcasted_iota(jnp.int32, (1, CMAX + fresh_len), 1)
    tok_pos = offset + lax.broadcasted_iota(jnp.int32, (token_rows, 1), 0)
    cached_ok = (key_pos >= tenant_start[request]) & (key_pos < cached_len[request])
    fresh_ok = (key_pos >= CMAX) & (key_pos - CMAX <= tok_pos)
    visible = cached_ok | fresh_ok
    scores = jnp.where(visible[:, None, :], scores, NEG_FILL)
    top_score = jnp.max(scores, axis=2, keepdims=True)
    weights = jnp.exp(scores - top_score)
    attn_probs = (weights / jnp.sum(weights, axis=2, keepdims=True)).astype(jnp.bfloat16)
    latent_out = jnp.einsum(
        "thk,kl->thl", attn_probs, all_keys[:, :LATENT], preferred_element_type=jnp.float32
    ).astype(jnp.bfloat16)
    value_heads = value_up.reshape(LATENT, heads_here, HEAD_DIM)
    head_out = jnp.einsum(
        "thl,lhd->thd", latent_out, value_heads, preferred_element_type=jnp.float32
    )
    head_out = head_out.astype(jnp.bfloat16).reshape(token_rows, heads_here * HEAD_DIM)
    partial_value = jnp.dot(head_out, out_proj, preferred_element_type=jnp.float32)
    column_count = feature_count // ffn_size
    attn_cols = lax.psum_scatter(
        partial_value.astype(jnp.bfloat16), "ffn", scatter_dimension=1, tiled=True
    ).astype(jnp.float32)
    residual_cols = lax.dynamic_slice_in_dim(residual, ffn_index * column_count, column_count, 1)
    hidden_out = (residual_cols.astype(jnp.float32) + attn_cols).astype(jnp.bfloat16)
    hidden_wide = hidden_out.astype(jnp.float32)
    square_sum = lax.psum(jnp.sum(hidden_wide * hidden_wide, axis=1, keepdims=True), "ffn")
    mean_square = square_sum / feature_count
    gain_cols = lax.dynamic_slice_in_dim(norm_gain, ffn_index * column_count, column_count, 0)
    normed_cols = (
        hidden_wide * lax.rsqrt(mean_square + EPSILON) * gain_cols.astype(jnp.float32)
    ).astype(jnp.bfloat16)
    normed_half = line_gather(normed_cols, "exp").reshape(group_rows, column_count)
    normed_all = lax.all_gather(normed_half, "ffn", axis=1, tiled=True)

    expert_ids = lax.broadcasted_iota(jnp.int32, (1, 1, EXPERTS), 2)
    route_hot = routes_all[:, :, None] == expert_ids
    blocks = group_rows // BLOCK_ROWS
    pair_count = BLOCK_ROWS * TOP
    pair_hot = route_hot.reshape(blocks, pair_count, EXPERTS).astype(jnp.bfloat16)
    earlier = (
        lax.broadcasted_iota(jnp.int32, (pair_count, pair_count), 1)
        < lax.broadcasted_iota(jnp.int32, (pair_count, pair_count), 0)
    ).astype(jnp.bfloat16)
    before = jnp.einsum("pq,bqx->bpx", earlier, pair_hot, preferred_element_type=jnp.float32)
    rank = jnp.sum(before * pair_hot.astype(jnp.float32), axis=2).astype(jnp.int32)
    block_base = lax.broadcasted_iota(jnp.int32, (blocks, 1), 0) * CAPACITY
    slot_index = (rank + block_base).reshape(group_rows, TOP)
    slot_count = blocks * CAPACITY
    local_count = gate_weight.shape[0]
    total_slots = local_count * slot_count
    local_expert = routes_all - exp_index * local_count
    is_local = (local_expert >= 0) & (local_expert < local_count)
    target = jnp.where(is_local, local_expert * slot_count + slot_index, -1)

    logits = jnp.dot(normed_all, router, preferred_element_type=jnp.float32)
    chosen = jnp.sum(jnp.where(route_hot, logits[:, None, :], 0.0), axis=2)
    raised = jnp.exp(chosen)
    gate_weights = raised / jnp.sum(raised, axis=1, keepdims=True)

    slot_ids = lax.broadcasted_iota(jnp.int32, (1, 1, total_slots), 2)
    slot_hit = target[:, :, None] == slot_ids
    combine = jnp.any(slot_hit, axis=1).astype(jnp.bfloat16)
    slot_weight = jnp.sum(jnp.where(slot_hit, gate_weights[:, :, None], 0.0), axis=(0, 1))
    dispatch_ids = lax.broadcasted_iota(jnp.int32, (total_slots, 1, 1), 0)
    dispatch = jnp.any(target[None, :, :] == dispatch_ids, axis=2).astype(jnp.bfloat16)
    grouped = jnp.dot(dispatch, normed_all, preferred_element_type=jnp.float32).astype(
        jnp.bfloat16
    )
    grouped = grouped.reshape(local_count, slot_count, feature_count)
    gate_part = jnp.einsum("jmd,jdf->jmf", grouped, gate_weight, preferred_element_type=jnp.float32)
    up_part = jnp.einsum("jmd,jdf->jmf", grouped, up_weight, preferred_element_type=jnp.float32)
    active = (jax.nn.silu(gate_part) * up_part).astype(jnp.bfloat16)
    outputs = jnp.einsum("jmf,jfd->jmd", active, down_weight, preferred_element_type=jnp.float32)
    weighted = (outputs.reshape(total_slots, feature_count) * slot_weight[:, None]).astype(
        jnp.bfloat16
    )
    mixture = jnp.dot(combine, weighted, preferred_element_type=jnp.float32).astype(jnp.bfloat16)
    moe_cols = lax.psum_scatter(mixture, "ffn", scatter_dimension=1, tiled=True)
    moe_out = lax.psum_scatter(moe_cols, "exp", scatter_dimension=0, tiled=True)
    return (hidden_out, moe_out)


def solution(mesh):
    in_specs = (
        P(("req", "exp"), None),
        P(("req", "exp"), "ffn"),
        P(("req", "exp"), None),
        P(("req", "exp"), None),
        P(),
        P(),
        P(),
        P(("req", "exp"), None),
        P(None, "ffn"),
        P("ffn", None),
        P(),
        P(),
        P("exp", None, "ffn"),
        P("exp", None, "ffn"),
        P("exp", "ffn", None),
    )
    out_specs = (P(("req", "exp"), "ffn"), P(("req", "exp"), "ffn"))
    return jax.shard_map(local, mesh=mesh, in_specs=in_specs, out_specs=out_specs, check_vma=False)
```

```python
import jax
import jax.numpy as jnp
from jax import lax
from jax.experimental import pallas as pl
from jax.experimental.pallas import tpu as pltpu
from jax.sharding import PartitionSpec as P

LATENT = 512
ROPE_DIM = 64
HEAD_DIM = 128
QKD = 576
EXPERTS = 32
TOP = 6
CAPACITY = 16
REQ_GRP = 2
CMAX = 1024
BLOCK_ROWS = 64


EPSILON = 1e-06
NEG_FILL = -1e30


SLOT_TILE = 128


def expert_kernel(rows_ref, gate_ref, up_ref, down_ref, scale_ref, out_ref):
    rows = rows_ref[0]
    contract = (((1,), (1,)), ((), ()))
    gate_part = lax.dot_general(rows, gate_ref[0], contract, preferred_element_type=jnp.float32)
    up_part = lax.dot_general(rows, up_ref[0], contract, preferred_element_type=jnp.float32)
    active = (gate_part / (1.0 + jnp.exp(-gate_part)) * up_part).astype(jnp.bfloat16)
    result = jnp.dot(active, down_ref[0], preferred_element_type=jnp.float32)
    out_ref[0] = (result * scale_ref[0]).astype(out_ref.dtype)


def expert_ffn(grouped, gate_weight, up_weight, down_weight, scale):
    local_count, slot_count, feature_count = grouped.shape
    hidden = gate_weight.shape[2]
    gate_rows = jnp.transpose(gate_weight, (0, 2, 1))
    up_rows = jnp.transpose(up_weight, (0, 2, 1))
    tile = min(SLOT_TILE, slot_count)
    return pl.pallas_call(
        expert_kernel,
        grid=(local_count, slot_count // tile),
        in_specs=[
            pl.BlockSpec((1, tile, feature_count), lambda j, m: (j, m, 0)),
            pl.BlockSpec((1, hidden, feature_count), lambda j, m: (j, 0, 0)),
            pl.BlockSpec((1, hidden, feature_count), lambda j, m: (j, 0, 0)),
            pl.BlockSpec((1, hidden, feature_count), lambda j, m: (j, 0, 0)),
            pl.BlockSpec((1, tile, 1), lambda j, m: (j, m, 0)),
        ],
        out_specs=pl.BlockSpec((1, tile, feature_count), lambda j, m: (j, m, 0)),
        out_shape=jax.ShapeDtypeStruct((local_count, slot_count, feature_count), jnp.bfloat16),
        compiler_params=pltpu.CompilerParams(
            dimension_semantics=("arbitrary", "arbitrary"),
            vmem_limit_bytes=56 * 1024 * 1024,
        ),
    )(grouped, gate_rows, up_rows, down_weight, scale)


def local(
    residual,
    queries,
    new_latent,
    cache_pool,
    page_table,
    cached_len,
    tenant_start,
    routes,
    value_up,
    out_proj,
    norm_gain,
    router,
    gate_weight,
    up_weight,
    down_weight,
):
    exp_size = lax.axis_size("exp")
    ffn_size = lax.axis_size("ffn")
    req_index = lax.axis_index("req")
    exp_index = lax.axis_index("exp")
    ffn_index = lax.axis_index("ffn")
    token_rows = residual.shape[0]
    feature_count = residual.shape[1]
    fresh_len = token_rows * exp_size // REQ_GRP
    first_token = (req_index * exp_size + exp_index) * token_rows
    request = first_token // fresh_len
    offset = first_token - request * fresh_len
    pool_pages = cache_pool.shape[0]
    page_width = cache_pool.shape[1]
    latent_pages = token_rows * QKD // page_width
    route_count = token_rows * TOP
    route_pages = -(-route_count // page_width)
    route_rows = jnp.pad(
        routes.reshape(route_count).astype(jnp.bfloat16),
        (0, route_pages * page_width - route_count),
    ).reshape(route_pages, page_width)
    packed_rows = pool_pages + latent_pages + route_pages
    share_rows = -(-packed_rows // ffn_size)
    packed = jnp.concatenate(
        [
            cache_pool,
            new_latent.reshape(latent_pages, page_width),
            route_rows,
            jnp.zeros((share_rows * ffn_size - packed_rows, page_width), jnp.bfloat16),
        ],
        axis=0,
    )
    share = lax.dynamic_slice_in_dim(packed, ffn_index * share_rows, share_rows, 0)
    gathered = lax.all_gather(share, ("exp", "ffn"), axis=0, tiled=False)
    gathered = gathered.reshape(exp_size, ffn_size * share_rows, page_width)
    stride = ffn_size * share_rows
    group_rows = exp_size * token_rows
    routes_all = (
        gathered[:, pool_pages + latent_pages : packed_rows]
        .reshape(exp_size, route_pages * page_width)[:, :route_count]
        .reshape(group_rows, TOP)
        .astype(jnp.int32)
    )
    flat_pages = gathered.reshape(exp_size * stride, page_width)
    pool_base = req_index * exp_size * pool_pages
    page_rows = page_table[request] - pool_base
    cached_rows = (page_rows // pool_pages) * stride + page_rows % pool_pages
    local_request = request - req_index * REQ_GRP
    fresh_devices = fresh_len // token_rows
    fresh_index = lax.broadcasted_iota(jnp.int32, (fresh_devices, latent_pages), 0)
    fresh_rows = (
        (local_request * fresh_devices + fresh_index) * stride
        + pool_pages
        + lax.broadcasted_iota(jnp.int32, (fresh_devices, latent_pages), 1)
    ).reshape(fresh_devices * latent_pages)
    key_rows = jnp.concatenate([cached_rows, fresh_rows], axis=0)
    all_keys = jnp.take(flat_pages, key_rows, axis=0).reshape(CMAX + fresh_len, QKD)
    heads_here = queries.shape[1] // QKD
    query_heads = queries.reshape(token_rows, heads_here, QKD)
    scale_factor = (HEAD_DIM + ROPE_DIM) ** (-0.5)
    scores = (
        jnp.einsum("thd,kd->thk", query_heads, all_keys, preferred_element_type=jnp.float32)
        * scale_factor
    )
    key_pos = lax.broadcasted_iota(jnp.int32, (1, CMAX + fresh_len), 1)
    tok_pos = offset + lax.broadcasted_iota(jnp.int32, (token_rows, 1), 0)
    cached_ok = (key_pos >= tenant_start[request]) & (key_pos < cached_len[request])
    fresh_ok = (key_pos >= CMAX) & (key_pos - CMAX <= tok_pos)
    visible = cached_ok | fresh_ok
    scores = jnp.where(visible[:, None, :], scores, NEG_FILL)
    top_score = jnp.max(scores, axis=2, keepdims=True)
    weights = jnp.exp(scores - top_score)
    attn_probs = (weights / jnp.sum(weights, axis=2, keepdims=True)).astype(jnp.bfloat16)
    latent_out = jnp.einsum(
        "thk,kl->thl", attn_probs, all_keys[:, :LATENT], preferred_element_type=jnp.float32
    ).astype(jnp.bfloat16)
    value_heads = value_up.reshape(LATENT, heads_here, HEAD_DIM)
    head_out = jnp.einsum(
        "thl,lhd->thd", latent_out, value_heads, preferred_element_type=jnp.float32
    )
    head_out = head_out.astype(jnp.bfloat16).reshape(token_rows, heads_here * HEAD_DIM)
    partial_value = jnp.dot(head_out, out_proj, preferred_element_type=jnp.float32)
    column_count = feature_count // ffn_size
    attn_cols = lax.psum_scatter(
        partial_value.astype(jnp.bfloat16), "ffn", scatter_dimension=1, tiled=True
    ).astype(jnp.float32)
    residual_cols = lax.dynamic_slice_in_dim(residual, ffn_index * column_count, column_count, 1)
    hidden_out = (residual_cols.astype(jnp.float32) + attn_cols).astype(jnp.bfloat16)
    hidden_wide = hidden_out.astype(jnp.float32)
    square_sum = lax.psum(jnp.sum(hidden_wide * hidden_wide, axis=1, keepdims=True), "ffn")
    mean_square = square_sum / feature_count
    gain_cols = lax.dynamic_slice_in_dim(norm_gain, ffn_index * column_count, column_count, 0)
    normed_cols = (
        hidden_wide * lax.rsqrt(mean_square + EPSILON) * gain_cols.astype(jnp.float32)
    ).astype(jnp.bfloat16)
    normed_half = lax.all_gather(normed_cols, "exp", axis=0, tiled=True)
    normed_all = lax.all_gather(normed_half, "ffn", axis=1, tiled=True)

    expert_ids = lax.broadcasted_iota(jnp.int32, (1, 1, EXPERTS), 2)
    route_hot = routes_all[:, :, None] == expert_ids
    blocks = group_rows // BLOCK_ROWS
    pair_count = BLOCK_ROWS * TOP
    pair_hot = route_hot.reshape(blocks, pair_count, EXPERTS).astype(jnp.bfloat16)
    earlier = (
        lax.broadcasted_iota(jnp.int32, (pair_count, pair_count), 1)
        < lax.broadcasted_iota(jnp.int32, (pair_count, pair_count), 0)
    ).astype(jnp.bfloat16)
    before = jnp.einsum("pq,bqx->bpx", earlier, pair_hot, preferred_element_type=jnp.float32)
    rank = jnp.sum(before * pair_hot.astype(jnp.float32), axis=2).astype(jnp.int32)
    block_base = lax.broadcasted_iota(jnp.int32, (blocks, 1), 0) * CAPACITY
    slot_index = (rank + block_base).reshape(group_rows, TOP)
    slot_count = blocks * CAPACITY
    local_count = gate_weight.shape[0]
    total_slots = local_count * slot_count
    local_expert = routes_all - exp_index * local_count
    is_local = (local_expert >= 0) & (local_expert < local_count)
    target = jnp.where(is_local, local_expert * slot_count + slot_index, -1)

    logits = jnp.dot(normed_all, router, preferred_element_type=jnp.float32)
    chosen = jnp.sum(jnp.where(route_hot, logits[:, None, :], 0.0), axis=2)
    raised = jnp.exp(chosen)
    gate_weights = raised / jnp.sum(raised, axis=1, keepdims=True)

    slot_ids = lax.broadcasted_iota(jnp.int32, (1, 1, total_slots), 2)
    slot_hit = target[:, :, None] == slot_ids
    combine = jnp.any(slot_hit, axis=1).astype(jnp.bfloat16)
    slot_weight = jnp.sum(jnp.where(slot_hit, gate_weights[:, :, None], 0.0), axis=(0, 1))
    dispatch_ids = lax.broadcasted_iota(jnp.int32, (total_slots, 1, 1), 0)
    dispatch = jnp.any(target[None, :, :] == dispatch_ids, axis=2).astype(jnp.bfloat16)
    grouped = jnp.dot(dispatch, normed_all, preferred_element_type=jnp.float32).astype(
        jnp.bfloat16
    )
    grouped = grouped.reshape(local_count, slot_count, feature_count)
    weighted = expert_ffn(
        grouped,
        gate_weight,
        up_weight,
        down_weight,
        slot_weight.reshape(local_count, slot_count, 1),
    ).reshape(total_slots, feature_count)
    mixture = jnp.dot(combine, weighted, preferred_element_type=jnp.float32).astype(jnp.bfloat16)
    moe_cols = lax.psum_scatter(mixture, "ffn", scatter_dimension=1, tiled=True)
    moe_out = lax.psum_scatter(moe_cols, "exp", scatter_dimension=0, tiled=True)
    return (hidden_out, moe_out)


def solution(mesh):
    in_specs = (
        P(("req", "exp"), None),
        P(("req", "exp"), "ffn"),
        P(("req", "exp"), None),
        P(("req", "exp"), None),
        P(),
        P(),
        P(),
        P(("req", "exp"), None),
        P(None, "ffn"),
        P("ffn", None),
        P(),
        P(),
        P("exp", None, "ffn"),
        P("exp", None, "ffn"),
        P("exp", "ffn", None),
    )
    out_specs = (P(("req", "exp"), "ffn"), P(("req", "exp"), "ffn"))
    return jax.shard_map(local, mesh=mesh, in_specs=in_specs, out_specs=out_specs, check_vma=False)
```

```python
import jax
import jax.numpy as jnp
from jax import lax
from jax.experimental import pallas as pl
from jax.experimental.pallas import tpu as pltpu
from jax.sharding import PartitionSpec as P

LATENT = 512
ROPE_DIM = 64
HEAD_DIM = 128
QKD = 576
EXPERTS = 32
TOP = 6
CAPACITY = 16
REQ_GRP = 2
CMAX = 1024
BLOCK_ROWS = 64


EPSILON = 1e-06
NEG_FILL = -1e30


SLOT_TILE = 128


def expert_kernel(rows_ref, gate_ref, up_ref, down_ref, scale_ref, out_ref):
    rows = rows_ref[0]
    contract = (((1,), (1,)), ((), ()))
    gate_part = lax.dot_general(rows, gate_ref[0], contract, preferred_element_type=jnp.float32)
    up_part = lax.dot_general(rows, up_ref[0], contract, preferred_element_type=jnp.float32)
    active = (gate_part / (1.0 + jnp.exp(-gate_part)) * up_part).astype(jnp.bfloat16)
    result = jnp.dot(active, down_ref[0], preferred_element_type=jnp.float32)
    out_ref[0] = (result * scale_ref[0]).astype(out_ref.dtype)


def expert_ffn(grouped, gate_weight, up_weight, down_weight, scale):
    local_count, slot_count, feature_count = grouped.shape
    hidden = gate_weight.shape[2]
    gate_rows = jnp.transpose(gate_weight, (0, 2, 1))
    up_rows = jnp.transpose(up_weight, (0, 2, 1))
    tile = min(SLOT_TILE, slot_count)
    return pl.pallas_call(
        expert_kernel,
        grid=(local_count, slot_count // tile),
        in_specs=[
            pl.BlockSpec((1, tile, feature_count), lambda j, m: (j, m, 0)),
            pl.BlockSpec((1, hidden, feature_count), lambda j, m: (j, 0, 0)),
            pl.BlockSpec((1, hidden, feature_count), lambda j, m: (j, 0, 0)),
            pl.BlockSpec((1, hidden, feature_count), lambda j, m: (j, 0, 0)),
            pl.BlockSpec((1, tile, 1), lambda j, m: (j, m, 0)),
        ],
        out_specs=pl.BlockSpec((1, tile, feature_count), lambda j, m: (j, m, 0)),
        out_shape=jax.ShapeDtypeStruct((local_count, slot_count, feature_count), jnp.bfloat16),
        compiler_params=pltpu.CompilerParams(
            dimension_semantics=("arbitrary", "arbitrary"),
            vmem_limit_bytes=56 * 1024 * 1024,
        ),
    )(grouped, gate_rows, up_rows, down_weight, scale)


def local(
    residual,
    queries,
    new_latent,
    cache_pool,
    page_table,
    cached_len,
    tenant_start,
    routes,
    value_up,
    out_proj,
    norm_gain,
    router,
    gate_weight,
    up_weight,
    down_weight,
):
    exp_size = lax.axis_size("exp")
    ffn_size = lax.axis_size("ffn")
    req_index = lax.axis_index("req")
    exp_index = lax.axis_index("exp")
    ffn_index = lax.axis_index("ffn")
    token_rows = residual.shape[0]
    feature_count = residual.shape[1]
    fresh_len = token_rows * exp_size // REQ_GRP
    first_token = (req_index * exp_size + exp_index) * token_rows
    request = first_token // fresh_len
    offset = first_token - request * fresh_len
    pool_pages = cache_pool.shape[0]
    page_width = cache_pool.shape[1]
    latent_pages = token_rows * QKD // page_width
    route_count = token_rows * TOP
    route_pages = -(-route_count // page_width)
    route_rows = jnp.pad(
        routes.reshape(route_count).astype(jnp.bfloat16),
        (0, route_pages * page_width - route_count),
    ).reshape(route_pages, page_width)
    packed_rows = pool_pages + latent_pages + route_pages
    share_rows = -(-packed_rows // (ffn_size * 8)) * 8
    packed = jnp.concatenate(
        [
            cache_pool,
            new_latent.reshape(latent_pages, page_width),
            route_rows,
            jnp.zeros((share_rows * ffn_size - packed_rows, page_width), jnp.bfloat16),
        ],
        axis=0,
    )
    share = lax.dynamic_slice_in_dim(packed, ffn_index * share_rows, share_rows, 0)
    gathered = lax.all_gather(share, ("exp", "ffn"), axis=0, tiled=False)
    gathered = gathered.reshape(exp_size, ffn_size * share_rows, page_width)
    stride = ffn_size * share_rows
    group_rows = exp_size * token_rows
    routes_all = (
        gathered[:, pool_pages + latent_pages : packed_rows]
        .reshape(exp_size, route_pages * page_width)[:, :route_count]
        .reshape(group_rows, TOP)
        .astype(jnp.int32)
    )
    flat_pages = gathered.reshape(exp_size * stride, page_width)
    pool_base = req_index * exp_size * pool_pages
    page_rows = page_table[request] - pool_base
    cached_rows = (page_rows // pool_pages) * stride + page_rows % pool_pages
    local_request = request - req_index * REQ_GRP
    fresh_devices = fresh_len // token_rows
    fresh_index = lax.broadcasted_iota(jnp.int32, (fresh_devices, latent_pages), 0)
    fresh_rows = (
        (local_request * fresh_devices + fresh_index) * stride
        + pool_pages
        + lax.broadcasted_iota(jnp.int32, (fresh_devices, latent_pages), 1)
    ).reshape(fresh_devices * latent_pages)
    key_rows = jnp.concatenate([cached_rows, fresh_rows], axis=0)
    all_keys = jnp.take(flat_pages, key_rows, axis=0, mode="clip").reshape(CMAX + fresh_len, QKD)
    heads_here = queries.shape[1] // QKD
    query_heads = queries.reshape(token_rows, heads_here, QKD)
    scale_factor = (HEAD_DIM + ROPE_DIM) ** (-0.5)
    scores = (
        jnp.einsum("thd,kd->thk", query_heads, all_keys, preferred_element_type=jnp.float32)
        * scale_factor
    )
    key_pos = lax.broadcasted_iota(jnp.int32, (1, CMAX + fresh_len), 1)
    tok_pos = offset + lax.broadcasted_iota(jnp.int32, (token_rows, 1), 0)
    cached_ok = (key_pos >= tenant_start[request]) & (key_pos < cached_len[request])
    fresh_ok = (key_pos >= CMAX) & (key_pos - CMAX <= tok_pos)
    visible = cached_ok | fresh_ok
    scores = jnp.where(visible[:, None, :], scores, NEG_FILL)
    top_score = jnp.max(scores, axis=2, keepdims=True)
    weights = jnp.exp(scores - top_score)
    attn_probs = (weights / jnp.sum(weights, axis=2, keepdims=True)).astype(jnp.bfloat16)
    latent_out = jnp.einsum(
        "thk,kl->thl", attn_probs, all_keys[:, :LATENT], preferred_element_type=jnp.float32
    ).astype(jnp.bfloat16)
    value_heads = value_up.reshape(LATENT, heads_here, HEAD_DIM)
    head_out = jnp.einsum(
        "thl,lhd->thd", latent_out, value_heads, preferred_element_type=jnp.float32
    )
    head_out = head_out.astype(jnp.bfloat16).reshape(token_rows, heads_here * HEAD_DIM)
    partial_value = jnp.dot(head_out, out_proj, preferred_element_type=jnp.float32)
    column_count = feature_count // ffn_size
    attn_cols = lax.psum_scatter(
        partial_value.astype(jnp.bfloat16), "ffn", scatter_dimension=1, tiled=True
    ).astype(jnp.float32)
    residual_cols = lax.dynamic_slice_in_dim(residual, ffn_index * column_count, column_count, 1)
    hidden_out = (residual_cols.astype(jnp.float32) + attn_cols).astype(jnp.bfloat16)
    hidden_wide = hidden_out.astype(jnp.float32)
    square_sum = lax.psum(jnp.sum(hidden_wide * hidden_wide, axis=1, keepdims=True), "ffn")
    mean_square = square_sum / feature_count
    gain_cols = lax.dynamic_slice_in_dim(norm_gain, ffn_index * column_count, column_count, 0)
    normed_cols = (
        hidden_wide * lax.rsqrt(mean_square + EPSILON) * gain_cols.astype(jnp.float32)
    ).astype(jnp.bfloat16)
    normed_half = lax.all_gather(normed_cols, "exp", axis=0, tiled=True)
    normed_all = lax.all_gather(normed_half, "ffn", axis=1, tiled=True)

    expert_ids = lax.broadcasted_iota(jnp.int32, (1, 1, EXPERTS), 2)
    route_hot = routes_all[:, :, None] == expert_ids
    blocks = group_rows // BLOCK_ROWS
    pair_count = BLOCK_ROWS * TOP
    pair_hot = route_hot.reshape(blocks, pair_count, EXPERTS).astype(jnp.bfloat16)
    earlier = (
        lax.broadcasted_iota(jnp.int32, (pair_count, pair_count), 1)
        < lax.broadcasted_iota(jnp.int32, (pair_count, pair_count), 0)
    ).astype(jnp.bfloat16)
    before = jnp.einsum("pq,bqx->bpx", earlier, pair_hot, preferred_element_type=jnp.float32)
    rank = jnp.sum(before * pair_hot.astype(jnp.float32), axis=2).astype(jnp.int32)
    block_base = lax.broadcasted_iota(jnp.int32, (blocks, 1), 0) * CAPACITY
    slot_index = (rank + block_base).reshape(group_rows, TOP)
    slot_count = blocks * CAPACITY
    local_count = gate_weight.shape[0]
    total_slots = local_count * slot_count
    local_expert = routes_all - exp_index * local_count
    is_local = (local_expert >= 0) & (local_expert < local_count)
    target = jnp.where(is_local, local_expert * slot_count + slot_index, -1)

    logits = jnp.dot(normed_all, router, preferred_element_type=jnp.float32)
    chosen = jnp.sum(jnp.where(route_hot, logits[:, None, :], 0.0), axis=2)
    raised = jnp.exp(chosen)
    gate_weights = raised / jnp.sum(raised, axis=1, keepdims=True)

    slot_ids = lax.broadcasted_iota(jnp.int32, (1, 1, total_slots), 2)
    slot_hit = target[:, :, None] == slot_ids
    combine = jnp.any(slot_hit, axis=1).astype(jnp.bfloat16)
    slot_weight = jnp.sum(jnp.where(slot_hit, gate_weights[:, :, None], 0.0), axis=(0, 1))
    dispatch_ids = lax.broadcasted_iota(jnp.int32, (total_slots, 1, 1), 0)
    dispatch = jnp.any(target[None, :, :] == dispatch_ids, axis=2).astype(jnp.bfloat16)
    grouped = jnp.dot(dispatch, normed_all, preferred_element_type=jnp.float32).astype(
        jnp.bfloat16
    )
    grouped = grouped.reshape(local_count, slot_count, feature_count)
    weighted = expert_ffn(
        grouped,
        gate_weight,
        up_weight,
        down_weight,
        slot_weight.reshape(local_count, slot_count, 1),
    ).reshape(total_slots, feature_count)
    mixture = jnp.dot(combine, weighted, preferred_element_type=jnp.float32).astype(jnp.bfloat16)
    moe_cols = lax.psum_scatter(mixture, "ffn", scatter_dimension=1, tiled=True)
    moe_out = lax.psum_scatter(moe_cols, "exp", scatter_dimension=0, tiled=True)
    return (hidden_out, moe_out)


def solution(mesh):
    in_specs = (
        P(("req", "exp"), None),
        P(("req", "exp"), "ffn"),
        P(("req", "exp"), None),
        P(("req", "exp"), None),
        P(),
        P(),
        P(),
        P(("req", "exp"), None),
        P(None, "ffn"),
        P("ffn", None),
        P(),
        P(),
        P("exp", None, "ffn"),
        P("exp", None, "ffn"),
        P("exp", "ffn", None),
    )
    out_specs = (P(("req", "exp"), "ffn"), P(("req", "exp"), "ffn"))
    return jax.shard_map(local, mesh=mesh, in_specs=in_specs, out_specs=out_specs, check_vma=False)
```

```python
import jax
import jax.numpy as jnp
from jax import lax
from jax.experimental import pallas as pl
from jax.experimental.pallas import tpu as pltpu
from jax.sharding import PartitionSpec as P

LATENT = 512
ROPE_DIM = 64
HEAD_DIM = 128
QKD = 576
EXPERTS = 32
TOP = 6
CAPACITY = 16
REQ_GRP = 2
CMAX = 1024
BLOCK_ROWS = 64


EPSILON = 1e-06
NEG_FILL = -1e30


SLOT_TILE = 128


def expert_kernel(rows_ref, gate_ref, up_ref, down_ref, scale_ref, out_ref):
    rows = rows_ref[0]
    contract = (((1,), (1,)), ((), ()))
    gate_part = lax.dot_general(rows, gate_ref[0], contract, preferred_element_type=jnp.float32)
    up_part = lax.dot_general(rows, up_ref[0], contract, preferred_element_type=jnp.float32)
    active = (gate_part / (1.0 + jnp.exp(-gate_part)) * up_part).astype(jnp.bfloat16)
    result = jnp.dot(active, down_ref[0], preferred_element_type=jnp.float32)
    out_ref[0] = (result * scale_ref[0]).astype(out_ref.dtype)


def expert_ffn(grouped, gate_weight, up_weight, down_weight, scale):
    local_count, slot_count, feature_count = grouped.shape
    hidden = gate_weight.shape[2]
    gate_rows = jnp.transpose(gate_weight, (0, 2, 1))
    up_rows = jnp.transpose(up_weight, (0, 2, 1))
    tile = min(SLOT_TILE, slot_count)
    return pl.pallas_call(
        expert_kernel,
        grid=(local_count, slot_count // tile),
        in_specs=[
            pl.BlockSpec((1, tile, feature_count), lambda j, m: (j, m, 0)),
            pl.BlockSpec((1, hidden, feature_count), lambda j, m: (j, 0, 0)),
            pl.BlockSpec((1, hidden, feature_count), lambda j, m: (j, 0, 0)),
            pl.BlockSpec((1, hidden, feature_count), lambda j, m: (j, 0, 0)),
            pl.BlockSpec((1, tile, 1), lambda j, m: (j, m, 0)),
        ],
        out_specs=pl.BlockSpec((1, tile, feature_count), lambda j, m: (j, m, 0)),
        out_shape=jax.ShapeDtypeStruct((local_count, slot_count, feature_count), jnp.bfloat16),
        compiler_params=pltpu.CompilerParams(
            dimension_semantics=("arbitrary", "arbitrary"),
            vmem_limit_bytes=56 * 1024 * 1024,
        ),
    )(grouped, gate_rows, up_rows, down_weight, scale)


def local(
    residual,
    queries,
    new_latent,
    cache_pool,
    page_table,
    cached_len,
    tenant_start,
    routes,
    value_up,
    out_proj,
    norm_gain,
    router,
    gate_weight,
    up_weight,
    down_weight,
):
    exp_size = lax.axis_size("exp")
    ffn_size = lax.axis_size("ffn")
    req_index = lax.axis_index("req")
    exp_index = lax.axis_index("exp")
    ffn_index = lax.axis_index("ffn")
    token_rows = residual.shape[0]
    feature_count = residual.shape[1]
    fresh_len = token_rows * exp_size // REQ_GRP
    first_token = (req_index * exp_size + exp_index) * token_rows
    request = first_token // fresh_len
    offset = first_token - request * fresh_len
    pool_pages = cache_pool.shape[0]
    page_width = cache_pool.shape[1]
    latent_pages = token_rows * QKD // page_width
    route_count = token_rows * TOP
    route_pages = -(-route_count // page_width)
    route_rows = jnp.pad(
        routes.reshape(route_count).astype(jnp.bfloat16),
        (0, route_pages * page_width - route_count),
    ).reshape(route_pages, page_width)
    packed_rows = pool_pages + latent_pages + route_pages
    share_rows = -(-packed_rows // (ffn_size * 8)) * 8
    packed = jnp.concatenate(
        [
            cache_pool,
            new_latent.reshape(latent_pages, page_width),
            route_rows,
            jnp.zeros((share_rows * ffn_size - packed_rows, page_width), jnp.bfloat16),
        ],
        axis=0,
    )
    share = lax.dynamic_slice_in_dim(packed, ffn_index * share_rows, share_rows, 0)
    gathered = lax.all_gather(share, ("exp", "ffn"), axis=0, tiled=False)
    gathered = gathered.reshape(exp_size, ffn_size * share_rows, page_width)
    stride = ffn_size * share_rows
    group_rows = exp_size * token_rows
    routes_all = (
        gathered[:, pool_pages + latent_pages : packed_rows]
        .reshape(exp_size, route_pages * page_width)[:, :route_count]
        .reshape(group_rows, TOP)
        .astype(jnp.int32)
    )
    flat_pages = gathered.reshape(exp_size * stride, page_width)
    pool_base = req_index * exp_size * pool_pages
    page_rows = page_table[request] - pool_base
    cached_rows = (page_rows // pool_pages) * stride + page_rows % pool_pages
    local_request = request - req_index * REQ_GRP
    fresh_devices = fresh_len // token_rows
    fresh_index = lax.broadcasted_iota(jnp.int32, (fresh_devices, latent_pages), 0)
    fresh_rows = (
        (local_request * fresh_devices + fresh_index) * stride
        + pool_pages
        + lax.broadcasted_iota(jnp.int32, (fresh_devices, latent_pages), 1)
    ).reshape(fresh_devices * latent_pages)
    key_rows = jnp.concatenate([cached_rows, fresh_rows], axis=0)
    all_keys = jnp.take(flat_pages, key_rows, axis=0, mode="clip").reshape(CMAX + fresh_len, QKD)
    heads_here = queries.shape[1] // QKD
    query_heads = queries.reshape(token_rows, heads_here, QKD)
    scale_factor = (HEAD_DIM + ROPE_DIM) ** (-0.5)
    scores = (
        jnp.einsum("thd,kd->thk", query_heads, all_keys, preferred_element_type=jnp.float32)
        * scale_factor
    )
    key_pos = lax.broadcasted_iota(jnp.int32, (1, CMAX + fresh_len), 1)
    tok_pos = offset + lax.broadcasted_iota(jnp.int32, (token_rows, 1), 0)
    cached_ok = (key_pos >= tenant_start[request]) & (key_pos < cached_len[request])
    fresh_ok = (key_pos >= CMAX) & (key_pos - CMAX <= tok_pos)
    visible = cached_ok | fresh_ok
    scores = jnp.where(visible[:, None, :], scores, NEG_FILL)
    top_score = jnp.max(scores, axis=2, keepdims=True)
    weights = jnp.exp(scores - top_score)
    attn_probs = (weights / jnp.sum(weights, axis=2, keepdims=True)).astype(jnp.bfloat16)
    latent_out = jnp.einsum(
        "thk,kl->thl", attn_probs, all_keys[:, :LATENT], preferred_element_type=jnp.float32
    ).astype(jnp.bfloat16)
    value_heads = value_up.reshape(LATENT, heads_here, HEAD_DIM)
    head_out = jnp.einsum(
        "thl,lhd->thd", latent_out, value_heads, preferred_element_type=jnp.float32
    )
    head_out = head_out.astype(jnp.bfloat16).reshape(token_rows, heads_here * HEAD_DIM)
    partial_value = jnp.dot(head_out, out_proj, preferred_element_type=jnp.float32)
    column_count = feature_count // ffn_size
    attn_cols = lax.psum_scatter(
        partial_value.astype(jnp.bfloat16), "ffn", scatter_dimension=1, tiled=True
    ).astype(jnp.float32)
    residual_cols = lax.dynamic_slice_in_dim(residual, ffn_index * column_count, column_count, 1)
    hidden_out = (residual_cols.astype(jnp.float32) + attn_cols).astype(jnp.bfloat16)
    hidden_wide = hidden_out.astype(jnp.float32)
    square_sum = lax.psum(jnp.sum(hidden_wide * hidden_wide, axis=1, keepdims=True), "ffn")
    mean_square = square_sum / feature_count
    gain_cols = lax.dynamic_slice_in_dim(norm_gain, ffn_index * column_count, column_count, 0)
    normed_cols = (
        hidden_wide * lax.rsqrt(mean_square + EPSILON) * gain_cols.astype(jnp.float32)
    ).astype(jnp.bfloat16)
    normed_half = lax.all_gather(normed_cols, "exp", axis=0, tiled=True)
    normed_all = lax.all_gather(normed_half, "ffn", axis=1, tiled=True)

    expert_ids = lax.broadcasted_iota(jnp.int32, (1, 1, EXPERTS), 2)
    route_hot = routes_all[:, :, None] == expert_ids
    blocks = group_rows // BLOCK_ROWS
    pair_count = BLOCK_ROWS * TOP
    pair_hot = route_hot.reshape(blocks, pair_count, EXPERTS).astype(jnp.bfloat16)
    earlier = (
        lax.broadcasted_iota(jnp.int32, (pair_count, pair_count), 1)
        < lax.broadcasted_iota(jnp.int32, (pair_count, pair_count), 0)
    ).astype(jnp.bfloat16)
    before = jnp.einsum("pq,bqx->bpx", earlier, pair_hot, preferred_element_type=jnp.float32)
    rank = jnp.sum(before * pair_hot.astype(jnp.float32), axis=2).astype(jnp.int32)
    block_base = lax.broadcasted_iota(jnp.int32, (blocks, 1), 0) * CAPACITY
    slot_index = (rank + block_base).reshape(group_rows, TOP)
    slot_count = blocks * CAPACITY
    local_count = gate_weight.shape[0]
    total_slots = local_count * slot_count
    local_expert = routes_all - exp_index * local_count
    is_local = (local_expert >= 0) & (local_expert < local_count)
    target = jnp.where(is_local, local_expert * slot_count + slot_index, -1)

    logits = jnp.dot(normed_all, router, preferred_element_type=jnp.float32)
    chosen = jnp.sum(jnp.where(route_hot, logits[:, None, :], 0.0), axis=2)
    raised = jnp.exp(chosen)
    gate_weights = raised / jnp.sum(raised, axis=1, keepdims=True)

    slot_ids = lax.broadcasted_iota(jnp.int32, (1, 1, total_slots), 2)
    slot_hit = target[:, :, None] == slot_ids
    combine = jnp.any(slot_hit, axis=1).astype(jnp.bfloat16)
    slot_weight = jnp.sum(jnp.where(slot_hit, gate_weights[:, :, None], 0.0), axis=(0, 1))
    dispatch_ids = lax.broadcasted_iota(jnp.int32, (total_slots, 1, 1), 0)
    dispatch = jnp.any(target[None, :, :] == dispatch_ids, axis=2).astype(jnp.bfloat16)
    grouped = jnp.dot(dispatch, normed_all, preferred_element_type=jnp.float32).astype(
        jnp.bfloat16
    )
    grouped = grouped.reshape(local_count, slot_count, feature_count)
    weighted = expert_ffn(
        grouped,
        gate_weight,
        up_weight,
        down_weight,
        slot_weight.reshape(local_count, slot_count, 1),
    ).reshape(total_slots, feature_count)
    mixture = jnp.stack(
        [
            jnp.dot(
                combine,
                weighted[:, part * column_count : (part + 1) * column_count],
                preferred_element_type=jnp.float32,
            ).astype(jnp.bfloat16)
            for part in range(ffn_size)
        ],
        axis=0,
    ).reshape(ffn_size * group_rows, column_count)
    moe_out = lax.psum_scatter(mixture, ("ffn", "exp"), scatter_dimension=0, tiled=True)
    return (hidden_out, moe_out)


def solution(mesh):
    in_specs = (
        P(("req", "exp"), None),
        P(("req", "exp"), "ffn"),
        P(("req", "exp"), None),
        P(("req", "exp"), None),
        P(),
        P(),
        P(),
        P(("req", "exp"), None),
        P(None, "ffn"),
        P("ffn", None),
        P(),
        P(),
        P("exp", None, "ffn"),
        P("exp", None, "ffn"),
        P("exp", "ffn", None),
    )
    out_specs = (P(("req", "exp"), "ffn"), P(("req", "exp"), "ffn"))
    return jax.shard_map(local, mesh=mesh, in_specs=in_specs, out_specs=out_specs, check_vma=False)
```

```python
import jax
import jax.numpy as jnp
from jax import lax
from jax.experimental import pallas as pl
from jax.experimental.pallas import tpu as pltpu
from jax.sharding import PartitionSpec as P

LATENT = 512
ROPE_DIM = 64
HEAD_DIM = 128
QKD = 576
EXPERTS = 32
TOP = 6
CAPACITY = 16
REQ_GRP = 2
CMAX = 1024
BLOCK_ROWS = 64


EPSILON = 1e-06
NEG_FILL = -1e30


SLOT_TILE = 128


def expert_kernel(rows_ref, gate_ref, up_ref, down_ref, scale_ref, out_ref):
    rows = rows_ref[0]
    contract = (((1,), (1,)), ((), ()))
    gate_part = lax.dot_general(rows, gate_ref[0], contract, preferred_element_type=jnp.float32)
    up_part = lax.dot_general(rows, up_ref[0], contract, preferred_element_type=jnp.float32)
    active = (gate_part / (1.0 + jnp.exp(-gate_part)) * up_part).astype(jnp.bfloat16)
    result = jnp.dot(active, down_ref[0], preferred_element_type=jnp.float32)
    out_ref[0] = (result * scale_ref[0]).astype(out_ref.dtype)


def expert_ffn(grouped, gate_weight, up_weight, down_weight, scale):
    local_count, slot_count, feature_count = grouped.shape
    hidden = gate_weight.shape[2]
    gate_rows = jnp.transpose(gate_weight, (0, 2, 1))
    up_rows = jnp.transpose(up_weight, (0, 2, 1))
    tile = min(SLOT_TILE, slot_count)
    return pl.pallas_call(
        expert_kernel,
        grid=(local_count, slot_count // tile),
        in_specs=[
            pl.BlockSpec((1, tile, feature_count), lambda j, m: (j, m, 0)),
            pl.BlockSpec((1, hidden, feature_count), lambda j, m: (j, 0, 0)),
            pl.BlockSpec((1, hidden, feature_count), lambda j, m: (j, 0, 0)),
            pl.BlockSpec((1, hidden, feature_count), lambda j, m: (j, 0, 0)),
            pl.BlockSpec((1, tile, 1), lambda j, m: (j, m, 0)),
        ],
        out_specs=pl.BlockSpec((1, tile, feature_count), lambda j, m: (j, m, 0)),
        out_shape=jax.ShapeDtypeStruct((local_count, slot_count, feature_count), jnp.bfloat16),
        compiler_params=pltpu.CompilerParams(
            dimension_semantics=("arbitrary", "arbitrary"),
            vmem_limit_bytes=56 * 1024 * 1024,
        ),
    )(grouped, gate_rows, up_rows, down_weight, scale)


def local(
    residual,
    queries,
    new_latent,
    cache_pool,
    page_table,
    cached_len,
    tenant_start,
    routes,
    value_up,
    out_proj,
    norm_gain,
    router,
    gate_weight,
    up_weight,
    down_weight,
):
    exp_size = lax.axis_size("exp")
    ffn_size = lax.axis_size("ffn")
    req_index = lax.axis_index("req")
    exp_index = lax.axis_index("exp")
    ffn_index = lax.axis_index("ffn")
    token_rows = residual.shape[0]
    feature_count = residual.shape[1]
    fresh_len = token_rows * exp_size // REQ_GRP
    first_token = (req_index * exp_size + exp_index) * token_rows
    request = first_token // fresh_len
    offset = first_token - request * fresh_len
    pool_pages = cache_pool.shape[0]
    page_width = cache_pool.shape[1]
    latent_pages = token_rows * QKD // page_width
    route_count = token_rows * TOP
    route_pages = -(-route_count // page_width)
    route_rows = jnp.pad(
        routes.reshape(route_count).astype(jnp.bfloat16),
        (0, route_pages * page_width - route_count),
    ).reshape(route_pages, page_width)
    packed_rows = pool_pages + latent_pages + route_pages
    share_rows = -(-packed_rows // (ffn_size * 8)) * 8
    packed = jnp.concatenate(
        [
            cache_pool,
            new_latent.reshape(latent_pages, page_width),
            route_rows,
            jnp.zeros((share_rows * ffn_size - packed_rows, page_width), jnp.bfloat16),
        ],
        axis=0,
    )
    share = lax.dynamic_slice_in_dim(packed, ffn_index * share_rows, share_rows, 0)
    gathered = lax.all_gather(share, ("exp", "ffn"), axis=0, tiled=False)
    gathered = gathered.reshape(exp_size, ffn_size * share_rows, page_width)
    stride = ffn_size * share_rows
    group_rows = exp_size * token_rows
    routes_all = (
        gathered[:, pool_pages + latent_pages : packed_rows]
        .reshape(exp_size, route_pages * page_width)[:, :route_count]
        .reshape(group_rows, TOP)
        .astype(jnp.int32)
    )
    flat_pages = gathered.reshape(exp_size * stride, page_width)
    pool_base = req_index * exp_size * pool_pages
    page_rows = page_table[request] - pool_base
    cached_rows = (page_rows // pool_pages) * stride + page_rows % pool_pages
    local_request = request - req_index * REQ_GRP
    fresh_devices = fresh_len // token_rows
    fresh_index = lax.broadcasted_iota(jnp.int32, (fresh_devices, latent_pages), 0)
    fresh_rows = (
        (local_request * fresh_devices + fresh_index) * stride
        + pool_pages
        + lax.broadcasted_iota(jnp.int32, (fresh_devices, latent_pages), 1)
    ).reshape(fresh_devices * latent_pages)
    key_rows = jnp.concatenate([cached_rows, fresh_rows], axis=0)
    all_keys = jnp.take(flat_pages, key_rows, axis=0, mode="clip").reshape(CMAX + fresh_len, QKD)
    heads_here = queries.shape[1] // QKD
    query_heads = queries.reshape(token_rows, heads_here, QKD)
    scale_factor = (HEAD_DIM + ROPE_DIM) ** (-0.5)
    scores = (
        jnp.einsum("thd,kd->thk", query_heads, all_keys, preferred_element_type=jnp.float32)
        * scale_factor
    )
    key_pos = lax.broadcasted_iota(jnp.int32, (1, CMAX + fresh_len), 1)
    tok_pos = offset + lax.broadcasted_iota(jnp.int32, (token_rows, 1), 0)
    cached_ok = (key_pos >= tenant_start[request]) & (key_pos < cached_len[request])
    fresh_ok = (key_pos >= CMAX) & (key_pos - CMAX <= tok_pos)
    visible = cached_ok | fresh_ok
    scores = jnp.where(visible[:, None, :], scores, NEG_FILL)
    top_score = jnp.max(scores, axis=2, keepdims=True)
    weights = jnp.exp(scores - top_score)
    attn_probs = (weights / jnp.sum(weights, axis=2, keepdims=True)).astype(jnp.bfloat16)
    latent_out = jnp.einsum(
        "thk,kl->thl", attn_probs, all_keys[:, :LATENT], preferred_element_type=jnp.float32
    ).astype(jnp.bfloat16)
    value_heads = value_up.reshape(LATENT, heads_here, HEAD_DIM)
    head_out = jnp.einsum(
        "thl,lhd->thd", latent_out, value_heads, preferred_element_type=jnp.float32
    )
    head_out = head_out.astype(jnp.bfloat16).reshape(token_rows, heads_here * HEAD_DIM)
    partial_value = jnp.dot(head_out, out_proj, preferred_element_type=jnp.float32)
    column_count = feature_count // ffn_size
    attn_cols = lax.psum_scatter(
        partial_value.astype(jnp.bfloat16), "ffn", scatter_dimension=1, tiled=True
    ).astype(jnp.float32)
    expert_ids = lax.broadcasted_iota(jnp.int32, (1, 1, EXPERTS), 2)
    route_hot = routes_all[:, :, None] == expert_ids
    blocks = group_rows // BLOCK_ROWS
    pair_count = BLOCK_ROWS * TOP
    pair_hot = route_hot.reshape(blocks, pair_count, EXPERTS).astype(jnp.bfloat16)
    earlier = (
        lax.broadcasted_iota(jnp.int32, (pair_count, pair_count), 1)
        < lax.broadcasted_iota(jnp.int32, (pair_count, pair_count), 0)
    ).astype(jnp.bfloat16)
    before = jnp.einsum("pq,bqx->bpx", earlier, pair_hot, preferred_element_type=jnp.float32)
    rank = jnp.sum(before * pair_hot.astype(jnp.float32), axis=2).astype(jnp.int32)
    block_base = lax.broadcasted_iota(jnp.int32, (blocks, 1), 0) * CAPACITY
    slot_index = (rank + block_base).reshape(group_rows, TOP)
    slot_count = blocks * CAPACITY
    local_count = gate_weight.shape[0]
    total_slots = local_count * slot_count
    local_expert = routes_all - exp_index * local_count
    is_local = (local_expert >= 0) & (local_expert < local_count)
    target = jnp.where(is_local, local_expert * slot_count + slot_index, -1)

    slot_ids = lax.broadcasted_iota(jnp.int32, (1, 1, total_slots), 2)
    combine = jnp.any(target[:, :, None] == slot_ids, axis=1).astype(jnp.bfloat16)
    dispatch_ids = lax.broadcasted_iota(jnp.int32, (total_slots, 1, 1), 0)
    dispatch = jnp.any(target[None, :, :] == dispatch_ids, axis=2).astype(jnp.bfloat16)
    attn_cols, target, combine, dispatch = lax.optimization_barrier(
        (attn_cols, target, combine, dispatch)
    )
    residual_cols = lax.dynamic_slice_in_dim(residual, ffn_index * column_count, column_count, 1)
    hidden_out = (residual_cols.astype(jnp.float32) + attn_cols).astype(jnp.bfloat16)
    hidden_wide = hidden_out.astype(jnp.float32)
    square_sum = lax.psum(jnp.sum(hidden_wide * hidden_wide, axis=1, keepdims=True), "ffn")
    mean_square = square_sum / feature_count
    gain_cols = lax.dynamic_slice_in_dim(norm_gain, ffn_index * column_count, column_count, 0)
    normed_cols = (
        hidden_wide * lax.rsqrt(mean_square + EPSILON) * gain_cols.astype(jnp.float32)
    ).astype(jnp.bfloat16)
    normed_half = lax.all_gather(normed_cols, "exp", axis=0, tiled=True)
    normed_all = lax.all_gather(normed_half, "ffn", axis=1, tiled=True)

    logits = jnp.dot(normed_all, router, preferred_element_type=jnp.float32)
    chosen = jnp.sum(jnp.where(route_hot, logits[:, None, :], 0.0), axis=2)
    raised = jnp.exp(chosen)
    gate_weights = raised / jnp.sum(raised, axis=1, keepdims=True)

    slot_hit = target[:, :, None] == slot_ids
    slot_weight = jnp.sum(jnp.where(slot_hit, gate_weights[:, :, None], 0.0), axis=(0, 1))
    grouped = jnp.dot(dispatch, normed_all, preferred_element_type=jnp.float32).astype(
        jnp.bfloat16
    )
    grouped = grouped.reshape(local_count, slot_count, feature_count)
    weighted = expert_ffn(
        grouped,
        gate_weight,
        up_weight,
        down_weight,
        slot_weight.reshape(local_count, slot_count, 1),
    ).reshape(total_slots, feature_count)
    mixture = jnp.dot(combine, weighted, preferred_element_type=jnp.float32).astype(jnp.bfloat16)
    moe_cols = lax.psum_scatter(mixture, "ffn", scatter_dimension=1, tiled=True)
    moe_out = lax.psum_scatter(moe_cols, "exp", scatter_dimension=0, tiled=True)
    return (hidden_out, moe_out)


def solution(mesh):
    in_specs = (
        P(("req", "exp"), None),
        P(("req", "exp"), "ffn"),
        P(("req", "exp"), None),
        P(("req", "exp"), None),
        P(),
        P(),
        P(),
        P(("req", "exp"), None),
        P(None, "ffn"),
        P("ffn", None),
        P(),
        P(),
        P("exp", None, "ffn"),
        P("exp", None, "ffn"),
        P("exp", "ffn", None),
    )
    out_specs = (P(("req", "exp"), "ffn"), P(("req", "exp"), "ffn"))
    return jax.shard_map(local, mesh=mesh, in_specs=in_specs, out_specs=out_specs, check_vma=False)
```

```python
import jax
import jax.numpy as jnp
from jax import lax
from jax.experimental import pallas as pl
from jax.experimental.pallas import tpu as pltpu
from jax.sharding import PartitionSpec as P

LATENT = 512
ROPE_DIM = 64
HEAD_DIM = 128
QKD = 576
EXPERTS = 32
TOP = 6
CAPACITY = 16
REQ_GRP = 2
CMAX = 1024
BLOCK_ROWS = 64


EPSILON = 1e-06
NEG_FILL = -1e30


SLOT_TILE = 512
HIDDEN_STEPS = 2


def expert_kernel(rows_ref, gate_ref, up_ref, down_ref, scale_ref, out_ref, acc_ref):
    step = pl.program_id(2)

    @pl.when(step == 0)
    def _():
        acc_ref[...] = jnp.zeros_like(acc_ref)

    rows = rows_ref[0]
    contract = (((1,), (1,)), ((), ()))
    gate_part = lax.dot_general(rows, gate_ref[0], contract, preferred_element_type=jnp.float32)
    up_part = lax.dot_general(rows, up_ref[0], contract, preferred_element_type=jnp.float32)
    active = (gate_part / (1.0 + jnp.exp(-gate_part)) * up_part).astype(jnp.bfloat16)
    acc_ref[...] += jnp.dot(active, down_ref[0], preferred_element_type=jnp.float32)

    @pl.when(step == pl.num_programs(2) - 1)
    def _():
        out_ref[0] = (acc_ref[...] * scale_ref[0]).astype(out_ref.dtype)


def expert_ffn(grouped, gate_weight, up_weight, down_weight, scale):
    local_count, slot_count, feature_count = grouped.shape
    hidden = gate_weight.shape[2]
    gate_rows = jnp.transpose(gate_weight, (0, 2, 1))
    up_rows = jnp.transpose(up_weight, (0, 2, 1))
    tile = min(SLOT_TILE, slot_count)
    steps = HIDDEN_STEPS if hidden % (HIDDEN_STEPS * 8) == 0 else 1
    part = hidden // steps
    return pl.pallas_call(
        expert_kernel,
        grid=(local_count, slot_count // tile, steps),
        in_specs=[
            pl.BlockSpec((1, tile, feature_count), lambda j, m, h: (j, m, 0)),
            pl.BlockSpec((1, part, feature_count), lambda j, m, h: (j, h, 0)),
            pl.BlockSpec((1, part, feature_count), lambda j, m, h: (j, h, 0)),
            pl.BlockSpec((1, part, feature_count), lambda j, m, h: (j, h, 0)),
            pl.BlockSpec((1, tile, 1), lambda j, m, h: (j, m, 0)),
        ],
        out_specs=pl.BlockSpec((1, tile, feature_count), lambda j, m, h: (j, m, 0)),
        out_shape=jax.ShapeDtypeStruct((local_count, slot_count, feature_count), jnp.bfloat16),
        scratch_shapes=[pltpu.VMEM((tile, feature_count), jnp.float32)],
        compiler_params=pltpu.CompilerParams(
            dimension_semantics=("arbitrary", "arbitrary", "arbitrary"),
            vmem_limit_bytes=56 * 1024 * 1024,
        ),
    )(grouped, gate_rows, up_rows, down_weight, scale)


def local(
    residual,
    queries,
    new_latent,
    cache_pool,
    page_table,
    cached_len,
    tenant_start,
    routes,
    value_up,
    out_proj,
    norm_gain,
    router,
    gate_weight,
    up_weight,
    down_weight,
):
    exp_size = lax.axis_size("exp")
    ffn_size = lax.axis_size("ffn")
    req_index = lax.axis_index("req")
    exp_index = lax.axis_index("exp")
    ffn_index = lax.axis_index("ffn")
    token_rows = residual.shape[0]
    feature_count = residual.shape[1]
    fresh_len = token_rows * exp_size // REQ_GRP
    first_token = (req_index * exp_size + exp_index) * token_rows
    request = first_token // fresh_len
    offset = first_token - request * fresh_len
    pool_pages = cache_pool.shape[0]
    page_width = cache_pool.shape[1]
    latent_pages = token_rows * QKD // page_width
    route_count = token_rows * TOP
    route_pages = -(-route_count // page_width)
    route_rows = jnp.pad(
        routes.reshape(route_count).astype(jnp.bfloat16),
        (0, route_pages * page_width - route_count),
    ).reshape(route_pages, page_width)
    packed_rows = pool_pages + latent_pages + route_pages
    share_rows = -(-packed_rows // (ffn_size * 8)) * 8
    packed = jnp.concatenate(
        [
            cache_pool,
            new_latent.reshape(latent_pages, page_width),
            route_rows,
            jnp.zeros((share_rows * ffn_size - packed_rows, page_width), jnp.bfloat16),
        ],
        axis=0,
    )
    share = lax.dynamic_slice_in_dim(packed, ffn_index * share_rows, share_rows, 0)
    gathered = lax.all_gather(share, ("exp", "ffn"), axis=0, tiled=False)
    gathered = gathered.reshape(exp_size, ffn_size * share_rows, page_width)
    stride = ffn_size * share_rows
    group_rows = exp_size * token_rows
    routes_all = (
        gathered[:, pool_pages + latent_pages : packed_rows]
        .reshape(exp_size, route_pages * page_width)[:, :route_count]
        .reshape(group_rows, TOP)
        .astype(jnp.int32)
    )
    flat_pages = gathered.reshape(exp_size * stride, page_width)
    pool_base = req_index * exp_size * pool_pages
    page_rows = page_table[request] - pool_base
    cached_rows = (page_rows // pool_pages) * stride + page_rows % pool_pages
    local_request = request - req_index * REQ_GRP
    fresh_devices = fresh_len // token_rows
    fresh_index = lax.broadcasted_iota(jnp.int32, (fresh_devices, latent_pages), 0)
    fresh_rows = (
        (local_request * fresh_devices + fresh_index) * stride
        + pool_pages
        + lax.broadcasted_iota(jnp.int32, (fresh_devices, latent_pages), 1)
    ).reshape(fresh_devices * latent_pages)
    key_rows = jnp.concatenate([cached_rows, fresh_rows], axis=0)
    all_keys = jnp.take(flat_pages, key_rows, axis=0, mode="clip").reshape(CMAX + fresh_len, QKD)
    heads_here = queries.shape[1] // QKD
    query_heads = queries.reshape(token_rows, heads_here, QKD)
    scale_factor = (HEAD_DIM + ROPE_DIM) ** (-0.5)
    scores = (
        jnp.einsum("thd,kd->thk", query_heads, all_keys, preferred_element_type=jnp.float32)
        * scale_factor
    )
    key_pos = lax.broadcasted_iota(jnp.int32, (1, CMAX + fresh_len), 1)
    tok_pos = offset + lax.broadcasted_iota(jnp.int32, (token_rows, 1), 0)
    cached_ok = (key_pos >= tenant_start[request]) & (key_pos < cached_len[request])
    fresh_ok = (key_pos >= CMAX) & (key_pos - CMAX <= tok_pos)
    visible = cached_ok | fresh_ok
    scores = jnp.where(visible[:, None, :], scores, NEG_FILL)
    top_score = jnp.max(scores, axis=2, keepdims=True)
    weights = jnp.exp(scores - top_score)
    attn_probs = (weights / jnp.sum(weights, axis=2, keepdims=True)).astype(jnp.bfloat16)
    latent_out = jnp.einsum(
        "thk,kl->thl", attn_probs, all_keys[:, :LATENT], preferred_element_type=jnp.float32
    ).astype(jnp.bfloat16)
    value_heads = value_up.reshape(LATENT, heads_here, HEAD_DIM)
    head_out = jnp.einsum(
        "thl,lhd->thd", latent_out, value_heads, preferred_element_type=jnp.float32
    )
    head_out = head_out.astype(jnp.bfloat16).reshape(token_rows, heads_here * HEAD_DIM)
    partial_value = jnp.dot(head_out, out_proj, preferred_element_type=jnp.float32)
    column_count = feature_count // ffn_size
    attn_cols = lax.psum_scatter(
        partial_value.astype(jnp.bfloat16), "ffn", scatter_dimension=1, tiled=True
    ).astype(jnp.float32)
    residual_cols = lax.dynamic_slice_in_dim(residual, ffn_index * column_count, column_count, 1)
    hidden_out = (residual_cols.astype(jnp.float32) + attn_cols).astype(jnp.bfloat16)
    hidden_wide = hidden_out.astype(jnp.float32)
    square_sum = lax.psum(jnp.sum(hidden_wide * hidden_wide, axis=1, keepdims=True), "ffn")
    mean_square = square_sum / feature_count
    gain_cols = lax.dynamic_slice_in_dim(norm_gain, ffn_index * column_count, column_count, 0)
    normed_cols = (
        hidden_wide * lax.rsqrt(mean_square + EPSILON) * gain_cols.astype(jnp.float32)
    ).astype(jnp.bfloat16)
    normed_half = lax.all_gather(normed_cols, "exp", axis=0, tiled=True)
    normed_all = lax.all_gather(normed_half, "ffn", axis=1, tiled=True)

    expert_ids = lax.broadcasted_iota(jnp.int32, (1, 1, EXPERTS), 2)
    route_hot = routes_all[:, :, None] == expert_ids
    blocks = group_rows // BLOCK_ROWS
    pair_count = BLOCK_ROWS * TOP
    pair_hot = route_hot.reshape(blocks, pair_count, EXPERTS).astype(jnp.bfloat16)
    earlier = (
        lax.broadcasted_iota(jnp.int32, (pair_count, pair_count), 1)
        < lax.broadcasted_iota(jnp.int32, (pair_count, pair_count), 0)
    ).astype(jnp.bfloat16)
    before = jnp.einsum("pq,bqx->bpx", earlier, pair_hot, preferred_element_type=jnp.float32)
    rank = jnp.sum(before * pair_hot.astype(jnp.float32), axis=2).astype(jnp.int32)
    block_base = lax.broadcasted_iota(jnp.int32, (blocks, 1), 0) * CAPACITY
    slot_index = (rank + block_base).reshape(group_rows, TOP)
    slot_count = blocks * CAPACITY
    local_count = gate_weight.shape[0]
    total_slots = local_count * slot_count
    local_expert = routes_all - exp_index * local_count
    is_local = (local_expert >= 0) & (local_expert < local_count)
    target = jnp.where(is_local, local_expert * slot_count + slot_index, -1)

    logits = jnp.dot(normed_all, router, preferred_element_type=jnp.float32)
    chosen = jnp.sum(jnp.where(route_hot, logits[:, None, :], 0.0), axis=2)
    raised = jnp.exp(chosen)
    gate_weights = raised / jnp.sum(raised, axis=1, keepdims=True)

    slot_ids = lax.broadcasted_iota(jnp.int32, (1, 1, total_slots), 2)
    slot_hit = target[:, :, None] == slot_ids
    combine = jnp.any(slot_hit, axis=1).astype(jnp.bfloat16)
    slot_weight = jnp.sum(jnp.where(slot_hit, gate_weights[:, :, None], 0.0), axis=(0, 1))
    dispatch_ids = lax.broadcasted_iota(jnp.int32, (total_slots, 1, 1), 0)
    dispatch = jnp.any(target[None, :, :] == dispatch_ids, axis=2).astype(jnp.bfloat16)
    grouped = jnp.dot(dispatch, normed_all, preferred_element_type=jnp.float32).astype(
        jnp.bfloat16
    )
    grouped = grouped.reshape(local_count, slot_count, feature_count)
    weighted = expert_ffn(
        grouped,
        gate_weight,
        up_weight,
        down_weight,
        slot_weight.reshape(local_count, slot_count, 1),
    ).reshape(total_slots, feature_count)
    mixture = jnp.dot(combine, weighted, preferred_element_type=jnp.float32).astype(jnp.bfloat16)
    moe_cols = lax.psum_scatter(mixture, "ffn", scatter_dimension=1, tiled=True)
    moe_out = lax.psum_scatter(moe_cols, "exp", scatter_dimension=0, tiled=True)
    return (hidden_out, moe_out)


def solution(mesh):
    in_specs = (
        P(("req", "exp"), None),
        P(("req", "exp"), "ffn"),
        P(("req", "exp"), None),
        P(("req", "exp"), None),
        P(),
        P(),
        P(),
        P(("req", "exp"), None),
        P(None, "ffn"),
        P("ffn", None),
        P(),
        P(),
        P("exp", None, "ffn"),
        P("exp", None, "ffn"),
        P("exp", "ffn", None),
    )
    out_specs = (P(("req", "exp"), "ffn"), P(("req", "exp"), "ffn"))
    return jax.shard_map(local, mesh=mesh, in_specs=in_specs, out_specs=out_specs, check_vma=False)
```

```python
import jax
import jax.numpy as jnp
from jax import lax
from jax.experimental import pallas as pl
from jax.experimental.pallas import tpu as pltpu
from jax.sharding import PartitionSpec as P

LATENT = 512
ROPE_DIM = 64
HEAD_DIM = 128
QKD = 576
EXPERTS = 32
TOP = 6
CAPACITY = 16
REQ_GRP = 2
CMAX = 1024
BLOCK_ROWS = 64


EPSILON = 1e-06
NEG_FILL = -1e30


SLOT_TILE = 512


def expert_kernel(rows_ref, gate_ref, up_ref, down_ref, scale_ref, out_ref):
    columns = rows_ref[...]
    gate_part = jnp.dot(gate_ref[0], columns, preferred_element_type=jnp.float32)
    up_part = jnp.dot(up_ref[0], columns, preferred_element_type=jnp.float32)
    active = (gate_part / (1.0 + jnp.exp(-gate_part)) * up_part).astype(jnp.bfloat16)
    contract = (((0,), (0,)), ((), ()))
    result = lax.dot_general(active, down_ref[0], contract, preferred_element_type=jnp.float32)
    out_ref[0] = (result * scale_ref[0]).astype(out_ref.dtype)


def expert_ffn(grouped_t, gate_weight, up_weight, down_weight, scale):
    feature_count = grouped_t.shape[0]
    local_count, slot_count, _ = scale.shape
    hidden = gate_weight.shape[2]
    gate_rows = jnp.transpose(gate_weight, (0, 2, 1))
    up_rows = jnp.transpose(up_weight, (0, 2, 1))
    tile = min(SLOT_TILE, slot_count)
    tiles = slot_count // tile
    return pl.pallas_call(
        expert_kernel,
        grid=(local_count, tiles),
        in_specs=[
            pl.BlockSpec((feature_count, tile), lambda j, m: (0, j * tiles + m)),
            pl.BlockSpec((1, hidden, feature_count), lambda j, m: (j, 0, 0)),
            pl.BlockSpec((1, hidden, feature_count), lambda j, m: (j, 0, 0)),
            pl.BlockSpec((1, hidden, feature_count), lambda j, m: (j, 0, 0)),
            pl.BlockSpec((1, tile, 1), lambda j, m: (j, m, 0)),
        ],
        out_specs=pl.BlockSpec((1, tile, feature_count), lambda j, m: (j, m, 0)),
        out_shape=jax.ShapeDtypeStruct((local_count, slot_count, feature_count), jnp.bfloat16),
        compiler_params=pltpu.CompilerParams(
            dimension_semantics=("arbitrary", "arbitrary"),
            vmem_limit_bytes=56 * 1024 * 1024,
        ),
    )(grouped_t, gate_rows, up_rows, down_weight, scale)


def local(
    residual,
    queries,
    new_latent,
    cache_pool,
    page_table,
    cached_len,
    tenant_start,
    routes,
    value_up,
    out_proj,
    norm_gain,
    router,
    gate_weight,
    up_weight,
    down_weight,
):
    exp_size = lax.axis_size("exp")
    ffn_size = lax.axis_size("ffn")
    req_index = lax.axis_index("req")
    exp_index = lax.axis_index("exp")
    ffn_index = lax.axis_index("ffn")
    token_rows = residual.shape[0]
    feature_count = residual.shape[1]
    fresh_len = token_rows * exp_size // REQ_GRP
    first_token = (req_index * exp_size + exp_index) * token_rows
    request = first_token // fresh_len
    offset = first_token - request * fresh_len
    pool_pages = cache_pool.shape[0]
    page_width = cache_pool.shape[1]
    latent_pages = token_rows * QKD // page_width
    route_count = token_rows * TOP
    route_pages = -(-route_count // page_width)
    route_rows = jnp.pad(
        routes.reshape(route_count).astype(jnp.bfloat16),
        (0, route_pages * page_width - route_count),
    ).reshape(route_pages, page_width)
    packed_rows = pool_pages + latent_pages + route_pages
    share_rows = -(-packed_rows // (ffn_size * 8)) * 8
    packed = jnp.concatenate(
        [
            cache_pool,
            new_latent.reshape(latent_pages, page_width),
            route_rows,
            jnp.zeros((share_rows * ffn_size - packed_rows, page_width), jnp.bfloat16),
        ],
        axis=0,
    )
    share = lax.dynamic_slice_in_dim(packed, ffn_index * share_rows, share_rows, 0)
    gathered = lax.all_gather(share, ("exp", "ffn"), axis=0, tiled=False)
    gathered = gathered.reshape(exp_size, ffn_size * share_rows, page_width)
    stride = ffn_size * share_rows
    group_rows = exp_size * token_rows
    routes_all = (
        gathered[:, pool_pages + latent_pages : packed_rows]
        .reshape(exp_size, route_pages * page_width)[:, :route_count]
        .reshape(group_rows, TOP)
        .astype(jnp.int32)
    )
    flat_pages = gathered.reshape(exp_size * stride, page_width)
    pool_base = req_index * exp_size * pool_pages
    page_rows = page_table[request] - pool_base
    cached_rows = (page_rows // pool_pages) * stride + page_rows % pool_pages
    local_request = request - req_index * REQ_GRP
    fresh_devices = fresh_len // token_rows
    fresh_index = lax.broadcasted_iota(jnp.int32, (fresh_devices, latent_pages), 0)
    fresh_rows = (
        (local_request * fresh_devices + fresh_index) * stride
        + pool_pages
        + lax.broadcasted_iota(jnp.int32, (fresh_devices, latent_pages), 1)
    ).reshape(fresh_devices * latent_pages)
    key_rows = jnp.concatenate([cached_rows, fresh_rows], axis=0)
    all_keys = jnp.take(flat_pages, key_rows, axis=0, mode="clip").reshape(CMAX + fresh_len, QKD)
    heads_here = queries.shape[1] // QKD
    query_heads = queries.reshape(token_rows, heads_here, QKD)
    scale_factor = (HEAD_DIM + ROPE_DIM) ** (-0.5)
    scores = (
        jnp.einsum("thd,kd->thk", query_heads, all_keys, preferred_element_type=jnp.float32)
        * scale_factor
    )
    key_pos = lax.broadcasted_iota(jnp.int32, (1, CMAX + fresh_len), 1)
    tok_pos = offset + lax.broadcasted_iota(jnp.int32, (token_rows, 1), 0)
    cached_ok = (key_pos >= tenant_start[request]) & (key_pos < cached_len[request])
    fresh_ok = (key_pos >= CMAX) & (key_pos - CMAX <= tok_pos)
    visible = cached_ok | fresh_ok
    scores = jnp.where(visible[:, None, :], scores, NEG_FILL)
    top_score = jnp.max(scores, axis=2, keepdims=True)
    weights = jnp.exp(scores - top_score)
    attn_probs = (weights / jnp.sum(weights, axis=2, keepdims=True)).astype(jnp.bfloat16)
    latent_out = jnp.einsum(
        "thk,kl->thl", attn_probs, all_keys[:, :LATENT], preferred_element_type=jnp.float32
    ).astype(jnp.bfloat16)
    value_heads = value_up.reshape(LATENT, heads_here, HEAD_DIM)
    head_out = jnp.einsum(
        "thl,lhd->thd", latent_out, value_heads, preferred_element_type=jnp.float32
    )
    head_out = head_out.astype(jnp.bfloat16).reshape(token_rows, heads_here * HEAD_DIM)
    partial_value = jnp.dot(head_out, out_proj, preferred_element_type=jnp.float32)
    column_count = feature_count // ffn_size
    attn_cols = lax.psum_scatter(
        partial_value.astype(jnp.bfloat16), "ffn", scatter_dimension=1, tiled=True
    ).astype(jnp.float32)
    residual_cols = lax.dynamic_slice_in_dim(residual, ffn_index * column_count, column_count, 1)
    hidden_out = (residual_cols.astype(jnp.float32) + attn_cols).astype(jnp.bfloat16)
    hidden_wide = hidden_out.astype(jnp.float32)
    square_sum = lax.psum(jnp.sum(hidden_wide * hidden_wide, axis=1, keepdims=True), "ffn")
    mean_square = square_sum / feature_count
    gain_cols = lax.dynamic_slice_in_dim(norm_gain, ffn_index * column_count, column_count, 0)
    normed_cols = (
        hidden_wide * lax.rsqrt(mean_square + EPSILON) * gain_cols.astype(jnp.float32)
    ).astype(jnp.bfloat16)
    normed_half = lax.all_gather(normed_cols, "exp", axis=0, tiled=True)
    normed_all = lax.all_gather(normed_half, "ffn", axis=1, tiled=True)

    expert_ids = lax.broadcasted_iota(jnp.int32, (1, 1, EXPERTS), 2)
    route_hot = routes_all[:, :, None] == expert_ids
    blocks = group_rows // BLOCK_ROWS
    pair_count = BLOCK_ROWS * TOP
    pair_hot = route_hot.reshape(blocks, pair_count, EXPERTS).astype(jnp.bfloat16)
    earlier = (
        lax.broadcasted_iota(jnp.int32, (pair_count, pair_count), 1)
        < lax.broadcasted_iota(jnp.int32, (pair_count, pair_count), 0)
    ).astype(jnp.bfloat16)
    before = jnp.einsum("pq,bqx->bpx", earlier, pair_hot, preferred_element_type=jnp.float32)
    rank = jnp.sum(before * pair_hot.astype(jnp.float32), axis=2).astype(jnp.int32)
    block_base = lax.broadcasted_iota(jnp.int32, (blocks, 1), 0) * CAPACITY
    slot_index = (rank + block_base).reshape(group_rows, TOP)
    slot_count = blocks * CAPACITY
    local_count = gate_weight.shape[0]
    total_slots = local_count * slot_count
    local_expert = routes_all - exp_index * local_count
    is_local = (local_expert >= 0) & (local_expert < local_count)
    target = jnp.where(is_local, local_expert * slot_count + slot_index, -1)

    logits = jnp.dot(normed_all, router, preferred_element_type=jnp.float32)
    chosen = jnp.sum(jnp.where(route_hot, logits[:, None, :], 0.0), axis=2)
    raised = jnp.exp(chosen)
    gate_weights = raised / jnp.sum(raised, axis=1, keepdims=True)

    slot_ids = lax.broadcasted_iota(jnp.int32, (1, 1, total_slots), 2)
    slot_hit = target[:, :, None] == slot_ids
    combine = jnp.any(slot_hit, axis=1).astype(jnp.bfloat16)
    slot_weight = jnp.sum(jnp.where(slot_hit, gate_weights[:, :, None], 0.0), axis=(0, 1))
    grouped_t = jnp.einsum(
        "td,ts->ds", normed_all, combine, preferred_element_type=jnp.float32
    ).astype(jnp.bfloat16)
    weighted = expert_ffn(
        grouped_t,
        gate_weight,
        up_weight,
        down_weight,
        slot_weight.reshape(local_count, slot_count, 1),
    ).reshape(total_slots, feature_count)
    mixture = jnp.dot(combine, weighted, preferred_element_type=jnp.float32).astype(jnp.bfloat16)
    moe_cols = lax.psum_scatter(mixture, "ffn", scatter_dimension=1, tiled=True)
    moe_out = lax.psum_scatter(moe_cols, "exp", scatter_dimension=0, tiled=True)
    return (hidden_out, moe_out)


def solution(mesh):
    in_specs = (
        P(("req", "exp"), None),
        P(("req", "exp"), "ffn"),
        P(("req", "exp"), None),
        P(("req", "exp"), None),
        P(),
        P(),
        P(),
        P(("req", "exp"), None),
        P(None, "ffn"),
        P("ffn", None),
        P(),
        P(),
        P("exp", None, "ffn"),
        P("exp", None, "ffn"),
        P("exp", "ffn", None),
    )
    out_specs = (P(("req", "exp"), "ffn"), P(("req", "exp"), "ffn"))
    return jax.shard_map(local, mesh=mesh, in_specs=in_specs, out_specs=out_specs, check_vma=False)
```

```python
import jax
import jax.numpy as jnp
from jax import lax
from jax.experimental import pallas as pl
from jax.experimental.pallas import tpu as pltpu
from jax.sharding import PartitionSpec as P

LATENT = 512
ROPE_DIM = 64
HEAD_DIM = 128
QKD = 576
EXPERTS = 32
TOP = 6
CAPACITY = 16
REQ_GRP = 2
CMAX = 1024
BLOCK_ROWS = 64


EPSILON = 1e-06
NEG_FILL = -1e30


SLOT_TILE = 512


def expert_kernel(rows_ref, gate_ref, up_ref, down_ref, scale_ref, out_ref):
    columns = rows_ref[...]
    gate_part = jnp.dot(gate_ref[0], columns, preferred_element_type=jnp.float32)
    up_part = jnp.dot(up_ref[0], columns, preferred_element_type=jnp.float32)
    active = (gate_part / (1.0 + jnp.exp(-gate_part)) * up_part).astype(jnp.bfloat16)
    contract = (((0,), (0,)), ((), ()))
    result = lax.dot_general(active, down_ref[0], contract, preferred_element_type=jnp.float32)
    out_ref[0] = (result * scale_ref[0]).astype(out_ref.dtype)


def expert_ffn(grouped_t, gate_weight, up_weight, down_weight, scale):
    feature_count = grouped_t.shape[0]
    local_count, slot_count, _ = scale.shape
    hidden = gate_weight.shape[2]
    gate_rows = jnp.transpose(gate_weight, (0, 2, 1))
    up_rows = jnp.transpose(up_weight, (0, 2, 1))
    tile = min(SLOT_TILE, slot_count)
    tiles = slot_count // tile
    return pl.pallas_call(
        expert_kernel,
        grid=(local_count, tiles),
        in_specs=[
            pl.BlockSpec((feature_count, tile), lambda j, m: (0, j * tiles + m)),
            pl.BlockSpec((1, hidden, feature_count), lambda j, m: (j, 0, 0)),
            pl.BlockSpec((1, hidden, feature_count), lambda j, m: (j, 0, 0)),
            pl.BlockSpec((1, hidden, feature_count), lambda j, m: (j, 0, 0)),
            pl.BlockSpec((1, tile, 1), lambda j, m: (j, m, 0)),
        ],
        out_specs=pl.BlockSpec((1, tile, feature_count), lambda j, m: (j, m, 0)),
        out_shape=jax.ShapeDtypeStruct((local_count, slot_count, feature_count), jnp.bfloat16),
        compiler_params=pltpu.CompilerParams(
            dimension_semantics=("arbitrary", "arbitrary"),
            vmem_limit_bytes=56 * 1024 * 1024,
        ),
    )(grouped_t, gate_rows, up_rows, down_weight, scale)


def pair_swap(x):
    return lax.ppermute(x, "ffn", [(0, 1), (1, 0)])


def ffn_sum_scatter(x, ffn_index, ffn_size, axis):
    if ffn_size != 2:
        return lax.psum_scatter(x, "ffn", scatter_dimension=axis, tiled=True).astype(jnp.float32)
    width = x.shape[axis] // 2
    mine = lax.dynamic_slice_in_dim(x, ffn_index * width, width, axis)
    other = lax.dynamic_slice_in_dim(x, (1 - ffn_index) * width, width, axis)
    return mine.astype(jnp.float32) + pair_swap(other).astype(jnp.float32)


def ffn_gather_columns(x, ffn_index, ffn_size):
    if ffn_size != 2:
        return lax.all_gather(x, "ffn", axis=1, tiled=True)
    other = pair_swap(x)
    first = jnp.where(ffn_index == 0, x, other)
    second = jnp.where(ffn_index == 0, other, x)
    return jnp.concatenate([first, second], axis=1)


def local(
    residual,
    queries,
    new_latent,
    cache_pool,
    page_table,
    cached_len,
    tenant_start,
    routes,
    value_up,
    out_proj,
    norm_gain,
    router,
    gate_weight,
    up_weight,
    down_weight,
):
    exp_size = lax.axis_size("exp")
    ffn_size = lax.axis_size("ffn")
    req_index = lax.axis_index("req")
    exp_index = lax.axis_index("exp")
    ffn_index = lax.axis_index("ffn")
    token_rows = residual.shape[0]
    feature_count = residual.shape[1]
    fresh_len = token_rows * exp_size // REQ_GRP
    first_token = (req_index * exp_size + exp_index) * token_rows
    request = first_token // fresh_len
    offset = first_token - request * fresh_len
    pool_pages = cache_pool.shape[0]
    page_width = cache_pool.shape[1]
    latent_pages = token_rows * QKD // page_width
    route_count = token_rows * TOP
    route_pages = -(-route_count // page_width)
    route_rows = jnp.pad(
        routes.reshape(route_count).astype(jnp.bfloat16),
        (0, route_pages * page_width - route_count),
    ).reshape(route_pages, page_width)
    packed_rows = pool_pages + latent_pages + route_pages
    share_rows = -(-packed_rows // (ffn_size * 8)) * 8
    packed = jnp.concatenate(
        [
            cache_pool,
            new_latent.reshape(latent_pages, page_width),
            route_rows,
            jnp.zeros((share_rows * ffn_size - packed_rows, page_width), jnp.bfloat16),
        ],
        axis=0,
    )
    share = lax.dynamic_slice_in_dim(packed, ffn_index * share_rows, share_rows, 0)
    gathered = lax.all_gather(share, ("exp", "ffn"), axis=0, tiled=False)
    gathered = gathered.reshape(exp_size, ffn_size * share_rows, page_width)
    stride = ffn_size * share_rows
    group_rows = exp_size * token_rows
    routes_all = (
        gathered[:, pool_pages + latent_pages : packed_rows]
        .reshape(exp_size, route_pages * page_width)[:, :route_count]
        .reshape(group_rows, TOP)
        .astype(jnp.int32)
    )
    flat_pages = gathered.reshape(exp_size * stride, page_width)
    pool_base = req_index * exp_size * pool_pages
    page_rows = page_table[request] - pool_base
    cached_rows = (page_rows // pool_pages) * stride + page_rows % pool_pages
    local_request = request - req_index * REQ_GRP
    fresh_devices = fresh_len // token_rows
    fresh_index = lax.broadcasted_iota(jnp.int32, (fresh_devices, latent_pages), 0)
    fresh_rows = (
        (local_request * fresh_devices + fresh_index) * stride
        + pool_pages
        + lax.broadcasted_iota(jnp.int32, (fresh_devices, latent_pages), 1)
    ).reshape(fresh_devices * latent_pages)
    key_rows = jnp.concatenate([cached_rows, fresh_rows], axis=0)
    all_keys = jnp.take(flat_pages, key_rows, axis=0, mode="clip").reshape(CMAX + fresh_len, QKD)
    heads_here = queries.shape[1] // QKD
    query_heads = queries.reshape(token_rows, heads_here, QKD)
    scale_factor = (HEAD_DIM + ROPE_DIM) ** (-0.5)
    scores = (
        jnp.einsum("thd,kd->thk", query_heads, all_keys, preferred_element_type=jnp.float32)
        * scale_factor
    )
    key_pos = lax.broadcasted_iota(jnp.int32, (1, CMAX + fresh_len), 1)
    tok_pos = offset + lax.broadcasted_iota(jnp.int32, (token_rows, 1), 0)
    cached_ok = (key_pos >= tenant_start[request]) & (key_pos < cached_len[request])
    fresh_ok = (key_pos >= CMAX) & (key_pos - CMAX <= tok_pos)
    visible = cached_ok | fresh_ok
    scores = jnp.where(visible[:, None, :], scores, NEG_FILL)
    top_score = jnp.max(scores, axis=2, keepdims=True)
    weights = jnp.exp(scores - top_score)
    attn_probs = (weights / jnp.sum(weights, axis=2, keepdims=True)).astype(jnp.bfloat16)
    latent_out = jnp.einsum(
        "thk,kl->thl", attn_probs, all_keys[:, :LATENT], preferred_element_type=jnp.float32
    ).astype(jnp.bfloat16)
    value_heads = value_up.reshape(LATENT, heads_here, HEAD_DIM)
    head_out = jnp.einsum(
        "thl,lhd->thd", latent_out, value_heads, preferred_element_type=jnp.float32
    )
    head_out = head_out.astype(jnp.bfloat16).reshape(token_rows, heads_here * HEAD_DIM)
    partial_value = jnp.dot(head_out, out_proj, preferred_element_type=jnp.float32)
    column_count = feature_count // ffn_size
    attn_cols = ffn_sum_scatter(partial_value.astype(jnp.bfloat16), ffn_index, ffn_size, 1)
    residual_cols = lax.dynamic_slice_in_dim(residual, ffn_index * column_count, column_count, 1)
    hidden_out = (residual_cols.astype(jnp.float32) + attn_cols).astype(jnp.bfloat16)
    hidden_wide = hidden_out.astype(jnp.float32)
    square_sum = lax.psum(jnp.sum(hidden_wide * hidden_wide, axis=1, keepdims=True), "ffn")
    mean_square = square_sum / feature_count
    gain_cols = lax.dynamic_slice_in_dim(norm_gain, ffn_index * column_count, column_count, 0)
    normed_cols = (
        hidden_wide * lax.rsqrt(mean_square + EPSILON) * gain_cols.astype(jnp.float32)
    ).astype(jnp.bfloat16)
    normed_half = lax.all_gather(normed_cols, "exp", axis=0, tiled=True)
    normed_all = ffn_gather_columns(normed_half, ffn_index, ffn_size)

    expert_ids = lax.broadcasted_iota(jnp.int32, (1, 1, EXPERTS), 2)
    route_hot = routes_all[:, :, None] == expert_ids
    blocks = group_rows // BLOCK_ROWS
    pair_count = BLOCK_ROWS * TOP
    pair_hot = route_hot.reshape(blocks, pair_count, EXPERTS).astype(jnp.bfloat16)
    earlier = (
        lax.broadcasted_iota(jnp.int32, (pair_count, pair_count), 1)
        < lax.broadcasted_iota(jnp.int32, (pair_count, pair_count), 0)
    ).astype(jnp.bfloat16)
    before = jnp.einsum("pq,bqx->bpx", earlier, pair_hot, preferred_element_type=jnp.float32)
    rank = jnp.sum(before * pair_hot.astype(jnp.float32), axis=2).astype(jnp.int32)
    block_base = lax.broadcasted_iota(jnp.int32, (blocks, 1), 0) * CAPACITY
    slot_index = (rank + block_base).reshape(group_rows, TOP)
    slot_count = blocks * CAPACITY
    local_count = gate_weight.shape[0]
    total_slots = local_count * slot_count
    local_expert = routes_all - exp_index * local_count
    is_local = (local_expert >= 0) & (local_expert < local_count)
    target = jnp.where(is_local, local_expert * slot_count + slot_index, -1)

    logits = jnp.dot(normed_all, router, preferred_element_type=jnp.float32)
    chosen = jnp.sum(jnp.where(route_hot, logits[:, None, :], 0.0), axis=2)
    raised = jnp.exp(chosen)
    gate_weights = raised / jnp.sum(raised, axis=1, keepdims=True)

    slot_ids = lax.broadcasted_iota(jnp.int32, (1, 1, total_slots), 2)
    slot_hit = target[:, :, None] == slot_ids
    combine = jnp.any(slot_hit, axis=1).astype(jnp.bfloat16)
    slot_weight = jnp.sum(jnp.where(slot_hit, gate_weights[:, :, None], 0.0), axis=(0, 1))
    grouped_t = jnp.einsum(
        "td,ts->ds", normed_all, combine, preferred_element_type=jnp.float32
    ).astype(jnp.bfloat16)
    weighted = expert_ffn(
        grouped_t,
        gate_weight,
        up_weight,
        down_weight,
        slot_weight.reshape(local_count, slot_count, 1),
    ).reshape(total_slots, feature_count)
    mixture = jnp.dot(combine, weighted, preferred_element_type=jnp.float32).astype(jnp.bfloat16)
    moe_cols = ffn_sum_scatter(mixture, ffn_index, ffn_size, 1).astype(jnp.bfloat16)
    moe_out = lax.psum_scatter(moe_cols, "exp", scatter_dimension=0, tiled=True)
    return (hidden_out, moe_out)


def solution(mesh):
    in_specs = (
        P(("req", "exp"), None),
        P(("req", "exp"), "ffn"),
        P(("req", "exp"), None),
        P(("req", "exp"), None),
        P(),
        P(),
        P(),
        P(("req", "exp"), None),
        P(None, "ffn"),
        P("ffn", None),
        P(),
        P(),
        P("exp", None, "ffn"),
        P("exp", None, "ffn"),
        P("exp", "ffn", None),
    )
    out_specs = (P(("req", "exp"), "ffn"), P(("req", "exp"), "ffn"))
    return jax.shard_map(local, mesh=mesh, in_specs=in_specs, out_specs=out_specs, check_vma=False)
```

```python
import jax
import jax.numpy as jnp
from jax import lax
from jax.experimental import pallas as pl
from jax.experimental.pallas import tpu as pltpu
from jax.sharding import PartitionSpec as P

LATENT = 512
ROPE_DIM = 64
HEAD_DIM = 128
QKD = 576
EXPERTS = 32
TOP = 6
CAPACITY = 16
REQ_GRP = 2
CMAX = 1024
BLOCK_ROWS = 64


EPSILON = 1e-06
NEG_FILL = -1e30


SLOT_TILE = 512


def expert_kernel(rows_ref, gate_ref, up_ref, down_ref, scale_ref, out_ref):
    columns = rows_ref[...]
    gate_part = jnp.dot(gate_ref[0], columns, preferred_element_type=jnp.float32)
    up_part = jnp.dot(up_ref[0], columns, preferred_element_type=jnp.float32)
    active = (gate_part / (1.0 + jnp.exp(-gate_part)) * up_part).astype(jnp.bfloat16)
    contract = (((0,), (0,)), ((), ()))
    result = lax.dot_general(active, down_ref[0], contract, preferred_element_type=jnp.float32)
    out_ref[0] = (result * scale_ref[0]).astype(out_ref.dtype)


def expert_ffn(grouped_t, gate_weight, up_weight, down_weight, scale):
    feature_count = grouped_t.shape[0]
    local_count, slot_count, _ = scale.shape
    hidden = gate_weight.shape[2]
    gate_rows = jnp.transpose(gate_weight, (0, 2, 1))
    up_rows = jnp.transpose(up_weight, (0, 2, 1))
    tile = min(SLOT_TILE, slot_count)
    tiles = slot_count // tile
    return pl.pallas_call(
        expert_kernel,
        grid=(local_count, tiles),
        in_specs=[
            pl.BlockSpec((feature_count, tile), lambda j, m: (0, j * tiles + m)),
            pl.BlockSpec((1, hidden, feature_count), lambda j, m: (j, 0, 0)),
            pl.BlockSpec((1, hidden, feature_count), lambda j, m: (j, 0, 0)),
            pl.BlockSpec((1, hidden, feature_count), lambda j, m: (j, 0, 0)),
            pl.BlockSpec((1, tile, 1), lambda j, m: (j, m, 0)),
        ],
        out_specs=pl.BlockSpec((1, tile, feature_count), lambda j, m: (j, m, 0)),
        out_shape=jax.ShapeDtypeStruct((local_count, slot_count, feature_count), jnp.bfloat16),
        compiler_params=pltpu.CompilerParams(
            dimension_semantics=("arbitrary", "arbitrary"),
            vmem_limit_bytes=56 * 1024 * 1024,
        ),
    )(grouped_t, gate_rows, up_rows, down_weight, scale)


def pair_swap(x):
    return lax.ppermute(x, "ffn", [(0, 1), (1, 0)])


def ffn_sum_scatter(x, ffn_index, ffn_size, axis):
    if ffn_size != 2:
        return lax.psum_scatter(x, "ffn", scatter_dimension=axis, tiled=True).astype(jnp.float32)
    width = x.shape[axis] // 2
    mine = lax.dynamic_slice_in_dim(x, ffn_index * width, width, axis)
    other = lax.dynamic_slice_in_dim(x, (1 - ffn_index) * width, width, axis)
    return mine.astype(jnp.float32) + pair_swap(other).astype(jnp.float32)


def ffn_gather_columns(x, ffn_index, ffn_size):
    if ffn_size != 2:
        return lax.all_gather(x, "ffn", axis=1, tiled=True)
    other = pair_swap(x)
    first = jnp.where(ffn_index == 0, x, other)
    second = jnp.where(ffn_index == 0, other, x)
    return jnp.concatenate([first, second], axis=1)


def local(
    residual,
    queries,
    new_latent,
    cache_pool,
    page_table,
    cached_len,
    tenant_start,
    routes,
    value_up,
    out_proj,
    norm_gain,
    router,
    gate_weight,
    up_weight,
    down_weight,
):
    exp_size = lax.axis_size("exp")
    ffn_size = lax.axis_size("ffn")
    req_index = lax.axis_index("req")
    exp_index = lax.axis_index("exp")
    ffn_index = lax.axis_index("ffn")
    token_rows = residual.shape[0]
    feature_count = residual.shape[1]
    fresh_len = token_rows * exp_size // REQ_GRP
    first_token = (req_index * exp_size + exp_index) * token_rows
    request = first_token // fresh_len
    offset = first_token - request * fresh_len
    pool_pages = cache_pool.shape[0]
    page_width = cache_pool.shape[1]
    latent_pages = token_rows * QKD // page_width
    route_count = token_rows * TOP
    route_pages = -(-route_count // page_width)
    route_rows = jnp.pad(
        routes.reshape(route_count).astype(jnp.bfloat16),
        (0, route_pages * page_width - route_count),
    ).reshape(route_pages, page_width)
    packed_rows = pool_pages + latent_pages + route_pages
    share_rows = -(-packed_rows // (ffn_size * 8)) * 8
    packed = jnp.concatenate(
        [
            cache_pool,
            new_latent.reshape(latent_pages, page_width),
            route_rows,
            jnp.zeros((share_rows * ffn_size - packed_rows, page_width), jnp.bfloat16),
        ],
        axis=0,
    )
    share = lax.dynamic_slice_in_dim(packed, ffn_index * share_rows, share_rows, 0)
    if ffn_size == 2:
        mine = lax.all_gather(share, "exp", axis=0, tiled=False)
        other = pair_swap(mine)
        gathered = jnp.concatenate(
            [jnp.where(ffn_index == 0, mine, other), jnp.where(ffn_index == 0, other, mine)],
            axis=1,
        )
    else:
        gathered = lax.all_gather(share, ("exp", "ffn"), axis=0, tiled=False)
        gathered = gathered.reshape(exp_size, ffn_size * share_rows, page_width)
    stride = ffn_size * share_rows
    group_rows = exp_size * token_rows
    routes_all = (
        gathered[:, pool_pages + latent_pages : packed_rows]
        .reshape(exp_size, route_pages * page_width)[:, :route_count]
        .reshape(group_rows, TOP)
        .astype(jnp.int32)
    )
    flat_pages = gathered.reshape(exp_size * stride, page_width)
    pool_base = req_index * exp_size * pool_pages
    page_rows = page_table[request] - pool_base
    cached_rows = (page_rows // pool_pages) * stride + page_rows % pool_pages
    local_request = request - req_index * REQ_GRP
    fresh_devices = fresh_len // token_rows
    fresh_index = lax.broadcasted_iota(jnp.int32, (fresh_devices, latent_pages), 0)
    fresh_rows = (
        (local_request * fresh_devices + fresh_index) * stride
        + pool_pages
        + lax.broadcasted_iota(jnp.int32, (fresh_devices, latent_pages), 1)
    ).reshape(fresh_devices * latent_pages)
    key_rows = jnp.concatenate([cached_rows, fresh_rows], axis=0)
    all_keys = jnp.take(flat_pages, key_rows, axis=0, mode="clip").reshape(CMAX + fresh_len, QKD)
    heads_here = queries.shape[1] // QKD
    query_heads = queries.reshape(token_rows, heads_here, QKD)
    scale_factor = (HEAD_DIM + ROPE_DIM) ** (-0.5)
    scores = (
        jnp.einsum("thd,kd->thk", query_heads, all_keys, preferred_element_type=jnp.float32)
        * scale_factor
    )
    key_pos = lax.broadcasted_iota(jnp.int32, (1, CMAX + fresh_len), 1)
    tok_pos = offset + lax.broadcasted_iota(jnp.int32, (token_rows, 1), 0)
    cached_ok = (key_pos >= tenant_start[request]) & (key_pos < cached_len[request])
    fresh_ok = (key_pos >= CMAX) & (key_pos - CMAX <= tok_pos)
    visible = cached_ok | fresh_ok
    scores = jnp.where(visible[:, None, :], scores, NEG_FILL)
    top_score = jnp.max(scores, axis=2, keepdims=True)
    weights = jnp.exp(scores - top_score)
    attn_probs = (weights / jnp.sum(weights, axis=2, keepdims=True)).astype(jnp.bfloat16)
    latent_out = jnp.einsum(
        "thk,kl->thl", attn_probs, all_keys[:, :LATENT], preferred_element_type=jnp.float32
    ).astype(jnp.bfloat16)
    value_heads = value_up.reshape(LATENT, heads_here, HEAD_DIM)
    head_out = jnp.einsum(
        "thl,lhd->thd", latent_out, value_heads, preferred_element_type=jnp.float32
    )
    head_out = head_out.astype(jnp.bfloat16).reshape(token_rows, heads_here * HEAD_DIM)
    partial_value = jnp.dot(head_out, out_proj, preferred_element_type=jnp.float32)
    column_count = feature_count // ffn_size
    attn_cols = ffn_sum_scatter(partial_value.astype(jnp.bfloat16), ffn_index, ffn_size, 1)
    residual_cols = lax.dynamic_slice_in_dim(residual, ffn_index * column_count, column_count, 1)
    hidden_out = (residual_cols.astype(jnp.float32) + attn_cols).astype(jnp.bfloat16)
    hidden_wide = hidden_out.astype(jnp.float32)
    square_sum = lax.psum(jnp.sum(hidden_wide * hidden_wide, axis=1, keepdims=True), "ffn")
    mean_square = square_sum / feature_count
    gain_cols = lax.dynamic_slice_in_dim(norm_gain, ffn_index * column_count, column_count, 0)
    normed_cols = (
        hidden_wide * lax.rsqrt(mean_square + EPSILON) * gain_cols.astype(jnp.float32)
    ).astype(jnp.bfloat16)
    normed_half = lax.all_gather(normed_cols, "exp", axis=0, tiled=True)
    normed_all = ffn_gather_columns(normed_half, ffn_index, ffn_size)

    expert_ids = lax.broadcasted_iota(jnp.int32, (1, 1, EXPERTS), 2)
    route_hot = routes_all[:, :, None] == expert_ids
    blocks = group_rows // BLOCK_ROWS
    pair_count = BLOCK_ROWS * TOP
    pair_hot = route_hot.reshape(blocks, pair_count, EXPERTS).astype(jnp.bfloat16)
    earlier = (
        lax.broadcasted_iota(jnp.int32, (pair_count, pair_count), 1)
        < lax.broadcasted_iota(jnp.int32, (pair_count, pair_count), 0)
    ).astype(jnp.bfloat16)
    before = jnp.einsum("pq,bqx->bpx", earlier, pair_hot, preferred_element_type=jnp.float32)
    rank = jnp.sum(before * pair_hot.astype(jnp.float32), axis=2).astype(jnp.int32)
    block_base = lax.broadcasted_iota(jnp.int32, (blocks, 1), 0) * CAPACITY
    slot_index = (rank + block_base).reshape(group_rows, TOP)
    slot_count = blocks * CAPACITY
    local_count = gate_weight.shape[0]
    total_slots = local_count * slot_count
    local_expert = routes_all - exp_index * local_count
    is_local = (local_expert >= 0) & (local_expert < local_count)
    target = jnp.where(is_local, local_expert * slot_count + slot_index, -1)

    logits = jnp.dot(normed_all, router, preferred_element_type=jnp.float32)
    chosen = jnp.sum(jnp.where(route_hot, logits[:, None, :], 0.0), axis=2)
    raised = jnp.exp(chosen)
    gate_weights = raised / jnp.sum(raised, axis=1, keepdims=True)

    slot_ids = lax.broadcasted_iota(jnp.int32, (1, 1, total_slots), 2)
    slot_hit = target[:, :, None] == slot_ids
    combine = jnp.any(slot_hit, axis=1).astype(jnp.bfloat16)
    slot_weight = jnp.sum(jnp.where(slot_hit, gate_weights[:, :, None], 0.0), axis=(0, 1))
    grouped_t = jnp.einsum(
        "td,ts->ds", normed_all, combine, preferred_element_type=jnp.float32
    ).astype(jnp.bfloat16)
    weighted = expert_ffn(
        grouped_t,
        gate_weight,
        up_weight,
        down_weight,
        slot_weight.reshape(local_count, slot_count, 1),
    ).reshape(total_slots, feature_count)
    mixture = jnp.dot(combine, weighted, preferred_element_type=jnp.float32).astype(jnp.bfloat16)
    moe_cols = ffn_sum_scatter(mixture, ffn_index, ffn_size, 1).astype(jnp.bfloat16)
    moe_out = lax.psum_scatter(moe_cols, "exp", scatter_dimension=0, tiled=True)
    return (hidden_out, moe_out)


def solution(mesh):
    in_specs = (
        P(("req", "exp"), None),
        P(("req", "exp"), "ffn"),
        P(("req", "exp"), None),
        P(("req", "exp"), None),
        P(),
        P(),
        P(),
        P(("req", "exp"), None),
        P(None, "ffn"),
        P("ffn", None),
        P(),
        P(),
        P("exp", None, "ffn"),
        P("exp", None, "ffn"),
        P("exp", "ffn", None),
    )
    out_specs = (P(("req", "exp"), "ffn"), P(("req", "exp"), "ffn"))
    return jax.shard_map(local, mesh=mesh, in_specs=in_specs, out_specs=out_specs, check_vma=False)
```

```python
import jax
import jax.numpy as jnp
from jax import lax
from jax.experimental import pallas as pl
from jax.experimental.pallas import tpu as pltpu
from jax.sharding import PartitionSpec as P

LATENT = 512
ROPE_DIM = 64
HEAD_DIM = 128
QKD = 576
EXPERTS = 32
TOP = 6
CAPACITY = 16
REQ_GRP = 2
CMAX = 1024
BLOCK_ROWS = 64


EPSILON = 1e-06
NEG_FILL = -1e30


SLOT_TILE = 512


def expert_kernel(rows_ref, gate_ref, up_ref, down_ref, scale_ref, out_ref):
    columns = rows_ref[...]
    gate_part = jnp.dot(gate_ref[0], columns, preferred_element_type=jnp.float32)
    up_part = jnp.dot(up_ref[0], columns, preferred_element_type=jnp.float32)
    active = (gate_part / (1.0 + jnp.exp(-gate_part)) * up_part).astype(jnp.bfloat16)
    contract = (((0,), (0,)), ((), ()))
    result = lax.dot_general(active, down_ref[0], contract, preferred_element_type=jnp.float32)
    out_ref[0] = (result * scale_ref[0]).astype(out_ref.dtype)


def expert_ffn(grouped_t, gate_weight, up_weight, down_weight, scale):
    feature_count = grouped_t.shape[0]
    local_count, slot_count, _ = scale.shape
    hidden = gate_weight.shape[2]
    gate_rows = jnp.transpose(gate_weight, (0, 2, 1))
    up_rows = jnp.transpose(up_weight, (0, 2, 1))
    tile = min(SLOT_TILE, slot_count)
    tiles = slot_count // tile
    return pl.pallas_call(
        expert_kernel,
        grid=(local_count, tiles),
        in_specs=[
            pl.BlockSpec((feature_count, tile), lambda j, m: (0, j * tiles + m)),
            pl.BlockSpec((1, hidden, feature_count), lambda j, m: (j, 0, 0)),
            pl.BlockSpec((1, hidden, feature_count), lambda j, m: (j, 0, 0)),
            pl.BlockSpec((1, hidden, feature_count), lambda j, m: (j, 0, 0)),
            pl.BlockSpec((1, tile, 1), lambda j, m: (j, m, 0)),
        ],
        out_specs=pl.BlockSpec((1, tile, feature_count), lambda j, m: (j, m, 0)),
        out_shape=jax.ShapeDtypeStruct((local_count, slot_count, feature_count), jnp.bfloat16),
        compiler_params=pltpu.CompilerParams(
            dimension_semantics=("arbitrary", "arbitrary"),
            vmem_limit_bytes=56 * 1024 * 1024,
        ),
    )(grouped_t, gate_rows, up_rows, down_weight, scale)


def pair_swap(x):
    return lax.ppermute(x, "ffn", [(0, 1), (1, 0)])


def ffn_sum_scatter(x, ffn_index, ffn_size, axis):
    if ffn_size != 2:
        return lax.psum_scatter(x, "ffn", scatter_dimension=axis, tiled=True).astype(jnp.float32)
    width = x.shape[axis] // 2
    mine = lax.dynamic_slice_in_dim(x, ffn_index * width, width, axis)
    other = lax.dynamic_slice_in_dim(x, (1 - ffn_index) * width, width, axis)
    return mine.astype(jnp.float32) + pair_swap(other).astype(jnp.float32)


def ffn_gather_columns(x, ffn_index, ffn_size):
    if ffn_size != 2:
        return lax.all_gather(x, "ffn", axis=1, tiled=True)
    other = pair_swap(x)
    first = jnp.where(ffn_index == 0, x, other)
    second = jnp.where(ffn_index == 0, other, x)
    return jnp.concatenate([first, second], axis=1)


def local(
    residual,
    queries,
    new_latent,
    cache_pool,
    page_table,
    cached_len,
    tenant_start,
    routes,
    value_up,
    out_proj,
    norm_gain,
    router,
    gate_weight,
    up_weight,
    down_weight,
):
    exp_size = lax.axis_size("exp")
    ffn_size = lax.axis_size("ffn")
    req_index = lax.axis_index("req")
    exp_index = lax.axis_index("exp")
    ffn_index = lax.axis_index("ffn")
    token_rows = residual.shape[0]
    feature_count = residual.shape[1]
    fresh_len = token_rows * exp_size // REQ_GRP
    first_token = (req_index * exp_size + exp_index) * token_rows
    request = first_token // fresh_len
    offset = first_token - request * fresh_len
    pool_pages = cache_pool.shape[0]
    page_width = cache_pool.shape[1]
    latent_pages = token_rows * QKD // page_width
    route_count = token_rows * TOP
    route_pages = -(-route_count // page_width)
    route_rows = jnp.pad(
        routes.reshape(route_count).astype(jnp.bfloat16),
        (0, route_pages * page_width - route_count),
    ).reshape(route_pages, page_width)
    packed_rows = pool_pages + latent_pages + route_pages
    share_rows = -(-packed_rows // (ffn_size * 8)) * 8
    packed = jnp.concatenate(
        [
            cache_pool,
            new_latent.reshape(latent_pages, page_width),
            route_rows,
            jnp.zeros((share_rows * ffn_size - packed_rows, page_width), jnp.bfloat16),
        ],
        axis=0,
    )
    share = lax.dynamic_slice_in_dim(packed, ffn_index * share_rows, share_rows, 0)
    gathered = lax.all_gather(share, ("exp", "ffn"), axis=0, tiled=False)
    gathered = gathered.reshape(exp_size, ffn_size * share_rows, page_width)
    stride = ffn_size * share_rows
    group_rows = exp_size * token_rows
    routes_all = (
        gathered[:, pool_pages + latent_pages : packed_rows]
        .reshape(exp_size, route_pages * page_width)[:, :route_count]
        .reshape(group_rows, TOP)
        .astype(jnp.int32)
    )
    flat_pages = gathered.reshape(exp_size * stride, page_width)
    pool_base = req_index * exp_size * pool_pages
    page_rows = page_table[request] - pool_base
    cached_rows = (page_rows // pool_pages) * stride + page_rows % pool_pages
    local_request = request - req_index * REQ_GRP
    fresh_devices = fresh_len // token_rows
    fresh_index = lax.broadcasted_iota(jnp.int32, (fresh_devices, latent_pages), 0)
    fresh_rows = (
        (local_request * fresh_devices + fresh_index) * stride
        + pool_pages
        + lax.broadcasted_iota(jnp.int32, (fresh_devices, latent_pages), 1)
    ).reshape(fresh_devices * latent_pages)
    key_rows = jnp.concatenate([cached_rows, fresh_rows], axis=0)
    all_keys = jnp.take(flat_pages, key_rows, axis=0, mode="clip").reshape(CMAX + fresh_len, QKD)
    heads_here = queries.shape[1] // QKD
    query_heads = queries.reshape(token_rows, heads_here, QKD)
    scale_factor = (HEAD_DIM + ROPE_DIM) ** (-0.5)
    scores = (
        jnp.einsum("thd,kd->thk", query_heads, all_keys, preferred_element_type=jnp.float32)
        * scale_factor
    )
    key_pos = lax.broadcasted_iota(jnp.int32, (1, CMAX + fresh_len), 1)
    tok_pos = offset + lax.broadcasted_iota(jnp.int32, (token_rows, 1), 0)
    cached_ok = (key_pos >= tenant_start[request]) & (key_pos < cached_len[request])
    fresh_ok = (key_pos >= CMAX) & (key_pos - CMAX <= tok_pos)
    visible = cached_ok | fresh_ok
    scores = jnp.where(visible[:, None, :], scores, NEG_FILL)
    top_score = jnp.max(scores, axis=2, keepdims=True)
    weights = jnp.exp(scores - top_score)
    attn_probs = (weights / jnp.sum(weights, axis=2, keepdims=True)).astype(jnp.bfloat16)
    latent_out = jnp.einsum(
        "thk,kl->thl", attn_probs, all_keys[:, :LATENT], preferred_element_type=jnp.float32
    ).astype(jnp.bfloat16)
    value_heads = value_up.reshape(LATENT, heads_here, HEAD_DIM)
    head_out = jnp.einsum(
        "thl,lhd->thd", latent_out, value_heads, preferred_element_type=jnp.float32
    )
    head_out = head_out.astype(jnp.bfloat16).reshape(token_rows, heads_here * HEAD_DIM)
    partial_value = jnp.dot(head_out, out_proj, preferred_element_type=jnp.float32)
    column_count = feature_count // ffn_size
    attn_cols = ffn_sum_scatter(partial_value.astype(jnp.bfloat16), ffn_index, ffn_size, 1)
    residual_cols = lax.dynamic_slice_in_dim(residual, ffn_index * column_count, column_count, 1)
    hidden_out = (residual_cols.astype(jnp.float32) + attn_cols).astype(jnp.bfloat16)
    hidden_wide = hidden_out.astype(jnp.float32)
    square_sum = lax.psum(jnp.sum(hidden_wide * hidden_wide, axis=1, keepdims=True), "ffn")
    mean_square = square_sum / feature_count
    gain_cols = lax.dynamic_slice_in_dim(norm_gain, ffn_index * column_count, column_count, 0)
    normed_cols = (
        hidden_wide * lax.rsqrt(mean_square + EPSILON) * gain_cols.astype(jnp.float32)
    ).astype(jnp.bfloat16)
    normed_grid = lax.all_gather(normed_cols, ("exp", "ffn"), axis=0, tiled=False)
    normed_all = (
        normed_grid.reshape(exp_size, ffn_size, token_rows, column_count)
        .transpose(0, 2, 1, 3)
        .reshape(group_rows, feature_count)
    )

    expert_ids = lax.broadcasted_iota(jnp.int32, (1, 1, EXPERTS), 2)
    route_hot = routes_all[:, :, None] == expert_ids
    blocks = group_rows // BLOCK_ROWS
    pair_count = BLOCK_ROWS * TOP
    pair_hot = route_hot.reshape(blocks, pair_count, EXPERTS).astype(jnp.bfloat16)
    earlier = (
        lax.broadcasted_iota(jnp.int32, (pair_count, pair_count), 1)
        < lax.broadcasted_iota(jnp.int32, (pair_count, pair_count), 0)
    ).astype(jnp.bfloat16)
    before = jnp.einsum("pq,bqx->bpx", earlier, pair_hot, preferred_element_type=jnp.float32)
    rank = jnp.sum(before * pair_hot.astype(jnp.float32), axis=2).astype(jnp.int32)
    block_base = lax.broadcasted_iota(jnp.int32, (blocks, 1), 0) * CAPACITY
    slot_index = (rank + block_base).reshape(group_rows, TOP)
    slot_count = blocks * CAPACITY
    local_count = gate_weight.shape[0]
    total_slots = local_count * slot_count
    local_expert = routes_all - exp_index * local_count
    is_local = (local_expert >= 0) & (local_expert < local_count)
    target = jnp.where(is_local, local_expert * slot_count + slot_index, -1)

    logits = jnp.dot(normed_all, router, preferred_element_type=jnp.float32)
    chosen = jnp.sum(jnp.where(route_hot, logits[:, None, :], 0.0), axis=2)
    raised = jnp.exp(chosen)
    gate_weights = raised / jnp.sum(raised, axis=1, keepdims=True)

    slot_ids = lax.broadcasted_iota(jnp.int32, (1, 1, total_slots), 2)
    slot_hit = target[:, :, None] == slot_ids
    combine = jnp.any(slot_hit, axis=1).astype(jnp.bfloat16)
    slot_weight = jnp.sum(jnp.where(slot_hit, gate_weights[:, :, None], 0.0), axis=(0, 1))
    grouped_t = jnp.einsum(
        "td,ts->ds", normed_all, combine, preferred_element_type=jnp.float32
    ).astype(jnp.bfloat16)
    weighted = expert_ffn(
        grouped_t,
        gate_weight,
        up_weight,
        down_weight,
        slot_weight.reshape(local_count, slot_count, 1),
    ).reshape(total_slots, feature_count)
    mixture = jnp.dot(combine, weighted, preferred_element_type=jnp.float32).astype(jnp.bfloat16)
    moe_cols = ffn_sum_scatter(mixture, ffn_index, ffn_size, 1).astype(jnp.bfloat16)
    moe_out = lax.psum_scatter(moe_cols, "exp", scatter_dimension=0, tiled=True)
    return (hidden_out, moe_out)


def solution(mesh):
    in_specs = (
        P(("req", "exp"), None),
        P(("req", "exp"), "ffn"),
        P(("req", "exp"), None),
        P(("req", "exp"), None),
        P(),
        P(),
        P(),
        P(("req", "exp"), None),
        P(None, "ffn"),
        P("ffn", None),
        P(),
        P(),
        P("exp", None, "ffn"),
        P("exp", None, "ffn"),
        P("exp", "ffn", None),
    )
    out_specs = (P(("req", "exp"), "ffn"), P(("req", "exp"), "ffn"))
    return jax.shard_map(local, mesh=mesh, in_specs=in_specs, out_specs=out_specs, check_vma=False)
```

```python
import jax
import jax.numpy as jnp
from jax import lax
from jax.experimental import pallas as pl
from jax.experimental.pallas import tpu as pltpu
from jax.sharding import PartitionSpec as P

LATENT = 512
ROPE_DIM = 64
HEAD_DIM = 128
QKD = 576
EXPERTS = 32
TOP = 6
CAPACITY = 16
REQ_GRP = 2
CMAX = 1024
BLOCK_ROWS = 64


EPSILON = 1e-06
NEG_FILL = -1e30


SLOT_TILE = 512


def expert_kernel(rows_ref, gate_ref, up_ref, down_ref, scale_ref, out_ref):
    columns = rows_ref[...]
    gate_part = jnp.dot(gate_ref[0], columns, preferred_element_type=jnp.float32)
    up_part = jnp.dot(up_ref[0], columns, preferred_element_type=jnp.float32)
    active = (gate_part / (1.0 + jnp.exp(-gate_part)) * up_part).astype(jnp.bfloat16)
    contract = (((0,), (0,)), ((), ()))
    result = lax.dot_general(active, down_ref[0], contract, preferred_element_type=jnp.float32)
    out_ref[0] = (result * scale_ref[0]).astype(out_ref.dtype)


def expert_ffn(grouped_t, gate_weight, up_weight, down_weight, scale):
    feature_count = grouped_t.shape[0]
    local_count, slot_count, _ = scale.shape
    hidden = gate_weight.shape[2]
    gate_rows = jnp.transpose(gate_weight, (0, 2, 1))
    up_rows = jnp.transpose(up_weight, (0, 2, 1))
    tile = min(SLOT_TILE, slot_count)
    tiles = slot_count // tile
    return pl.pallas_call(
        expert_kernel,
        grid=(local_count, tiles),
        in_specs=[
            pl.BlockSpec((feature_count, tile), lambda j, m: (0, j * tiles + m)),
            pl.BlockSpec((1, hidden, feature_count), lambda j, m: (j, 0, 0)),
            pl.BlockSpec((1, hidden, feature_count), lambda j, m: (j, 0, 0)),
            pl.BlockSpec((1, hidden, feature_count), lambda j, m: (j, 0, 0)),
            pl.BlockSpec((1, tile, 1), lambda j, m: (j, m, 0)),
        ],
        out_specs=pl.BlockSpec((1, tile, feature_count), lambda j, m: (j, m, 0)),
        out_shape=jax.ShapeDtypeStruct((local_count, slot_count, feature_count), jnp.bfloat16),
        compiler_params=pltpu.CompilerParams(
            dimension_semantics=("arbitrary", "arbitrary"),
            vmem_limit_bytes=56 * 1024 * 1024,
        ),
    )(grouped_t, gate_rows, up_rows, down_weight, scale)


def pair_swap(x):
    return lax.ppermute(x, "ffn", [(0, 1), (1, 0)])


def ffn_sum_scatter(x, ffn_index, ffn_size, axis):
    if ffn_size != 2:
        return lax.psum_scatter(x, "ffn", scatter_dimension=axis, tiled=True).astype(jnp.float32)
    width = x.shape[axis] // 2
    mine = lax.dynamic_slice_in_dim(x, ffn_index * width, width, axis)
    other = lax.dynamic_slice_in_dim(x, (1 - ffn_index) * width, width, axis)
    return mine.astype(jnp.float32) + pair_swap(other).astype(jnp.float32)


def ffn_gather_columns(x, ffn_index, ffn_size):
    if ffn_size != 2:
        return lax.all_gather(x, "ffn", axis=1, tiled=True)
    other = pair_swap(x)
    first = jnp.where(ffn_index == 0, x, other)
    second = jnp.where(ffn_index == 0, other, x)
    return jnp.concatenate([first, second], axis=1)


def local(
    residual,
    queries,
    new_latent,
    cache_pool,
    page_table,
    cached_len,
    tenant_start,
    routes,
    value_up,
    out_proj,
    norm_gain,
    router,
    gate_weight,
    up_weight,
    down_weight,
):
    exp_size = lax.axis_size("exp")
    ffn_size = lax.axis_size("ffn")
    req_index = lax.axis_index("req")
    exp_index = lax.axis_index("exp")
    ffn_index = lax.axis_index("ffn")
    token_rows = residual.shape[0]
    feature_count = residual.shape[1]
    fresh_len = token_rows * exp_size // REQ_GRP
    first_token = (req_index * exp_size + exp_index) * token_rows
    request = first_token // fresh_len
    offset = first_token - request * fresh_len
    pool_pages = cache_pool.shape[0]
    page_width = cache_pool.shape[1]
    latent_pages = token_rows * QKD // page_width
    route_count = token_rows * TOP
    route_width = 128
    route_lines = -(-route_count // (route_width * 8)) * 8
    route_rows = jnp.pad(
        routes.reshape(route_count).astype(jnp.bfloat16),
        (0, route_lines * route_width - route_count),
    ).reshape(route_lines, route_width)
    group_rows = exp_size * token_rows
    routes_all = (
        lax.all_gather(route_rows, "exp", axis=0, tiled=False)
        .reshape(exp_size, route_lines * route_width)[:, :route_count]
        .reshape(group_rows, TOP)
        .astype(jnp.int32)
    )
    pool_share = pool_pages // ffn_size
    latent_share = latent_pages // ffn_size
    share = jnp.concatenate(
        [
            lax.dynamic_slice_in_dim(cache_pool, ffn_index * pool_share, pool_share, 0),
            lax.dynamic_slice_in_dim(
                new_latent.reshape(latent_pages, page_width),
                ffn_index * latent_share,
                latent_share,
                0,
            ),
        ],
        axis=0,
    )
    gathered = lax.all_gather(share, ("exp", "ffn"), axis=0, tiled=False)
    pool_base = req_index * exp_size * pool_pages
    page_rows = page_table[request] - pool_base
    page_within = page_rows % pool_pages
    cached_share = (page_rows // pool_pages) * ffn_size + page_within // pool_share
    cached_row = page_within % pool_share
    local_request = request - req_index * REQ_GRP
    fresh_devices = fresh_len // token_rows
    fresh_device = local_request * fresh_devices + lax.broadcasted_iota(
        jnp.int32, (fresh_devices, latent_pages), 0
    )
    fresh_page = lax.broadcasted_iota(jnp.int32, (fresh_devices, latent_pages), 1)
    fresh_share = (fresh_device * ffn_size + fresh_page // latent_share).reshape(-1)
    fresh_row = (pool_share + fresh_page % latent_share).reshape(-1)
    key_share = jnp.concatenate([cached_share, fresh_share], axis=0)
    key_row = jnp.concatenate([cached_row, fresh_row], axis=0)
    all_keys = (
        gathered.at[key_share, key_row].get(mode="clip").reshape(CMAX + fresh_len, QKD)
    )
    heads_here = queries.shape[1] // QKD
    query_heads = queries.reshape(token_rows, heads_here, QKD)
    scale_factor = (HEAD_DIM + ROPE_DIM) ** (-0.5)
    scores = (
        jnp.einsum("thd,kd->thk", query_heads, all_keys, preferred_element_type=jnp.float32)
        * scale_factor
    )
    key_pos = lax.broadcasted_iota(jnp.int32, (1, CMAX + fresh_len), 1)
    tok_pos = offset + lax.broadcasted_iota(jnp.int32, (token_rows, 1), 0)
    cached_ok = (key_pos >= tenant_start[request]) & (key_pos < cached_len[request])
    fresh_ok = (key_pos >= CMAX) & (key_pos - CMAX <= tok_pos)
    visible = cached_ok | fresh_ok
    scores = jnp.where(visible[:, None, :], scores, NEG_FILL)
    top_score = jnp.max(scores, axis=2, keepdims=True)
    weights = jnp.exp(scores - top_score)
    attn_probs = (weights / jnp.sum(weights, axis=2, keepdims=True)).astype(jnp.bfloat16)
    latent_out = jnp.einsum(
        "thk,kl->thl", attn_probs, all_keys[:, :LATENT], preferred_element_type=jnp.float32
    ).astype(jnp.bfloat16)
    value_heads = value_up.reshape(LATENT, heads_here, HEAD_DIM)
    head_out = jnp.einsum(
        "thl,lhd->thd", latent_out, value_heads, preferred_element_type=jnp.float32
    )
    head_out = head_out.astype(jnp.bfloat16).reshape(token_rows, heads_here * HEAD_DIM)
    partial_value = jnp.dot(head_out, out_proj, preferred_element_type=jnp.float32)
    column_count = feature_count // ffn_size
    attn_cols = ffn_sum_scatter(partial_value.astype(jnp.bfloat16), ffn_index, ffn_size, 1)
    residual_cols = lax.dynamic_slice_in_dim(residual, ffn_index * column_count, column_count, 1)
    hidden_out = (residual_cols.astype(jnp.float32) + attn_cols).astype(jnp.bfloat16)
    hidden_wide = hidden_out.astype(jnp.float32)
    square_sum = lax.psum(jnp.sum(hidden_wide * hidden_wide, axis=1, keepdims=True), "ffn")
    mean_square = square_sum / feature_count
    gain_cols = lax.dynamic_slice_in_dim(norm_gain, ffn_index * column_count, column_count, 0)
    normed_cols = (
        hidden_wide * lax.rsqrt(mean_square + EPSILON) * gain_cols.astype(jnp.float32)
    ).astype(jnp.bfloat16)
    normed_grid = lax.all_gather(normed_cols, ("exp", "ffn"), axis=0, tiled=False)
    normed_all = (
        normed_grid.reshape(exp_size, ffn_size, token_rows, column_count)
        .transpose(0, 2, 1, 3)
        .reshape(group_rows, feature_count)
    )

    expert_ids = lax.broadcasted_iota(jnp.int32, (1, 1, EXPERTS), 2)
    route_hot = routes_all[:, :, None] == expert_ids
    blocks = group_rows // BLOCK_ROWS
    pair_count = BLOCK_ROWS * TOP
    pair_hot = route_hot.reshape(blocks, pair_count, EXPERTS).astype(jnp.bfloat16)
    earlier = (
        lax.broadcasted_iota(jnp.int32, (pair_count, pair_count), 1)
        < lax.broadcasted_iota(jnp.int32, (pair_count, pair_count), 0)
    ).astype(jnp.bfloat16)
    before = jnp.einsum("pq,bqx->bpx", earlier, pair_hot, preferred_element_type=jnp.float32)
    rank = jnp.sum(before * pair_hot.astype(jnp.float32), axis=2).astype(jnp.int32)
    block_base = lax.broadcasted_iota(jnp.int32, (blocks, 1), 0) * CAPACITY
    slot_index = (rank + block_base).reshape(group_rows, TOP)
    slot_count = blocks * CAPACITY
    local_count = gate_weight.shape[0]
    total_slots = local_count * slot_count
    local_expert = routes_all - exp_index * local_count
    is_local = (local_expert >= 0) & (local_expert < local_count)
    target = jnp.where(is_local, local_expert * slot_count + slot_index, -1)

    logits = jnp.dot(normed_all, router, preferred_element_type=jnp.float32)
    chosen = jnp.sum(jnp.where(route_hot, logits[:, None, :], 0.0), axis=2)
    raised = jnp.exp(chosen)
    gate_weights = raised / jnp.sum(raised, axis=1, keepdims=True)

    slot_ids = lax.broadcasted_iota(jnp.int32, (1, 1, total_slots), 2)
    slot_hit = target[:, :, None] == slot_ids
    combine = jnp.any(slot_hit, axis=1).astype(jnp.bfloat16)
    slot_weight = jnp.sum(jnp.where(slot_hit, gate_weights[:, :, None], 0.0), axis=(0, 1))
    grouped_t = jnp.einsum(
        "td,ts->ds", normed_all, combine, preferred_element_type=jnp.float32
    ).astype(jnp.bfloat16)
    weighted = expert_ffn(
        grouped_t,
        gate_weight,
        up_weight,
        down_weight,
        slot_weight.reshape(local_count, slot_count, 1),
    ).reshape(total_slots, feature_count)
    mixture = jnp.dot(combine, weighted, preferred_element_type=jnp.float32).astype(jnp.bfloat16)
    moe_cols = ffn_sum_scatter(mixture, ffn_index, ffn_size, 1).astype(jnp.bfloat16)
    moe_out = lax.psum_scatter(moe_cols, "exp", scatter_dimension=0, tiled=True)
    return (hidden_out, moe_out)


def solution(mesh):
    in_specs = (
        P(("req", "exp"), None),
        P(("req", "exp"), "ffn"),
        P(("req", "exp"), None),
        P(("req", "exp"), None),
        P(),
        P(),
        P(),
        P(("req", "exp"), None),
        P(None, "ffn"),
        P("ffn", None),
        P(),
        P(),
        P("exp", None, "ffn"),
        P("exp", None, "ffn"),
        P("exp", "ffn", None),
    )
    out_specs = (P(("req", "exp"), "ffn"), P(("req", "exp"), "ffn"))
    return jax.shard_map(local, mesh=mesh, in_specs=in_specs, out_specs=out_specs, check_vma=False)
```

```python
import jax
import jax.numpy as jnp
from jax import lax
from jax.experimental import pallas as pl
from jax.experimental.pallas import tpu as pltpu
from jax.sharding import PartitionSpec as P

LATENT = 512
ROPE_DIM = 64
HEAD_DIM = 128
QKD = 576
EXPERTS = 32
TOP = 6
CAPACITY = 16
REQ_GRP = 2
CMAX = 1024
BLOCK_ROWS = 64


EPSILON = 1e-06
NEG_FILL = -1e30


SLOT_TILE = 512


def expert_kernel(rows_ref, gate_ref, up_ref, down_ref, scale_ref, out_ref):
    columns = rows_ref[...]
    gate_part = jnp.dot(gate_ref[0], columns, preferred_element_type=jnp.float32)
    up_part = jnp.dot(up_ref[0], columns, preferred_element_type=jnp.float32)
    active = (gate_part / (1.0 + jnp.exp(-gate_part)) * up_part).astype(jnp.bfloat16)
    contract = (((0,), (0,)), ((), ()))
    result = lax.dot_general(active, down_ref[0], contract, preferred_element_type=jnp.float32)
    out_ref[0] = (result * scale_ref[0]).astype(out_ref.dtype)


def expert_ffn(grouped_t, gate_weight, up_weight, down_weight, scale):
    feature_count = grouped_t.shape[0]
    local_count, slot_count, _ = scale.shape
    hidden = gate_weight.shape[2]
    gate_rows = jnp.transpose(gate_weight, (0, 2, 1))
    up_rows = jnp.transpose(up_weight, (0, 2, 1))
    tile = min(SLOT_TILE, slot_count)
    tiles = slot_count // tile
    return pl.pallas_call(
        expert_kernel,
        grid=(local_count, tiles),
        in_specs=[
            pl.BlockSpec((feature_count, tile), lambda j, m: (0, j * tiles + m)),
            pl.BlockSpec((1, hidden, feature_count), lambda j, m: (j, 0, 0)),
            pl.BlockSpec((1, hidden, feature_count), lambda j, m: (j, 0, 0)),
            pl.BlockSpec((1, hidden, feature_count), lambda j, m: (j, 0, 0)),
            pl.BlockSpec((1, tile, 1), lambda j, m: (j, m, 0)),
        ],
        out_specs=pl.BlockSpec((1, tile, feature_count), lambda j, m: (j, m, 0)),
        out_shape=jax.ShapeDtypeStruct((local_count, slot_count, feature_count), jnp.bfloat16),
        compiler_params=pltpu.CompilerParams(
            dimension_semantics=("arbitrary", "arbitrary"),
            vmem_limit_bytes=56 * 1024 * 1024,
        ),
    )(grouped_t, gate_rows, up_rows, down_weight, scale)


def pair_swap(x):
    return lax.ppermute(x, "ffn", [(0, 1), (1, 0)])


def ffn_sum_scatter(x, ffn_index, ffn_size, axis):
    if ffn_size != 2:
        return lax.psum_scatter(x, "ffn", scatter_dimension=axis, tiled=True).astype(jnp.float32)
    width = x.shape[axis] // 2
    mine = lax.dynamic_slice_in_dim(x, ffn_index * width, width, axis)
    other = lax.dynamic_slice_in_dim(x, (1 - ffn_index) * width, width, axis)
    return mine.astype(jnp.float32) + pair_swap(other).astype(jnp.float32)


def ffn_gather_columns(x, ffn_index, ffn_size):
    if ffn_size != 2:
        return lax.all_gather(x, "ffn", axis=1, tiled=True)
    other = pair_swap(x)
    first = jnp.where(ffn_index == 0, x, other)
    second = jnp.where(ffn_index == 0, other, x)
    return jnp.concatenate([first, second], axis=1)


def local(
    residual,
    queries,
    new_latent,
    cache_pool,
    page_table,
    cached_len,
    tenant_start,
    routes,
    value_up,
    out_proj,
    norm_gain,
    router,
    gate_weight,
    up_weight,
    down_weight,
):
    exp_size = lax.axis_size("exp")
    ffn_size = lax.axis_size("ffn")
    req_index = lax.axis_index("req")
    exp_index = lax.axis_index("exp")
    ffn_index = lax.axis_index("ffn")
    token_rows = residual.shape[0]
    feature_count = residual.shape[1]
    fresh_len = token_rows * exp_size // REQ_GRP
    first_token = (req_index * exp_size + exp_index) * token_rows
    request = first_token // fresh_len
    offset = first_token - request * fresh_len
    pool_pages = cache_pool.shape[0]
    page_width = cache_pool.shape[1]
    latent_pages = token_rows * QKD // page_width
    route_count = token_rows * TOP
    route_pages = -(-route_count // page_width)
    route_rows = jnp.pad(
        routes.reshape(route_count).astype(jnp.bfloat16),
        (0, route_pages * page_width - route_count),
    ).reshape(route_pages, page_width)
    packed_rows = pool_pages + latent_pages + route_pages
    share_rows = -(-packed_rows // (ffn_size * 8)) * 8
    packed = jnp.concatenate(
        [
            cache_pool,
            new_latent.reshape(latent_pages, page_width),
            route_rows,
            jnp.zeros((share_rows * ffn_size - packed_rows, page_width), jnp.bfloat16),
        ],
        axis=0,
    )
    share = lax.dynamic_slice_in_dim(packed, ffn_index * share_rows, share_rows, 0)
    gathered = lax.all_gather(share, ("exp", "ffn"), axis=0, tiled=False)
    gathered = gathered.reshape(exp_size, ffn_size * share_rows, page_width)
    stride = ffn_size * share_rows
    group_rows = exp_size * token_rows
    routes_all = (
        gathered[:, pool_pages + latent_pages : packed_rows]
        .reshape(exp_size, route_pages * page_width)[:, :route_count]
        .reshape(group_rows, TOP)
        .astype(jnp.int32)
    )
    flat_pages = gathered.reshape(exp_size * stride, page_width)
    pool_base = req_index * exp_size * pool_pages
    page_rows = page_table[request] - pool_base
    cached_rows = (page_rows // pool_pages) * stride + page_rows % pool_pages
    local_request = request - req_index * REQ_GRP
    fresh_devices = fresh_len // token_rows
    fresh_index = lax.broadcasted_iota(jnp.int32, (fresh_devices, latent_pages), 0)
    fresh_rows = (
        (local_request * fresh_devices + fresh_index) * stride
        + pool_pages
        + lax.broadcasted_iota(jnp.int32, (fresh_devices, latent_pages), 1)
    ).reshape(fresh_devices * latent_pages)
    key_rows = jnp.concatenate([cached_rows, fresh_rows], axis=0)
    all_keys = jnp.take(flat_pages, key_rows, axis=0, mode="clip").reshape(CMAX + fresh_len, QKD)
    heads_here = queries.shape[1] // QKD
    query_heads = queries.reshape(token_rows, heads_here, QKD)
    scale_factor = (HEAD_DIM + ROPE_DIM) ** (-0.5)
    scores = (
        jnp.einsum("thd,kd->thk", query_heads, all_keys, preferred_element_type=jnp.float32)
        * scale_factor
    )
    key_pos = lax.broadcasted_iota(jnp.int32, (1, CMAX + fresh_len), 1)
    tok_pos = offset + lax.broadcasted_iota(jnp.int32, (token_rows, 1), 0)
    cached_ok = (key_pos >= tenant_start[request]) & (key_pos < cached_len[request])
    fresh_ok = (key_pos >= CMAX) & (key_pos - CMAX <= tok_pos)
    visible = cached_ok | fresh_ok
    scores = jnp.where(visible[:, None, :], scores, NEG_FILL)
    top_score = jnp.max(scores, axis=2, keepdims=True)
    weights = jnp.exp(scores - top_score)
    attn_probs = (weights / jnp.sum(weights, axis=2, keepdims=True)).astype(jnp.bfloat16)
    latent_out = jnp.einsum(
        "thk,kl->thl", attn_probs, all_keys[:, :LATENT], preferred_element_type=jnp.float32
    ).astype(jnp.bfloat16)
    value_heads = value_up.reshape(LATENT, heads_here, HEAD_DIM)
    head_out = jnp.einsum(
        "thl,lhd->thd", latent_out, value_heads, preferred_element_type=jnp.float32
    )
    head_out = head_out.astype(jnp.bfloat16).reshape(token_rows, heads_here * HEAD_DIM)
    partial_value = jnp.dot(head_out, out_proj, preferred_element_type=jnp.float32)
    column_count = feature_count // ffn_size
    attn_cols = ffn_sum_scatter(partial_value.astype(jnp.bfloat16), ffn_index, ffn_size, 1)
    residual_cols = lax.dynamic_slice_in_dim(residual, ffn_index * column_count, column_count, 1)
    hidden_out = (residual_cols.astype(jnp.float32) + attn_cols).astype(jnp.bfloat16)
    hidden_wide = hidden_out.astype(jnp.float32)
    square_part = jnp.sum(hidden_wide * hidden_wide, axis=1, keepdims=True)
    if ffn_size == 2:
        square_sum = square_part + pair_swap(square_part)
    else:
        square_sum = lax.psum(square_part, "ffn")
    mean_square = square_sum / feature_count
    gain_cols = lax.dynamic_slice_in_dim(norm_gain, ffn_index * column_count, column_count, 0)
    normed_cols = (
        hidden_wide * lax.rsqrt(mean_square + EPSILON) * gain_cols.astype(jnp.float32)
    ).astype(jnp.bfloat16)
    normed_grid = lax.all_gather(normed_cols, ("exp", "ffn"), axis=0, tiled=False)
    normed_all = (
        normed_grid.reshape(exp_size, ffn_size, token_rows, column_count)
        .transpose(0, 2, 1, 3)
        .reshape(group_rows, feature_count)
    )

    expert_ids = lax.broadcasted_iota(jnp.int32, (1, 1, EXPERTS), 2)
    route_hot = routes_all[:, :, None] == expert_ids
    blocks = group_rows // BLOCK_ROWS
    pair_count = BLOCK_ROWS * TOP
    pair_hot = route_hot.reshape(blocks, pair_count, EXPERTS).astype(jnp.bfloat16)
    earlier = (
        lax.broadcasted_iota(jnp.int32, (pair_count, pair_count), 1)
        < lax.broadcasted_iota(jnp.int32, (pair_count, pair_count), 0)
    ).astype(jnp.bfloat16)
    before = jnp.einsum("pq,bqx->bpx", earlier, pair_hot, preferred_element_type=jnp.float32)
    rank = jnp.sum(before * pair_hot.astype(jnp.float32), axis=2).astype(jnp.int32)
    block_base = lax.broadcasted_iota(jnp.int32, (blocks, 1), 0) * CAPACITY
    slot_index = (rank + block_base).reshape(group_rows, TOP)
    slot_count = blocks * CAPACITY
    local_count = gate_weight.shape[0]
    total_slots = local_count * slot_count
    local_expert = routes_all - exp_index * local_count
    is_local = (local_expert >= 0) & (local_expert < local_count)
    target = jnp.where(is_local, local_expert * slot_count + slot_index, -1)

    logits = jnp.dot(normed_all, router, preferred_element_type=jnp.float32)
    chosen = jnp.sum(jnp.where(route_hot, logits[:, None, :], 0.0), axis=2)
    raised = jnp.exp(chosen)
    gate_weights = raised / jnp.sum(raised, axis=1, keepdims=True)

    slot_ids = lax.broadcasted_iota(jnp.int32, (1, 1, total_slots), 2)
    slot_hit = target[:, :, None] == slot_ids
    combine = jnp.any(slot_hit, axis=1).astype(jnp.bfloat16)
    slot_weight = jnp.sum(jnp.where(slot_hit, gate_weights[:, :, None], 0.0), axis=(0, 1))
    grouped_t = jnp.einsum(
        "td,ts->ds", normed_all, combine, preferred_element_type=jnp.float32
    ).astype(jnp.bfloat16)
    weighted = expert_ffn(
        grouped_t,
        gate_weight,
        up_weight,
        down_weight,
        slot_weight.reshape(local_count, slot_count, 1),
    ).reshape(total_slots, feature_count)
    mixture = jnp.dot(combine, weighted, preferred_element_type=jnp.float32).astype(jnp.bfloat16)
    moe_cols = ffn_sum_scatter(mixture, ffn_index, ffn_size, 1).astype(jnp.bfloat16)
    moe_out = lax.psum_scatter(moe_cols, "exp", scatter_dimension=0, tiled=True)
    return (hidden_out, moe_out)


def solution(mesh):
    in_specs = (
        P(("req", "exp"), None),
        P(("req", "exp"), "ffn"),
        P(("req", "exp"), None),
        P(("req", "exp"), None),
        P(),
        P(),
        P(),
        P(("req", "exp"), None),
        P(None, "ffn"),
        P("ffn", None),
        P(),
        P(),
        P("exp", None, "ffn"),
        P("exp", None, "ffn"),
        P("exp", "ffn", None),
    )
    out_specs = (P(("req", "exp"), "ffn"), P(("req", "exp"), "ffn"))
    return jax.shard_map(local, mesh=mesh, in_specs=in_specs, out_specs=out_specs, check_vma=False)
```

```python
import jax
import jax.numpy as jnp
from jax import lax
from jax.experimental import pallas as pl
from jax.experimental.pallas import tpu as pltpu
from jax.sharding import PartitionSpec as P

LATENT = 512
ROPE_DIM = 64
HEAD_DIM = 128
QKD = 576
EXPERTS = 32
TOP = 6
CAPACITY = 16
REQ_GRP = 2
CMAX = 1024
BLOCK_ROWS = 64


EPSILON = 1e-06
NEG_FILL = -1e30


SLOT_TILE = 512


def expert_kernel(rows_ref, gate_ref, up_ref, down_ref, scale_ref, out_ref):
    columns = rows_ref[...]
    gate_part = jnp.dot(gate_ref[0], columns, preferred_element_type=jnp.float32)
    up_part = jnp.dot(up_ref[0], columns, preferred_element_type=jnp.float32)
    active = (gate_part / (1.0 + jnp.exp(-gate_part)) * up_part).astype(jnp.bfloat16)
    contract = (((0,), (0,)), ((), ()))
    result = lax.dot_general(active, down_ref[0], contract, preferred_element_type=jnp.float32)
    out_ref[0] = (result * scale_ref[0]).astype(out_ref.dtype)


def expert_ffn(grouped_t, gate_weight, up_weight, down_weight, scale):
    feature_count = grouped_t.shape[0]
    local_count, slot_count, _ = scale.shape
    hidden = gate_weight.shape[2]
    gate_rows = jnp.transpose(gate_weight, (0, 2, 1))
    up_rows = jnp.transpose(up_weight, (0, 2, 1))
    tile = min(SLOT_TILE, slot_count)
    tiles = slot_count // tile
    return pl.pallas_call(
        expert_kernel,
        grid=(local_count, tiles),
        in_specs=[
            pl.BlockSpec((feature_count, tile), lambda j, m: (0, j * tiles + m)),
            pl.BlockSpec((1, hidden, feature_count), lambda j, m: (j, 0, 0)),
            pl.BlockSpec((1, hidden, feature_count), lambda j, m: (j, 0, 0)),
            pl.BlockSpec((1, hidden, feature_count), lambda j, m: (j, 0, 0)),
            pl.BlockSpec((1, tile, 1), lambda j, m: (j, m, 0)),
        ],
        out_specs=pl.BlockSpec((1, tile, feature_count), lambda j, m: (j, m, 0)),
        out_shape=jax.ShapeDtypeStruct((local_count, slot_count, feature_count), jnp.bfloat16),
        compiler_params=pltpu.CompilerParams(
            dimension_semantics=("arbitrary", "arbitrary"),
            vmem_limit_bytes=56 * 1024 * 1024,
        ),
    )(grouped_t, gate_rows, up_rows, down_weight, scale)


def pair_swap(x):
    return lax.ppermute(x, "ffn", [(0, 1), (1, 0)])


def ffn_sum_scatter(x, ffn_index, ffn_size, axis):
    if ffn_size != 2:
        return lax.psum_scatter(x, "ffn", scatter_dimension=axis, tiled=True).astype(jnp.float32)
    width = x.shape[axis] // 2
    mine = lax.dynamic_slice_in_dim(x, ffn_index * width, width, axis)
    other = lax.dynamic_slice_in_dim(x, (1 - ffn_index) * width, width, axis)
    return mine.astype(jnp.float32) + pair_swap(other).astype(jnp.float32)


def ffn_gather_columns(x, ffn_index, ffn_size):
    if ffn_size != 2:
        return lax.all_gather(x, "ffn", axis=1, tiled=True)
    other = pair_swap(x)
    first = jnp.where(ffn_index == 0, x, other)
    second = jnp.where(ffn_index == 0, other, x)
    return jnp.concatenate([first, second], axis=1)


def local(
    residual,
    queries,
    new_latent,
    cache_pool,
    page_table,
    cached_len,
    tenant_start,
    routes,
    value_up,
    out_proj,
    norm_gain,
    router,
    gate_weight,
    up_weight,
    down_weight,
):
    exp_size = lax.axis_size("exp")
    ffn_size = lax.axis_size("ffn")
    req_index = lax.axis_index("req")
    exp_index = lax.axis_index("exp")
    ffn_index = lax.axis_index("ffn")
    token_rows = residual.shape[0]
    feature_count = residual.shape[1]
    fresh_len = token_rows * exp_size // REQ_GRP
    first_token = (req_index * exp_size + exp_index) * token_rows
    request = first_token // fresh_len
    offset = first_token - request * fresh_len
    pool_pages = cache_pool.shape[0]
    page_width = cache_pool.shape[1]
    latent_pages = token_rows * QKD // page_width
    route_count = token_rows * TOP
    route_pages = -(-route_count // page_width)
    route_rows = jnp.pad(
        routes.reshape(route_count).astype(jnp.bfloat16),
        (0, route_pages * page_width - route_count),
    ).reshape(route_pages, page_width)
    packed_rows = pool_pages + latent_pages + route_pages
    share_rows = -(-packed_rows // (ffn_size * 8)) * 8
    packed = jnp.concatenate(
        [
            cache_pool,
            new_latent.reshape(latent_pages, page_width),
            route_rows,
            jnp.zeros((share_rows * ffn_size - packed_rows, page_width), jnp.bfloat16),
        ],
        axis=0,
    )
    share = lax.dynamic_slice_in_dim(packed, ffn_index * share_rows, share_rows, 0)
    gathered = lax.all_gather(share, ("exp", "ffn"), axis=0, tiled=False)
    gathered = gathered.reshape(exp_size, ffn_size * share_rows, page_width)
    stride = ffn_size * share_rows
    group_rows = exp_size * token_rows
    routes_all = (
        gathered[:, pool_pages + latent_pages : packed_rows]
        .reshape(exp_size, route_pages * page_width)[:, :route_count]
        .reshape(group_rows, TOP)
        .astype(jnp.int32)
    )
    flat_pages = gathered.reshape(exp_size * stride, page_width)
    pool_base = req_index * exp_size * pool_pages
    page_rows = page_table[request] - pool_base
    cached_rows = (page_rows // pool_pages) * stride + page_rows % pool_pages
    local_request = request - req_index * REQ_GRP
    fresh_devices = fresh_len // token_rows
    fresh_index = lax.broadcasted_iota(jnp.int32, (fresh_devices, latent_pages), 0)
    fresh_rows = (
        (local_request * fresh_devices + fresh_index) * stride
        + pool_pages
        + lax.broadcasted_iota(jnp.int32, (fresh_devices, latent_pages), 1)
    ).reshape(fresh_devices * latent_pages)
    key_rows = jnp.concatenate([cached_rows, fresh_rows], axis=0)
    all_keys = jnp.take(flat_pages, key_rows, axis=0, mode="clip").reshape(CMAX + fresh_len, QKD)
    heads_here = queries.shape[1] // QKD
    query_heads = queries.reshape(token_rows, heads_here, QKD)
    scale_factor = (HEAD_DIM + ROPE_DIM) ** (-0.5)
    scores = (
        jnp.einsum("thd,kd->thk", query_heads, all_keys, preferred_element_type=jnp.float32)
        * scale_factor
    )
    key_pos = lax.broadcasted_iota(jnp.int32, (1, CMAX + fresh_len), 1)
    tok_pos = offset + lax.broadcasted_iota(jnp.int32, (token_rows, 1), 0)
    cached_ok = (key_pos >= tenant_start[request]) & (key_pos < cached_len[request])
    fresh_ok = (key_pos >= CMAX) & (key_pos - CMAX <= tok_pos)
    visible = cached_ok | fresh_ok
    scores = jnp.where(visible[:, None, :], scores, NEG_FILL)
    top_score = jnp.max(scores, axis=2, keepdims=True)
    weights = jnp.exp(scores - top_score)
    attn_probs = (weights / jnp.sum(weights, axis=2, keepdims=True)).astype(jnp.bfloat16)
    latent_out = jnp.einsum(
        "thk,kl->thl", attn_probs, all_keys[:, :LATENT], preferred_element_type=jnp.float32
    ).astype(jnp.bfloat16)
    value_heads = value_up.reshape(LATENT, heads_here, HEAD_DIM)
    head_out = jnp.einsum(
        "thl,lhd->thd", latent_out, value_heads, preferred_element_type=jnp.float32
    )
    head_out = head_out.astype(jnp.bfloat16).reshape(token_rows, heads_here * HEAD_DIM)
    partial_value = jnp.dot(head_out, out_proj, preferred_element_type=jnp.float32)
    column_count = feature_count // ffn_size
    attn_cols = ffn_sum_scatter(partial_value.astype(jnp.bfloat16), ffn_index, ffn_size, 1)
    residual_cols = lax.dynamic_slice_in_dim(residual, ffn_index * column_count, column_count, 1)
    hidden_out = (residual_cols.astype(jnp.float32) + attn_cols).astype(jnp.bfloat16)
    hidden_wide = hidden_out.astype(jnp.float32)
    square_part = jnp.sum(hidden_wide * hidden_wide, axis=1, keepdims=True)
    if ffn_size == 2:
        square_sum = square_part + pair_swap(square_part)
    else:
        square_sum = lax.psum(square_part, "ffn")
    mean_square = square_sum / feature_count
    gain_cols = lax.dynamic_slice_in_dim(norm_gain, ffn_index * column_count, column_count, 0)
    normed_cols = (
        hidden_wide * lax.rsqrt(mean_square + EPSILON) * gain_cols.astype(jnp.float32)
    ).astype(jnp.bfloat16)
    normed_grid = lax.all_gather(normed_cols, ("ffn", "exp"), axis=0, tiled=False)
    normed_grid = normed_grid.reshape(ffn_size, group_rows, column_count)

    expert_ids = lax.broadcasted_iota(jnp.int32, (1, 1, EXPERTS), 2)
    route_hot = routes_all[:, :, None] == expert_ids
    blocks = group_rows // BLOCK_ROWS
    pair_count = BLOCK_ROWS * TOP
    pair_hot = route_hot.reshape(blocks, pair_count, EXPERTS).astype(jnp.bfloat16)
    earlier = (
        lax.broadcasted_iota(jnp.int32, (pair_count, pair_count), 1)
        < lax.broadcasted_iota(jnp.int32, (pair_count, pair_count), 0)
    ).astype(jnp.bfloat16)
    before = jnp.einsum("pq,bqx->bpx", earlier, pair_hot, preferred_element_type=jnp.float32)
    rank = jnp.sum(before * pair_hot.astype(jnp.float32), axis=2).astype(jnp.int32)
    block_base = lax.broadcasted_iota(jnp.int32, (blocks, 1), 0) * CAPACITY
    slot_index = (rank + block_base).reshape(group_rows, TOP)
    slot_count = blocks * CAPACITY
    local_count = gate_weight.shape[0]
    total_slots = local_count * slot_count
    local_expert = routes_all - exp_index * local_count
    is_local = (local_expert >= 0) & (local_expert < local_count)
    target = jnp.where(is_local, local_expert * slot_count + slot_index, -1)

    router_parts = router.reshape(ffn_size, column_count, EXPERTS)
    logits = sum(
        jnp.dot(normed_grid[part], router_parts[part], preferred_element_type=jnp.float32)
        for part in range(ffn_size)
    )
    chosen = jnp.sum(jnp.where(route_hot, logits[:, None, :], 0.0), axis=2)
    raised = jnp.exp(chosen)
    gate_weights = raised / jnp.sum(raised, axis=1, keepdims=True)

    slot_ids = lax.broadcasted_iota(jnp.int32, (1, 1, total_slots), 2)
    slot_hit = target[:, :, None] == slot_ids
    combine = jnp.any(slot_hit, axis=1).astype(jnp.bfloat16)
    slot_weight = jnp.sum(jnp.where(slot_hit, gate_weights[:, :, None], 0.0), axis=(0, 1))
    grouped_t = jnp.einsum(
        "ftc,ts->fcs", normed_grid, combine, preferred_element_type=jnp.float32
    ).astype(jnp.bfloat16).reshape(feature_count, total_slots)
    weighted = expert_ffn(
        grouped_t,
        gate_weight,
        up_weight,
        down_weight,
        slot_weight.reshape(local_count, slot_count, 1),
    ).reshape(total_slots, feature_count)
    mixture = jnp.dot(combine, weighted, preferred_element_type=jnp.float32).astype(jnp.bfloat16)
    moe_cols = ffn_sum_scatter(mixture, ffn_index, ffn_size, 1).astype(jnp.bfloat16)
    moe_out = lax.psum_scatter(moe_cols, "exp", scatter_dimension=0, tiled=True)
    return (hidden_out, moe_out)


def solution(mesh):
    in_specs = (
        P(("req", "exp"), None),
        P(("req", "exp"), "ffn"),
        P(("req", "exp"), None),
        P(("req", "exp"), None),
        P(),
        P(),
        P(),
        P(("req", "exp"), None),
        P(None, "ffn"),
        P("ffn", None),
        P(),
        P(),
        P("exp", None, "ffn"),
        P("exp", None, "ffn"),
        P("exp", "ffn", None),
    )
    out_specs = (P(("req", "exp"), "ffn"), P(("req", "exp"), "ffn"))
    return jax.shard_map(local, mesh=mesh, in_specs=in_specs, out_specs=out_specs, check_vma=False)
```

```python
import jax
import jax.numpy as jnp
from jax import lax
from jax.experimental import pallas as pl
from jax.experimental.pallas import tpu as pltpu
from jax.sharding import PartitionSpec as P

LATENT = 512
ROPE_DIM = 64
HEAD_DIM = 128
QKD = 576
EXPERTS = 32
TOP = 6
CAPACITY = 16
REQ_GRP = 2
CMAX = 1024
BLOCK_ROWS = 64


EPSILON = 1e-06
NEG_FILL = -1e30


SLOT_TILE = 512


def expert_kernel(rows_ref, gate_ref, up_ref, down_ref, scale_ref, out_ref):
    columns = rows_ref[...]
    gate_part = jnp.dot(gate_ref[0], columns, preferred_element_type=jnp.float32)
    up_part = jnp.dot(up_ref[0], columns, preferred_element_type=jnp.float32)
    active = gate_part / (1.0 + jnp.exp(-gate_part)) * up_part
    active = (active * scale_ref[0]).astype(jnp.bfloat16)
    contract = (((0,), (0,)), ((), ()))
    result = lax.dot_general(active, down_ref[0], contract, preferred_element_type=jnp.float32)
    out_ref[0] = result.astype(out_ref.dtype)


def expert_ffn(grouped_t, gate_weight, up_weight, down_weight, scale):
    feature_count = grouped_t.shape[0]
    local_count, _, slot_count = scale.shape
    hidden = gate_weight.shape[2]
    gate_rows = jnp.transpose(gate_weight, (0, 2, 1))
    up_rows = jnp.transpose(up_weight, (0, 2, 1))
    tile = min(SLOT_TILE, slot_count)
    tiles = slot_count // tile
    return pl.pallas_call(
        expert_kernel,
        grid=(local_count, tiles),
        in_specs=[
            pl.BlockSpec((feature_count, tile), lambda j, m: (0, j * tiles + m)),
            pl.BlockSpec((1, hidden, feature_count), lambda j, m: (j, 0, 0)),
            pl.BlockSpec((1, hidden, feature_count), lambda j, m: (j, 0, 0)),
            pl.BlockSpec((1, hidden, feature_count), lambda j, m: (j, 0, 0)),
            pl.BlockSpec((1, 1, tile), lambda j, m: (j, 0, m)),
        ],
        out_specs=pl.BlockSpec((1, tile, feature_count), lambda j, m: (j, m, 0)),
        out_shape=jax.ShapeDtypeStruct((local_count, slot_count, feature_count), jnp.bfloat16),
        compiler_params=pltpu.CompilerParams(
            dimension_semantics=("arbitrary", "arbitrary"),
            vmem_limit_bytes=56 * 1024 * 1024,
        ),
    )(grouped_t, gate_rows, up_rows, down_weight, scale)


def pair_swap(x):
    return lax.ppermute(x, "ffn", [(0, 1), (1, 0)])


def ffn_sum_scatter(x, ffn_index, ffn_size, axis):
    if ffn_size != 2:
        return lax.psum_scatter(x, "ffn", scatter_dimension=axis, tiled=True).astype(jnp.float32)
    width = x.shape[axis] // 2
    mine = lax.dynamic_slice_in_dim(x, ffn_index * width, width, axis)
    other = lax.dynamic_slice_in_dim(x, (1 - ffn_index) * width, width, axis)
    return mine.astype(jnp.float32) + pair_swap(other).astype(jnp.float32)


def ffn_gather_columns(x, ffn_index, ffn_size):
    if ffn_size != 2:
        return lax.all_gather(x, "ffn", axis=1, tiled=True)
    other = pair_swap(x)
    first = jnp.where(ffn_index == 0, x, other)
    second = jnp.where(ffn_index == 0, other, x)
    return jnp.concatenate([first, second], axis=1)


def local(
    residual,
    queries,
    new_latent,
    cache_pool,
    page_table,
    cached_len,
    tenant_start,
    routes,
    value_up,
    out_proj,
    norm_gain,
    router,
    gate_weight,
    up_weight,
    down_weight,
):
    exp_size = lax.axis_size("exp")
    ffn_size = lax.axis_size("ffn")
    req_index = lax.axis_index("req")
    exp_index = lax.axis_index("exp")
    ffn_index = lax.axis_index("ffn")
    token_rows = residual.shape[0]
    feature_count = residual.shape[1]
    fresh_len = token_rows * exp_size // REQ_GRP
    first_token = (req_index * exp_size + exp_index) * token_rows
    request = first_token // fresh_len
    offset = first_token - request * fresh_len
    pool_pages = cache_pool.shape[0]
    page_width = cache_pool.shape[1]
    latent_pages = token_rows * QKD // page_width
    route_count = token_rows * TOP
    route_pages = -(-route_count // page_width)
    route_rows = jnp.pad(
        routes.reshape(route_count).astype(jnp.bfloat16),
        (0, route_pages * page_width - route_count),
    ).reshape(route_pages, page_width)
    packed_rows = pool_pages + latent_pages + route_pages
    share_rows = -(-packed_rows // (ffn_size * 8)) * 8
    packed = jnp.concatenate(
        [
            cache_pool,
            new_latent.reshape(latent_pages, page_width),
            route_rows,
            jnp.zeros((share_rows * ffn_size - packed_rows, page_width), jnp.bfloat16),
        ],
        axis=0,
    )
    share = lax.dynamic_slice_in_dim(packed, ffn_index * share_rows, share_rows, 0)
    gathered = lax.all_gather(share, ("exp", "ffn"), axis=0, tiled=False)
    gathered = gathered.reshape(exp_size, ffn_size * share_rows, page_width)
    stride = ffn_size * share_rows
    group_rows = exp_size * token_rows
    routes_all = (
        gathered[:, pool_pages + latent_pages : packed_rows]
        .reshape(exp_size, route_pages * page_width)[:, :route_count]
        .reshape(group_rows, TOP)
        .astype(jnp.int32)
    )
    flat_pages = gathered.reshape(exp_size * stride, page_width)
    pool_base = req_index * exp_size * pool_pages
    page_rows = page_table[request] - pool_base
    cached_rows = (page_rows // pool_pages) * stride + page_rows % pool_pages
    local_request = request - req_index * REQ_GRP
    fresh_devices = fresh_len // token_rows
    fresh_index = lax.broadcasted_iota(jnp.int32, (fresh_devices, latent_pages), 0)
    fresh_rows = (
        (local_request * fresh_devices + fresh_index) * stride
        + pool_pages
        + lax.broadcasted_iota(jnp.int32, (fresh_devices, latent_pages), 1)
    ).reshape(fresh_devices * latent_pages)
    key_rows = jnp.concatenate([cached_rows, fresh_rows], axis=0)
    all_keys = jnp.take(flat_pages, key_rows, axis=0, mode="clip").reshape(CMAX + fresh_len, QKD)
    heads_here = queries.shape[1] // QKD
    query_heads = queries.reshape(token_rows, heads_here, QKD)
    scale_factor = (HEAD_DIM + ROPE_DIM) ** (-0.5)
    scores = (
        jnp.einsum("thd,kd->thk", query_heads, all_keys, preferred_element_type=jnp.float32)
        * scale_factor
    )
    key_pos = lax.broadcasted_iota(jnp.int32, (1, CMAX + fresh_len), 1)
    tok_pos = offset + lax.broadcasted_iota(jnp.int32, (token_rows, 1), 0)
    cached_ok = (key_pos >= tenant_start[request]) & (key_pos < cached_len[request])
    fresh_ok = (key_pos >= CMAX) & (key_pos - CMAX <= tok_pos)
    visible = cached_ok | fresh_ok
    scores = jnp.where(visible[:, None, :], scores, NEG_FILL)
    top_score = jnp.max(scores, axis=2, keepdims=True)
    weights = jnp.exp(scores - top_score)
    attn_probs = (weights / jnp.sum(weights, axis=2, keepdims=True)).astype(jnp.bfloat16)
    latent_out = jnp.einsum(
        "thk,kl->thl", attn_probs, all_keys[:, :LATENT], preferred_element_type=jnp.float32
    ).astype(jnp.bfloat16)
    value_heads = value_up.reshape(LATENT, heads_here, HEAD_DIM)
    head_out = jnp.einsum(
        "thl,lhd->thd", latent_out, value_heads, preferred_element_type=jnp.float32
    )
    head_out = head_out.astype(jnp.bfloat16).reshape(token_rows, heads_here * HEAD_DIM)
    partial_value = jnp.dot(head_out, out_proj, preferred_element_type=jnp.float32)
    column_count = feature_count // ffn_size
    attn_cols = ffn_sum_scatter(partial_value.astype(jnp.bfloat16), ffn_index, ffn_size, 1)
    residual_cols = lax.dynamic_slice_in_dim(residual, ffn_index * column_count, column_count, 1)
    hidden_out = (residual_cols.astype(jnp.float32) + attn_cols).astype(jnp.bfloat16)
    hidden_wide = hidden_out.astype(jnp.float32)
    square_part = jnp.sum(hidden_wide * hidden_wide, axis=1, keepdims=True)
    if ffn_size == 2:
        square_sum = square_part + pair_swap(square_part)
    else:
        square_sum = lax.psum(square_part, "ffn")
    mean_square = square_sum / feature_count
    gain_cols = lax.dynamic_slice_in_dim(norm_gain, ffn_index * column_count, column_count, 0)
    normed_cols = (
        hidden_wide * lax.rsqrt(mean_square + EPSILON) * gain_cols.astype(jnp.float32)
    ).astype(jnp.bfloat16)
    normed_grid = lax.all_gather(normed_cols, ("ffn", "exp"), axis=0, tiled=False)
    normed_grid = normed_grid.reshape(ffn_size, group_rows, column_count)

    expert_ids = lax.broadcasted_iota(jnp.int32, (1, 1, EXPERTS), 2)
    route_hot = routes_all[:, :, None] == expert_ids
    blocks = group_rows // BLOCK_ROWS
    pair_count = BLOCK_ROWS * TOP
    pair_hot = route_hot.reshape(blocks, pair_count, EXPERTS).astype(jnp.bfloat16)
    earlier = (
        lax.broadcasted_iota(jnp.int32, (pair_count, pair_count), 1)
        < lax.broadcasted_iota(jnp.int32, (pair_count, pair_count), 0)
    ).astype(jnp.bfloat16)
    before = jnp.einsum("pq,bqx->bpx", earlier, pair_hot, preferred_element_type=jnp.float32)
    rank = jnp.sum(before * pair_hot.astype(jnp.float32), axis=2).astype(jnp.int32)
    block_base = lax.broadcasted_iota(jnp.int32, (blocks, 1), 0) * CAPACITY
    slot_index = (rank + block_base).reshape(group_rows, TOP)
    slot_count = blocks * CAPACITY
    local_count = gate_weight.shape[0]
    total_slots = local_count * slot_count
    local_expert = routes_all - exp_index * local_count
    is_local = (local_expert >= 0) & (local_expert < local_count)
    target = jnp.where(is_local, local_expert * slot_count + slot_index, -1)

    router_parts = router.reshape(ffn_size, column_count, EXPERTS)
    logits = sum(
        jnp.dot(normed_grid[part], router_parts[part], preferred_element_type=jnp.float32)
        for part in range(ffn_size)
    )
    chosen = jnp.sum(jnp.where(route_hot, logits[:, None, :], 0.0), axis=2)
    raised = jnp.exp(chosen)
    gate_weights = raised / jnp.sum(raised, axis=1, keepdims=True)

    slot_ids = lax.broadcasted_iota(jnp.int32, (1, 1, total_slots), 2)
    slot_hit = target[:, :, None] == slot_ids
    combine = jnp.any(slot_hit, axis=1).astype(jnp.bfloat16)
    slot_weight = jnp.sum(jnp.where(slot_hit, gate_weights[:, :, None], 0.0), axis=(0, 1))
    grouped_t = jnp.einsum(
        "ftc,ts->fcs", normed_grid, combine, preferred_element_type=jnp.float32
    ).astype(jnp.bfloat16).reshape(feature_count, total_slots)
    weighted = expert_ffn(
        grouped_t,
        gate_weight,
        up_weight,
        down_weight,
        slot_weight.reshape(local_count, 1, slot_count),
    ).reshape(total_slots, feature_count)
    mixture = jnp.dot(combine, weighted, preferred_element_type=jnp.float32).astype(jnp.bfloat16)
    moe_cols = ffn_sum_scatter(mixture, ffn_index, ffn_size, 1).astype(jnp.bfloat16)
    moe_out = lax.psum_scatter(moe_cols, "exp", scatter_dimension=0, tiled=True)
    return (hidden_out, moe_out)


def solution(mesh):
    in_specs = (
        P(("req", "exp"), None),
        P(("req", "exp"), "ffn"),
        P(("req", "exp"), None),
        P(("req", "exp"), None),
        P(),
        P(),
        P(),
        P(("req", "exp"), None),
        P(None, "ffn"),
        P("ffn", None),
        P(),
        P(),
        P("exp", None, "ffn"),
        P("exp", None, "ffn"),
        P("exp", "ffn", None),
    )
    out_specs = (P(("req", "exp"), "ffn"), P(("req", "exp"), "ffn"))
    return jax.shard_map(local, mesh=mesh, in_specs=in_specs, out_specs=out_specs, check_vma=False)
```

```python
import jax
import jax.numpy as jnp
from jax import lax
from jax.experimental import pallas as pl
from jax.experimental.pallas import tpu as pltpu
from jax.sharding import PartitionSpec as P

LATENT = 512
ROPE_DIM = 64
HEAD_DIM = 128
QKD = 576
EXPERTS = 32
TOP = 6
CAPACITY = 16
REQ_GRP = 2
CMAX = 1024
BLOCK_ROWS = 64


EPSILON = 1e-06
NEG_FILL = -1e30


SLOT_TILE = 512


def expert_kernel(rows_ref, gate_ref, up_ref, down_ref, scale_ref, out_ref):
    columns = rows_ref[...]
    gate_part = jnp.dot(gate_ref[0], columns, preferred_element_type=jnp.float32)
    up_part = jnp.dot(up_ref[0], columns, preferred_element_type=jnp.float32)
    active = gate_part / (1.0 + jnp.exp(-gate_part)) * up_part
    active = (active * scale_ref[0]).astype(jnp.bfloat16)
    contract = (((0,), (0,)), ((), ()))
    result = lax.dot_general(active, down_ref[0], contract, preferred_element_type=jnp.float32)
    out_ref[0] = result.astype(out_ref.dtype)


def expert_ffn(grouped_t, gate_weight, up_weight, down_weight, scale):
    feature_count = grouped_t.shape[0]
    local_count, _, slot_count = scale.shape
    hidden = gate_weight.shape[2]
    gate_rows = jnp.transpose(gate_weight, (0, 2, 1))
    up_rows = jnp.transpose(up_weight, (0, 2, 1))
    tile = min(SLOT_TILE, slot_count)
    tiles = slot_count // tile
    return pl.pallas_call(
        expert_kernel,
        grid=(local_count, tiles),
        in_specs=[
            pl.BlockSpec((feature_count, tile), lambda j, m: (0, j * tiles + m)),
            pl.BlockSpec((1, hidden, feature_count), lambda j, m: (j, 0, 0)),
            pl.BlockSpec((1, hidden, feature_count), lambda j, m: (j, 0, 0)),
            pl.BlockSpec((1, hidden, feature_count), lambda j, m: (j, 0, 0)),
            pl.BlockSpec((1, 1, tile), lambda j, m: (j, 0, m)),
        ],
        out_specs=pl.BlockSpec((1, tile, feature_count), lambda j, m: (j, m, 0)),
        out_shape=jax.ShapeDtypeStruct((local_count, slot_count, feature_count), jnp.bfloat16),
        compiler_params=pltpu.CompilerParams(
            dimension_semantics=("arbitrary", "arbitrary"),
            vmem_limit_bytes=56 * 1024 * 1024,
        ),
    )(grouped_t, gate_rows, up_rows, down_weight, scale)


def pair_swap(x):
    return lax.ppermute(x, "ffn", [(0, 1), (1, 0)])


def ffn_sum_scatter(x, ffn_index, ffn_size, axis):
    if ffn_size != 2:
        return lax.psum_scatter(x, "ffn", scatter_dimension=axis, tiled=True).astype(jnp.float32)
    width = x.shape[axis] // 2
    mine = lax.dynamic_slice_in_dim(x, ffn_index * width, width, axis)
    other = lax.dynamic_slice_in_dim(x, (1 - ffn_index) * width, width, axis)
    return mine.astype(jnp.float32) + pair_swap(other).astype(jnp.float32)


def ffn_gather_columns(x, ffn_index, ffn_size):
    if ffn_size != 2:
        return lax.all_gather(x, "ffn", axis=1, tiled=True)
    other = pair_swap(x)
    first = jnp.where(ffn_index == 0, x, other)
    second = jnp.where(ffn_index == 0, other, x)
    return jnp.concatenate([first, second], axis=1)


def local(
    residual,
    queries,
    new_latent,
    cache_pool,
    page_table,
    cached_len,
    tenant_start,
    routes,
    value_up,
    out_proj,
    norm_gain,
    router,
    gate_weight,
    up_weight,
    down_weight,
):
    exp_size = lax.axis_size("exp")
    ffn_size = lax.axis_size("ffn")
    req_index = lax.axis_index("req")
    exp_index = lax.axis_index("exp")
    ffn_index = lax.axis_index("ffn")
    token_rows = residual.shape[0]
    feature_count = residual.shape[1]
    fresh_len = token_rows * exp_size // REQ_GRP
    first_token = (req_index * exp_size + exp_index) * token_rows
    request = first_token // fresh_len
    offset = first_token - request * fresh_len
    pool_pages = cache_pool.shape[0]
    page_width = cache_pool.shape[1]
    latent_pages = token_rows * QKD // page_width
    route_count = token_rows * TOP
    route_pages = -(-route_count // page_width)
    route_rows = jnp.pad(
        routes.reshape(route_count).astype(jnp.bfloat16),
        (0, route_pages * page_width - route_count),
    ).reshape(route_pages, page_width)
    packed_rows = pool_pages + latent_pages + route_pages
    share_rows = -(-packed_rows // (ffn_size * 8)) * 8
    packed = jnp.concatenate(
        [
            cache_pool,
            new_latent.reshape(latent_pages, page_width),
            route_rows,
            jnp.zeros((share_rows * ffn_size - packed_rows, page_width), jnp.bfloat16),
        ],
        axis=0,
    )
    share = lax.select_n(
        ffn_index,
        *[packed[part * share_rows : (part + 1) * share_rows] for part in range(ffn_size)],
    )
    gathered = lax.all_gather(share, ("exp", "ffn"), axis=0, tiled=False)
    gathered = gathered.reshape(exp_size, ffn_size * share_rows, page_width)
    stride = ffn_size * share_rows
    group_rows = exp_size * token_rows
    routes_all = (
        gathered[:, pool_pages + latent_pages : packed_rows]
        .reshape(exp_size, route_pages * page_width)[:, :route_count]
        .reshape(group_rows, TOP)
        .astype(jnp.int32)
    )
    flat_pages = gathered.reshape(exp_size * stride, page_width)
    pool_base = req_index * exp_size * pool_pages
    page_rows = page_table[request] - pool_base
    cached_rows = (page_rows // pool_pages) * stride + page_rows % pool_pages
    local_request = request - req_index * REQ_GRP
    fresh_devices = fresh_len // token_rows
    fresh_index = lax.broadcasted_iota(jnp.int32, (fresh_devices, latent_pages), 0)
    fresh_rows = (
        (local_request * fresh_devices + fresh_index) * stride
        + pool_pages
        + lax.broadcasted_iota(jnp.int32, (fresh_devices, latent_pages), 1)
    ).reshape(fresh_devices * latent_pages)
    key_rows = jnp.concatenate([cached_rows, fresh_rows], axis=0)
    all_keys = jnp.take(flat_pages, key_rows, axis=0, mode="clip").reshape(CMAX + fresh_len, QKD)
    heads_here = queries.shape[1] // QKD
    query_heads = queries.reshape(token_rows, heads_here, QKD)
    scale_factor = (HEAD_DIM + ROPE_DIM) ** (-0.5)
    scores = (
        jnp.einsum("thd,kd->thk", query_heads, all_keys, preferred_element_type=jnp.float32)
        * scale_factor
    )
    key_pos = lax.broadcasted_iota(jnp.int32, (1, CMAX + fresh_len), 1)
    tok_pos = offset + lax.broadcasted_iota(jnp.int32, (token_rows, 1), 0)
    cached_ok = (key_pos >= tenant_start[request]) & (key_pos < cached_len[request])
    fresh_ok = (key_pos >= CMAX) & (key_pos - CMAX <= tok_pos)
    visible = cached_ok | fresh_ok
    scores = jnp.where(visible[:, None, :], scores, NEG_FILL)
    top_score = jnp.max(scores, axis=2, keepdims=True)
    weights = jnp.exp(scores - top_score)
    attn_probs = (weights / jnp.sum(weights, axis=2, keepdims=True)).astype(jnp.bfloat16)
    latent_out = jnp.einsum(
        "thk,kl->thl", attn_probs, all_keys[:, :LATENT], preferred_element_type=jnp.float32
    ).astype(jnp.bfloat16)
    value_heads = value_up.reshape(LATENT, heads_here, HEAD_DIM)
    head_out = jnp.einsum(
        "thl,lhd->thd", latent_out, value_heads, preferred_element_type=jnp.float32
    )
    head_out = head_out.astype(jnp.bfloat16).reshape(token_rows, heads_here * HEAD_DIM)
    partial_value = jnp.dot(head_out, out_proj, preferred_element_type=jnp.float32)
    column_count = feature_count // ffn_size
    attn_cols = ffn_sum_scatter(partial_value.astype(jnp.bfloat16), ffn_index, ffn_size, 1)
    residual_cols = lax.dynamic_slice_in_dim(residual, ffn_index * column_count, column_count, 1)
    hidden_out = (residual_cols.astype(jnp.float32) + attn_cols).astype(jnp.bfloat16)
    hidden_wide = hidden_out.astype(jnp.float32)
    square_part = jnp.sum(hidden_wide * hidden_wide, axis=1, keepdims=True)
    if ffn_size == 2:
        square_sum = square_part + pair_swap(square_part)
    else:
        square_sum = lax.psum(square_part, "ffn")
    mean_square = square_sum / feature_count
    gain_cols = lax.dynamic_slice_in_dim(norm_gain, ffn_index * column_count, column_count, 0)
    normed_cols = (
        hidden_wide * lax.rsqrt(mean_square + EPSILON) * gain_cols.astype(jnp.float32)
    ).astype(jnp.bfloat16)
    normed_grid = lax.all_gather(normed_cols, ("ffn", "exp"), axis=0, tiled=False)
    normed_grid = normed_grid.reshape(ffn_size, group_rows, column_count)

    expert_ids = lax.broadcasted_iota(jnp.int32, (1, 1, EXPERTS), 2)
    route_hot = routes_all[:, :, None] == expert_ids
    blocks = group_rows // BLOCK_ROWS
    pair_count = BLOCK_ROWS * TOP
    pair_hot = route_hot.reshape(blocks, pair_count, EXPERTS).astype(jnp.bfloat16)
    earlier = (
        lax.broadcasted_iota(jnp.int32, (pair_count, pair_count), 1)
        < lax.broadcasted_iota(jnp.int32, (pair_count, pair_count), 0)
    ).astype(jnp.bfloat16)
    before = jnp.einsum("pq,bqx->bpx", earlier, pair_hot, preferred_element_type=jnp.float32)
    rank = jnp.sum(before * pair_hot.astype(jnp.float32), axis=2).astype(jnp.int32)
    block_base = lax.broadcasted_iota(jnp.int32, (blocks, 1), 0) * CAPACITY
    slot_index = (rank + block_base).reshape(group_rows, TOP)
    slot_count = blocks * CAPACITY
    local_count = gate_weight.shape[0]
    total_slots = local_count * slot_count
    local_expert = routes_all - exp_index * local_count
    is_local = (local_expert >= 0) & (local_expert < local_count)
    target = jnp.where(is_local, local_expert * slot_count + slot_index, -1)

    router_parts = router.reshape(ffn_size, column_count, EXPERTS)
    logits = sum(
        jnp.dot(normed_grid[part], router_parts[part], preferred_element_type=jnp.float32)
        for part in range(ffn_size)
    )
    chosen = jnp.sum(jnp.where(route_hot, logits[:, None, :], 0.0), axis=2)
    raised = jnp.exp(chosen)
    gate_weights = raised / jnp.sum(raised, axis=1, keepdims=True)

    slot_ids = lax.broadcasted_iota(jnp.int32, (1, 1, total_slots), 2)
    slot_hit = target[:, :, None] == slot_ids
    combine = jnp.any(slot_hit, axis=1).astype(jnp.bfloat16)
    slot_weight = jnp.sum(jnp.where(slot_hit, gate_weights[:, :, None], 0.0), axis=(0, 1))
    grouped_t = jnp.einsum(
        "ftc,ts->fcs", normed_grid, combine, preferred_element_type=jnp.float32
    ).astype(jnp.bfloat16).reshape(feature_count, total_slots)
    weighted = expert_ffn(
        grouped_t,
        gate_weight,
        up_weight,
        down_weight,
        slot_weight.reshape(local_count, 1, slot_count),
    ).reshape(total_slots, feature_count)
    mixture = jnp.dot(combine, weighted, preferred_element_type=jnp.float32).astype(jnp.bfloat16)
    moe_cols = ffn_sum_scatter(mixture, ffn_index, ffn_size, 1).astype(jnp.bfloat16)
    moe_out = lax.psum_scatter(moe_cols, "exp", scatter_dimension=0, tiled=True)
    return (hidden_out, moe_out)


def solution(mesh):
    in_specs = (
        P(("req", "exp"), None),
        P(("req", "exp"), "ffn"),
        P(("req", "exp"), None),
        P(("req", "exp"), None),
        P(),
        P(),
        P(),
        P(("req", "exp"), None),
        P(None, "ffn"),
        P("ffn", None),
        P(),
        P(),
        P("exp", None, "ffn"),
        P("exp", None, "ffn"),
        P("exp", "ffn", None),
    )
    out_specs = (P(("req", "exp"), "ffn"), P(("req", "exp"), "ffn"))
    return jax.shard_map(local, mesh=mesh, in_specs=in_specs, out_specs=out_specs, check_vma=False)
```
